32 devices in a mesh: tm: 8 (over z, y), lm: 4 (over x, core).
Axes of the slice: x: 2, y: 2, z: 4, core: 2. Of those that a mesh axis runs over, the one named last changes fastest.
Arguments:
- cam_diag: float32 [12288, 384], P('tm'), as said below
- cam_lower: float32 [12288, 384], P('tm')
- cam_rhs: float32 [32, 384], P('tm'), may hold values from -6 to 6
- obs_cam_jac: float32 [4, 24, 32, 128], P(None, None, 'tm', 'lm'), may hold values from -2 to 2
- obs_point_jac: float32 [4, 3, 32, 128], P(None, None, 'tm', 'lm'), may hold values from -6 to 6
- obs_residual: float32 [4, 32, 128], P(None, 'tm', 'lm'), may hold values from -6 to 6
- point_prior: float32 [32, 128], P('tm', 'lm'), may hold values from 0.2 to 5
- knot_start: int32 [32, 128], P('tm', 'lm'), may hold values from 0 to 63, as said below
Outputs:
- reduced_diag: float32 [3072, 384], P('tm')
- reduced_lower: float32 [3072, 384], P('tm')
- reduced_rhs: float32 [8, 384], P('tm')
The draws below stay inside these ranges and needn't reach their ends.
Inputs may be any that keep to these rules, and one draw needn't show every extreme that they name: Each 384 x 384 block of cam_diag is symmetric, and the periodic block tridiagonal matrix with diagonal blocks from cam_diag and blocks of cam_lower beside them (block 0 in the corners) is positive definite. A landmark's window covers knots knot_start to knot_start + 3 counted from its segment's first knot; knots past 64 - 1 are the next segment's first ones, those of segment 0 for the last segment.
All inputs are finite; a program needn't handle non-finite values.
Results may differ from the reference program's by a relative error of at most 0.0003.
Values sent between devices are 32-bit elements; how exact they have to be, the bound alone decides.
No kernel may reach another device: no remote copies, remote signals or barrier semaphores. Data moves between devices by JAX's collectives and lax.ppermute only.
A program may use at most 128 MiB of HBM per device.

```python
import math
import jax
import jax.numpy as jnp
from jax import lax

KNOTS = 64
DOF = 6
ORDER = 4
OBS_ROWS = 4
LMK_DEV = 32
SEGMENTS = 32
BLOCK = 384
LMK_SEG = 128


CHAIN_WEIGHT = 6.0


def draw_cam_diag(key, part):
    blocks = KNOTS * DOF
    jitter = 0.25 * jax.random.uniform(jax.random.fold_in(key, 11), (SEGMENTS, blocks, blocks), jnp.float32, -1.0, 1.0) / blocks
    symmetric = jitter + jnp.swapaxes(jitter, 1, 2)
    values = jax.random.uniform(jax.random.fold_in(key, 12), (SEGMENTS, blocks), jnp.float32, 7.5, 9.0)
    identity = jnp.eye(blocks, dtype=jnp.float32)
    index = jnp.arange(blocks, dtype=jnp.int32)
    distance = jnp.abs(index[:, None] - index[None, :])
    chain = 2.0 * (distance == 0).astype(jnp.float32) - (distance == DOF).astype(jnp.float32)
    assembled = symmetric + values[:, :, None] * identity[None, :, :] + CHAIN_WEIGHT * chain[None, :, :]
    return assembled.reshape(SEGMENTS * blocks, blocks)


def draw_cam_lower(key, part):
    blocks = KNOTS * DOF
    jitter = 0.25 * jax.random.uniform(jax.random.fold_in(key, 21), (SEGMENTS, blocks, blocks), jnp.float32, -1.0, 1.0) / blocks
    signs = jax.random.rademacher(jax.random.fold_in(key, 23), (SEGMENTS, blocks), dtype=jnp.float32)
    fraction = jax.random.uniform(jax.random.fold_in(key, 22), (SEGMENTS, blocks), jnp.float32, 0.0, 1.0)
    magnitude = 0.6 + 0.4 * fraction
    values = 3.2 * signs * magnitude
    identity = jnp.eye(blocks, dtype=jnp.float32)
    assembled = jitter + values[:, :, None] * identity[None, :, :]
    return assembled.reshape(SEGMENTS * blocks, blocks)


def draw_knot_start(key, part):
    raw_draw = jax.random.randint(key, (SEGMENTS, LMK_SEG), 0, KNOTS, dtype=jnp.int32)
    position = jnp.arange(LMK_SEG, dtype=jnp.int32)[None, :]
    highest = jnp.where(position % LMK_DEV == 0, KNOTS - 1, raw_draw)
    return jnp.where(position % LMK_DEV == 1, 0, highest)


def block_levels(stream_key, shape, pieces, least, largest):
    gain, own = 1.0, jax.random.fold_in(stream_key, 6)
    for axis_at, shards_of in pieces:
        heights = jnp.exp(jax.random.uniform(jax.random.fold_in(own, axis_at), (shards_of,), jnp.float32, least / len(pieces), largest / len(pieces)))
        gain = gain * jnp.repeat(heights, shape[axis_at] // shards_of).reshape([-1 if axis == axis_at else 1 for axis in range(len(shape))])
    return gain


def centred(key, extent, deviation, bound, split=(), held_as=jnp.bfloat16):
    loudness = block_levels(key, extent, split, -0.22, 0.18) if split else 1.0
    values = jax.random.normal(key, extent, jnp.float32) * deviation * loudness
    return jnp.minimum(jnp.maximum(values, -bound), bound).astype(held_as)


def setup_inputs(seed: int = 0) -> dict:
    seeds = jax.random.split(jax.random.key(seed), 9)
    return {
        "cam_diag": draw_cam_diag(jax.random.fold_in(seeds[8], 71), 0),
        "cam_lower": draw_cam_lower(jax.random.fold_in(seeds[8], 71), 0),
        "cam_rhs": centred(seeds[2], (SEGMENTS, BLOCK), 1.0, 6.0, ((0, 8),), jnp.float32),
        "obs_cam_jac": centred(seeds[3], (OBS_ROWS, ORDER * DOF, SEGMENTS, LMK_SEG), 0.15, 2.0, ((2, 8), (3, 4)), jnp.float32),
        "obs_point_jac": centred(seeds[4], (OBS_ROWS, 3, SEGMENTS, LMK_SEG), 0.5, 6.0, ((2, 8), (3, 4)), jnp.float32),
        "obs_residual": centred(seeds[5], (OBS_ROWS, SEGMENTS, LMK_SEG), 1.0, 6.0, ((1, 8), (2, 4)), jnp.float32),
        "point_prior": jnp.clip(jnp.exp(math.log(5.0) - 3.218876 * jax.random.uniform(seeds[6], (SEGMENTS, LMK_SEG), jnp.float32) ** block_levels(seeds[6], (SEGMENTS, LMK_SEG), ((0, 8), (1, 4)), -0.2, 0.2)), 0.2, 5.0),
        "knot_start": draw_knot_start(jax.random.fold_in(seeds[8], 71), 0),
    }


PRECISE = lax.Precision.HIGHEST

def point_inverse(normal):
    adj_rows = []
    for row_at in range(3):
        entries = []
        for col_at in range(3):
            entries.append(normal[(col_at + 1) % 3, (row_at + 1) % 3] * normal[(col_at + 2) % 3, (row_at + 2) % 3] - normal[(col_at + 1) % 3, (row_at + 2) % 3] * normal[(col_at + 2) % 3, (row_at + 1) % 3])
        adj_rows.append(jnp.stack(entries))
    adjugate = jnp.stack(adj_rows)
    determ = normal[0, 0] * adjugate[0, 0] + normal[0, 1] * adjugate[1, 0] + normal[0, 2] * adjugate[2, 0]
    return adjugate / determ

def landmark_project(cam_jac, point_jac, residual, prior):
    normal = jnp.einsum('ral,rbl->abl', point_jac, point_jac, precision=PRECISE)
    normal = normal + prior[None, None, :] * jnp.eye(3, dtype=jnp.float32)[:, :, None]
    inverse = point_inverse(normal)
    cross = jnp.einsum('ral,rml->aml', point_jac, cam_jac, precision=PRECISE)
    cross_res = jnp.einsum('ral,rl->al', point_jac, residual, precision=PRECISE)
    solved = jnp.einsum('abl,bml->aml', inverse, cross, precision=PRECISE)
    solved_res = jnp.einsum('abl,bl->al', inverse, cross_res, precision=PRECISE)
    projected = cam_jac - jnp.einsum('ral,aml->rml', point_jac, solved, precision=PRECISE)
    projected_res = residual - jnp.einsum('ral,al->rl', point_jac, solved_res, precision=PRECISE)
    return (projected, projected_res)

def place_rows(values, window_start, extended):
    offsets = jnp.arange(extended, dtype=jnp.int32)[:, None] - DOF * window_start[None, :]
    onehot = (offsets[:, None, :] == jnp.arange(ORDER * DOF, dtype=jnp.int32)[None, :, None]).astype(jnp.float32)
    return jnp.einsum('eml,rml->erl', onehot, values, precision=PRECISE)

def schur_terms(cam_jac, point_jac, residual, prior, window_start):
    landmarks = window_start.shape[0]
    group_size = min(128, landmarks)
    extended = (KNOTS + ORDER - 1) * DOF

    def one_group(totals, group_index):

        def pick_group(array):
            return lax.dynamic_slice_in_dim(array, group_index * group_size, group_size, array.ndim - 1)
        group_cam = pick_group(cam_jac)
        group_start = pick_group(window_start)
        projected, projected_res = landmark_project(group_cam, pick_group(point_jac), pick_group(residual), pick_group(prior))
        placed_cam = place_rows(group_cam, group_start, extended)
        placed_proj = place_rows(projected, group_start, extended)
        new_mat = totals[0] + jnp.einsum('erl,frl->ef', placed_cam, placed_proj, precision=PRECISE)
        new_vec = totals[1] + jnp.einsum('erl,rl->e', placed_cam, projected_res, precision=PRECISE)
        return ((new_mat, new_vec), None)
    start_totals = (jnp.zeros((extended, extended), jnp.float32), jnp.zeros((extended,), jnp.float32))
    totals, _ = lax.scan(one_group, start_totals, jnp.arange(landmarks // group_size, dtype=jnp.int32))
    return totals

def lower_solve(factor, right_hand):
    return jax.scipy.linalg.solve_triangular(factor, right_hand, lower=True)

def eliminate(operands):
    diagonal, coupling, right_side, next_coupling = operands
    factor = jnp.linalg.cholesky(diagonal)
    left_part = lower_solve(factor, coupling)
    right_part = lower_solve(factor, next_coupling.T)
    solved_rhs = lower_solve(factor, right_side[:, None])[:, 0]
    to_next = (jnp.dot(right_part.T, right_part, precision=PRECISE), jnp.dot(right_part.T, left_part, precision=PRECISE), jnp.dot(right_part.T, solved_rhs, precision=PRECISE))
    to_prev = (jnp.dot(left_part.T, left_part, precision=PRECISE), jnp.dot(left_part.T, solved_rhs, precision=PRECISE))
    return (to_next, to_prev)

def reduce_once(diagonal, coupling, right_side):
    next_coupling = jnp.concatenate([coupling[2::2], coupling[:1]], 0)
    to_next, to_prev = jax.vmap(eliminate)((diagonal[1::2], coupling[1::2], right_side[1::2], next_coupling))
    new_diag = diagonal[0::2] - jnp.roll(to_next[0], 1, 0) - to_prev[0]
    new_coupling = -jnp.roll(to_next[1], 1, 0)
    new_rhs = right_side[0::2] - jnp.roll(to_next[2], 1, 0) - to_prev[1]
    return (new_diag, new_coupling, new_rhs)

def reference(cam_diag, cam_lower, cam_rhs, obs_cam_jac, obs_point_jac, obs_residual, point_prior, knot_start):
    blocks = KNOTS * DOF
    border = (ORDER - 1) * DOF

    def segment_terms(segment):

        def pick_segment(array):
            return lax.dynamic_index_in_dim(array, segment, array.ndim - 2, keepdims=False)
        return schur_terms(pick_segment(obs_cam_jac), pick_segment(obs_point_jac), pick_segment(obs_residual), pick_segment(point_prior), pick_segment(knot_start))
    schur_mat, schur_vec = lax.map(segment_terms, jnp.arange(SEGMENTS, dtype=jnp.int32))
    spill_mat = jnp.roll(schur_mat[:, blocks:, :], 1, 0)
    spill_vec = jnp.roll(schur_vec[:, blocks:], 1, 0)
    diagonal = cam_diag.reshape(SEGMENTS, blocks, blocks) + schur_mat[:, :blocks, :blocks] + jnp.pad(spill_mat[:, :, blocks:], ((0, 0), (0, blocks - border), (0, blocks - border)))
    coupling = cam_lower.reshape(SEGMENTS, blocks, blocks) + jnp.pad(spill_mat[:, :, :blocks], ((0, 0), (0, blocks - border), (0, 0)))
    right_side = cam_rhs - schur_vec[:, :blocks] - jnp.pad(spill_vec, ((0, 0), (0, blocks - border)))
    for _ in range(2):
        diagonal, coupling, right_side = reduce_once(diagonal, coupling, right_side)
    remaining = SEGMENTS // 4
    return (diagonal.reshape(remaining * blocks, blocks), coupling.reshape(remaining * blocks, blocks), right_side)
```

```python
import jax
import jax.numpy as jnp
from jax import lax
from jax.sharding import PartitionSpec as P

KNOTS = 64
DOF = 6
ORDER = 4


PRECISE = lax.Precision.HIGHEST


def passed_along(block, axis, distance):
    devices = range(lax.axis_size(axis))
    route = [((i - distance) % len(devices), i) for i in devices]
    return lax.ppermute(block, axis, route)


def point_inverse(normal):
    adj_rows = []
    for row_at in range(3):
        entries = []
        for col_at in range(3):
            entries.append(
                normal[(col_at + 1) % 3, (row_at + 1) % 3]
                * normal[(col_at + 2) % 3, (row_at + 2) % 3]
                - normal[(col_at + 1) % 3, (row_at + 2) % 3]
                * normal[(col_at + 2) % 3, (row_at + 1) % 3]
            )
        adj_rows.append(jnp.stack(entries))
    adjugate = jnp.stack(adj_rows)
    determ = (
        normal[0, 0] * adjugate[0, 0]
        + normal[0, 1] * adjugate[1, 0]
        + normal[0, 2] * adjugate[2, 0]
    )
    return adjugate / determ


def landmark_project(cam_jac, point_jac, residual, prior):
    normal = jnp.einsum("rasl,rbsl->absl", point_jac, point_jac, precision=PRECISE)
    normal = normal + prior[None, None] * jnp.eye(3, dtype=jnp.float32)[:, :, None, None]
    inverse = point_inverse(normal)
    cross = jnp.einsum("rasl,rmsl->amsl", point_jac, cam_jac, precision=PRECISE)
    cross_res = jnp.einsum("rasl,rsl->asl", point_jac, residual, precision=PRECISE)
    solved = jnp.einsum("absl,bmsl->amsl", inverse, cross, precision=PRECISE)
    solved_res = jnp.einsum("absl,bsl->asl", inverse, cross_res, precision=PRECISE)
    projected = cam_jac - jnp.einsum("rasl,amsl->rmsl", point_jac, solved, precision=PRECISE)
    projected_res = residual - jnp.einsum("rasl,asl->rsl", point_jac, solved_res, precision=PRECISE)
    return (projected, projected_res)


def place_knots(values, window_start):
    rows_count = values.shape[0]
    seg_count = values.shape[2]
    group_size = values.shape[3]
    knot_span = KNOTS + ORDER - 1
    offsets = jnp.arange(knot_span, dtype=jnp.int32)[:, None, None] - window_start[None]
    onehot = (offsets[:, None] == jnp.arange(ORDER, dtype=jnp.int32)[None, :, None, None]).astype(
        jnp.float32
    )
    shaped = values.reshape(rows_count, ORDER, DOF, seg_count, group_size)
    placed = jnp.einsum("kosl,rodsl->kdrsl", onehot, shaped, precision=PRECISE)
    return placed.reshape(knot_span * DOF, rows_count, seg_count, group_size)


def batched_terms(cam_jac, point_jac, residual, prior, window_start):
    seg_count = window_start.shape[0]
    landmarks = window_start.shape[1]
    group_size = min(128, landmarks)
    extended = (KNOTS + ORDER - 1) * DOF

    def one_group(totals, group_index):
        projected, projected_res = landmark_project(cam_jac, point_jac, residual, prior)
        placed_cam = place_knots(cam_jac, window_start)
        placed_proj = place_knots(projected, window_start)
        new_mat = totals[0] + jnp.einsum(
            "ersl,frsl->sef", placed_cam, placed_proj, precision=PRECISE
        )
        new_vec = totals[1] + jnp.einsum(
            "ersl,rsl->se", placed_cam, projected_res, precision=PRECISE
        )
        return ((new_mat, new_vec), None)

    start_totals = (
        jnp.zeros((seg_count, extended, extended), jnp.float32),
        jnp.zeros((seg_count, extended), jnp.float32),
    )
    totals, _ = lax.scan(
        one_group, start_totals, jnp.arange(landmarks // group_size, dtype=jnp.int32)
    )
    return totals


def lower_solve(factor, right_hand):
    return jax.scipy.linalg.solve_triangular(factor, right_hand, lower=True)


def eliminate(operands):
    diagonal, coupling, right_side, next_coupling = operands
    factor = jnp.linalg.cholesky(diagonal)
    left_part = lower_solve(factor, coupling)
    right_part = lower_solve(factor, next_coupling.T)
    solved_rhs = lower_solve(factor, right_side[:, None])[:, 0]
    to_next = (
        jnp.dot(right_part.T, right_part, precision=PRECISE),
        jnp.dot(right_part.T, left_part, precision=PRECISE),
        jnp.dot(right_part.T, solved_rhs, precision=PRECISE),
    )
    to_prev = (
        jnp.dot(left_part.T, left_part, precision=PRECISE),
        jnp.dot(left_part.T, solved_rhs, precision=PRECISE),
    )
    return (to_next, to_prev)


def local(
    cam_diag, cam_lower, cam_rhs, obs_cam_jac, obs_point_jac, obs_residual, point_prior, knot_start
):
    blocks = cam_diag.shape[1]
    border = (ORDER - 1) * DOF
    local_count = cam_rhs.shape[0]
    schur_mat, schur_vec = batched_terms(
        obs_cam_jac, obs_point_jac, obs_residual, point_prior, knot_start
    )
    schur_mat, schur_vec = lax.psum((schur_mat, schur_vec), "lm")
    arrived_mat, arrived_vec = passed_along(
        (schur_mat[local_count - 1, blocks:, :], schur_vec[local_count - 1, blocks:]), "tm", 1
    )
    spill_mat = jnp.concatenate([arrived_mat[None], schur_mat[:-1, blocks:, :]], 0)
    spill_vec = jnp.concatenate([arrived_vec[None], schur_vec[:-1, blocks:]], 0)
    diagonal = (
        cam_diag.reshape(local_count, blocks, blocks)
        + schur_mat[:, :blocks, :blocks]
        + jnp.pad(spill_mat[:, :, blocks:], ((0, 0), (0, blocks - border), (0, blocks - border)))
    )
    coupling = cam_lower.reshape(local_count, blocks, blocks) + jnp.pad(
        spill_mat[:, :, :blocks], ((0, 0), (0, blocks - border), (0, 0))
    )
    right_side = (
        cam_rhs - schur_vec[:, :blocks] - jnp.pad(spill_vec, ((0, 0), (0, blocks - border)))
    )
    after_coupling = passed_along(coupling[0], "tm", -1)
    pair = jax.vmap(eliminate)(
        (
            jnp.stack([diagonal[1], diagonal[3]]),
            jnp.stack([coupling[1], coupling[3]]),
            jnp.stack([right_side[1], right_side[3]]),
            jnp.stack([coupling[2], after_coupling]),
        )
    )
    next_first, prev_first = jax.tree.map(lambda x: x[0], pair)
    next_last, prev_last = jax.tree.map(lambda x: x[1], pair)
    mid_diag = diagonal[2] - next_first[0] - prev_last[0]
    mid_coupling = -next_first[1]
    mid_rhs = right_side[2] - next_first[2] - prev_last[1]
    next_mid, prev_mid = eliminate((mid_diag, mid_coupling, mid_rhs, -next_last[1]))
    head_diag = diagonal[0] - prev_first[0] - prev_mid[0]
    head_rhs = right_side[0] - prev_first[1] - prev_mid[1]
    arrived = passed_along(
        (next_last[0] + next_mid[0], next_mid[1], next_last[2] + next_mid[2]), "tm", 1
    )
    out_diag = head_diag - arrived[0]
    out_coupling = -arrived[1]
    out_rhs = head_rhs - arrived[2]
    return (out_diag, out_coupling, out_rhs[None, :])


def solution(mesh):
    placed = (
        P("tm", None),
        P("tm", None),
        P("tm", None),
        P(None, None, "tm", "lm"),
        P(None, None, "tm", "lm"),
        P(None, "tm", "lm"),
        P("tm", "lm"),
        P("tm", "lm"),
    )
    return jax.shard_map(
        local,
        mesh=mesh,
        in_specs=placed,
        out_specs=(P("tm", None), P("tm", None), P("tm", None)),
        check_vma=False,
    )
```

```python
import jax
import jax.numpy as jnp
from jax import lax
from jax.sharding import PartitionSpec as P

KNOTS = 64
DOF = 6
ORDER = 4


PRECISE = lax.Precision.HIGHEST


def passed_along(block, axis, distance):
    devices = range(lax.axis_size(axis))
    route = [((i - distance) % len(devices), i) for i in devices]
    return lax.ppermute(block, axis, route)


def point_inverse(normal):
    adj_rows = []
    for row_at in range(3):
        entries = []
        for col_at in range(3):
            entries.append(
                normal[(col_at + 1) % 3, (row_at + 1) % 3]
                * normal[(col_at + 2) % 3, (row_at + 2) % 3]
                - normal[(col_at + 1) % 3, (row_at + 2) % 3]
                * normal[(col_at + 2) % 3, (row_at + 1) % 3]
            )
        adj_rows.append(jnp.stack(entries))
    adjugate = jnp.stack(adj_rows)
    determ = (
        normal[0, 0] * adjugate[0, 0]
        + normal[0, 1] * adjugate[1, 0]
        + normal[0, 2] * adjugate[2, 0]
    )
    return adjugate / determ


def landmark_project(cam_jac, point_jac, residual, prior):
    normal = jnp.einsum("rasl,rbsl->absl", point_jac, point_jac, precision=PRECISE)
    normal = normal + prior[None, None] * jnp.eye(3, dtype=jnp.float32)[:, :, None, None]
    inverse = point_inverse(normal)
    cross = jnp.einsum("rasl,rmsl->amsl", point_jac, cam_jac, precision=PRECISE)
    cross_res = jnp.einsum("rasl,rsl->asl", point_jac, residual, precision=PRECISE)
    solved = jnp.einsum("absl,bmsl->amsl", inverse, cross, precision=PRECISE)
    solved_res = jnp.einsum("absl,bsl->asl", inverse, cross_res, precision=PRECISE)
    projected = cam_jac - jnp.einsum("rasl,amsl->rmsl", point_jac, solved, precision=PRECISE)
    projected_res = residual - jnp.einsum("rasl,asl->rsl", point_jac, solved_res, precision=PRECISE)
    return (projected, projected_res)


def place_knots(values, window_start):
    rows_count = values.shape[0]
    seg_count = values.shape[2]
    group_size = values.shape[3]
    knot_span = KNOTS + ORDER - 1
    offsets = jnp.arange(knot_span, dtype=jnp.int32)[:, None, None] - window_start[None]
    onehot = (offsets[:, None] == jnp.arange(ORDER, dtype=jnp.int32)[None, :, None, None]).astype(
        jnp.float32
    )
    shaped = values.reshape(rows_count, ORDER, DOF, seg_count, group_size)
    placed = jnp.einsum("kosl,rodsl->kdrsl", onehot, shaped, precision=PRECISE)
    return placed.reshape(knot_span * DOF, rows_count, seg_count, group_size)


def batched_terms(cam_jac, point_jac, residual, prior, window_start):
    seg_count = window_start.shape[0]
    landmarks = window_start.shape[1]
    group_size = min(128, landmarks)
    extended = (KNOTS + ORDER - 1) * DOF

    def one_group(totals, group_index):
        projected, projected_res = landmark_project(cam_jac, point_jac, residual, prior)
        placed_cam = place_knots(cam_jac, window_start)
        placed_proj = place_knots(projected, window_start)
        new_mat = totals[0] + jnp.einsum(
            "ersl,frsl->sef", placed_cam, placed_proj, precision=PRECISE
        )
        new_vec = totals[1] + jnp.einsum(
            "ersl,rsl->se", placed_cam, projected_res, precision=PRECISE
        )
        return ((new_mat, new_vec), None)

    start_totals = (
        jnp.zeros((seg_count, extended, extended), jnp.float32),
        jnp.zeros((seg_count, extended), jnp.float32),
    )
    totals, _ = lax.scan(
        one_group, start_totals, jnp.arange(landmarks // group_size, dtype=jnp.int32)
    )
    return totals


def lower_solve(factor, right_hand):
    return jax.scipy.linalg.solve_triangular(factor, right_hand, lower=True)


def eliminate(operands):
    diagonal, coupling, right_side, next_coupling = operands
    factor = jnp.linalg.cholesky(diagonal)
    inverse = lower_solve(factor, jnp.eye(diagonal.shape[0], dtype=diagonal.dtype))
    left_part = jnp.dot(inverse, coupling, precision=PRECISE)
    right_part = jnp.dot(inverse, next_coupling.T, precision=PRECISE)
    solved_rhs = jnp.dot(inverse, right_side, precision=PRECISE)
    to_next = (
        jnp.dot(right_part.T, right_part, precision=PRECISE),
        jnp.dot(right_part.T, left_part, precision=PRECISE),
        jnp.dot(right_part.T, solved_rhs, precision=PRECISE),
    )
    to_prev = (
        jnp.dot(left_part.T, left_part, precision=PRECISE),
        jnp.dot(left_part.T, solved_rhs, precision=PRECISE),
    )
    return (to_next, to_prev)


def local(
    cam_diag, cam_lower, cam_rhs, obs_cam_jac, obs_point_jac, obs_residual, point_prior, knot_start
):
    blocks = cam_diag.shape[1]
    border = (ORDER - 1) * DOF
    local_count = cam_rhs.shape[0]
    schur_mat, schur_vec = batched_terms(
        obs_cam_jac, obs_point_jac, obs_residual, point_prior, knot_start
    )
    schur_mat, schur_vec = lax.psum((schur_mat, schur_vec), "lm")
    arrived_mat, arrived_vec = passed_along(
        (schur_mat[local_count - 1, blocks:, :], schur_vec[local_count - 1, blocks:]), "tm", 1
    )
    spill_mat = jnp.concatenate([arrived_mat[None], schur_mat[:-1, blocks:, :]], 0)
    spill_vec = jnp.concatenate([arrived_vec[None], schur_vec[:-1, blocks:]], 0)
    diagonal = (
        cam_diag.reshape(local_count, blocks, blocks)
        + schur_mat[:, :blocks, :blocks]
        + jnp.pad(spill_mat[:, :, blocks:], ((0, 0), (0, blocks - border), (0, blocks - border)))
    )
    coupling = cam_lower.reshape(local_count, blocks, blocks) + jnp.pad(
        spill_mat[:, :, :blocks], ((0, 0), (0, blocks - border), (0, 0))
    )
    right_side = (
        cam_rhs - schur_vec[:, :blocks] - jnp.pad(spill_vec, ((0, 0), (0, blocks - border)))
    )
    after_coupling = passed_along(coupling[0], "tm", -1)
    pair = jax.vmap(eliminate)(
        (
            jnp.stack([diagonal[1], diagonal[3]]),
            jnp.stack([coupling[1], coupling[3]]),
            jnp.stack([right_side[1], right_side[3]]),
            jnp.stack([coupling[2], after_coupling]),
        )
    )
    next_first, prev_first = jax.tree.map(lambda x: x[0], pair)
    next_last, prev_last = jax.tree.map(lambda x: x[1], pair)
    mid_diag = diagonal[2] - next_first[0] - prev_last[0]
    mid_coupling = -next_first[1]
    mid_rhs = right_side[2] - next_first[2] - prev_last[1]
    arrived_last = passed_along((next_last[0], next_last[2]), "tm", 1)
    next_mid, prev_mid = eliminate((mid_diag, mid_coupling, mid_rhs, -next_last[1]))
    head_diag = diagonal[0] - prev_first[0] - prev_mid[0] - arrived_last[0]
    head_rhs = right_side[0] - prev_first[1] - prev_mid[1] - arrived_last[1]
    arrived = passed_along((next_mid[0], next_mid[1], next_mid[2]), "tm", 1)
    out_diag = head_diag - arrived[0]
    out_coupling = -arrived[1]
    out_rhs = head_rhs - arrived[2]
    return (out_diag, out_coupling, out_rhs[None, :])


def solution(mesh):
    placed = (
        P("tm", None),
        P("tm", None),
        P("tm", None),
        P(None, None, "tm", "lm"),
        P(None, None, "tm", "lm"),
        P(None, "tm", "lm"),
        P("tm", "lm"),
        P("tm", "lm"),
    )
    return jax.shard_map(
        local,
        mesh=mesh,
        in_specs=placed,
        out_specs=(P("tm", None), P("tm", None), P("tm", None)),
        check_vma=False,
    )
```

```python
import jax
import jax.numpy as jnp
from jax import lax
from jax.sharding import PartitionSpec as P
from jax.experimental import pallas as pl
from jax.experimental.pallas import tpu as pltpu

KNOTS = 64
DOF = 6
ORDER = 4


PRECISE = lax.Precision.HIGHEST


def passed_along(block, axis, distance):
    devices = range(lax.axis_size(axis))
    route = [((i - distance) % len(devices), i) for i in devices]
    return lax.ppermute(block, axis, route)


def point_inverse(normal):
    adj_rows = []
    for row_at in range(3):
        entries = []
        for col_at in range(3):
            entries.append(
                normal[(col_at + 1) % 3, (row_at + 1) % 3]
                * normal[(col_at + 2) % 3, (row_at + 2) % 3]
                - normal[(col_at + 1) % 3, (row_at + 2) % 3]
                * normal[(col_at + 2) % 3, (row_at + 1) % 3]
            )
        adj_rows.append(jnp.stack(entries))
    adjugate = jnp.stack(adj_rows)
    determ = (
        normal[0, 0] * adjugate[0, 0]
        + normal[0, 1] * adjugate[1, 0]
        + normal[0, 2] * adjugate[2, 0]
    )
    return adjugate / determ


def landmark_project(cam_jac, point_jac, residual, prior):
    normal = jnp.einsum("rasl,rbsl->absl", point_jac, point_jac, precision=PRECISE)
    normal = normal + prior[None, None] * jnp.eye(3, dtype=jnp.float32)[:, :, None, None]
    inverse = point_inverse(normal)
    cross = jnp.einsum("rasl,rmsl->amsl", point_jac, cam_jac, precision=PRECISE)
    cross_res = jnp.einsum("rasl,rsl->asl", point_jac, residual, precision=PRECISE)
    solved = jnp.einsum("absl,bmsl->amsl", inverse, cross, precision=PRECISE)
    solved_res = jnp.einsum("absl,bsl->asl", inverse, cross_res, precision=PRECISE)
    projected = cam_jac - jnp.einsum("rasl,amsl->rmsl", point_jac, solved, precision=PRECISE)
    projected_res = residual - jnp.einsum("rasl,asl->rsl", point_jac, solved_res, precision=PRECISE)
    return (projected, projected_res)


def place_knots(values, window_start):
    rows_count = values.shape[0]
    seg_count = values.shape[2]
    group_size = values.shape[3]
    knot_span = KNOTS + ORDER - 1
    offsets = jnp.arange(knot_span, dtype=jnp.int32)[:, None, None] - window_start[None]
    onehot = (offsets[:, None] == jnp.arange(ORDER, dtype=jnp.int32)[None, :, None, None]).astype(
        jnp.float32
    )
    shaped = values.reshape(rows_count, ORDER, DOF, seg_count, group_size)
    placed = jnp.einsum("kosl,rodsl->kdrsl", onehot, shaped, precision=PRECISE)
    return placed.reshape(knot_span * DOF, rows_count, seg_count, group_size)


def batched_terms(cam_jac, point_jac, residual, prior, window_start):
    seg_count = window_start.shape[0]
    landmarks = window_start.shape[1]
    group_size = min(128, landmarks)
    extended = (KNOTS + ORDER - 1) * DOF

    def one_group(totals, group_index):
        projected, projected_res = landmark_project(cam_jac, point_jac, residual, prior)
        placed_cam = place_knots(cam_jac, window_start)
        placed_proj = place_knots(projected, window_start)
        new_mat = totals[0] + jnp.einsum(
            "ersl,frsl->sef", placed_cam, placed_proj, precision=PRECISE
        )
        new_vec = totals[1] + jnp.einsum(
            "ersl,rsl->se", placed_cam, projected_res, precision=PRECISE
        )
        return ((new_mat, new_vec), None)

    start_totals = (
        jnp.zeros((seg_count, extended, extended), jnp.float32),
        jnp.zeros((seg_count, extended), jnp.float32),
    )
    totals, _ = lax.scan(
        one_group, start_totals, jnp.arange(landmarks // group_size, dtype=jnp.int32)
    )
    return totals


PIVOT = 128


def sweep_kernel(d_ref, o_ref, p_ref):
    count, order, _ = d_ref.shape
    o_ref[...] = d_ref[...]
    lane = lax.broadcasted_iota(jnp.int32, (PIVOT, PIVOT), 1)
    sub = lax.broadcasted_iota(jnp.int32, (PIVOT, PIVOT), 0)
    lane_row = lax.broadcasted_iota(jnp.int32, (1, PIVOT), 1)
    for blk in range(order // PIVOT):
        lo = blk * PIVOT
        p_ref[...] = o_ref[:, lo:lo + PIVOT, lo:lo + PIVOT]

        def step(k, carry):
            for b in range(count):
                row = p_ref[b, pl.ds(k, 1), :]
                piv = jnp.sum(jnp.where(lane_row == k, row, 0.0), axis=1, keepdims=True)
                inv = 1.0 / piv
                col = jnp.transpose(jnp.broadcast_to(row, (8, PIVOT)))[:, 0:1]
                scaled = row * inv
                mat = p_ref[b]
                upd = mat - col * scaled
                upd = jnp.where(lane == k, col * inv, upd)
                upd = jnp.where(sub == k, jnp.broadcast_to(scaled, (PIVOT, PIVOT)), upd)
                upd = jnp.where((sub == k) & (lane == k), jnp.broadcast_to(-inv, (PIVOT, PIVOT)), upd)
                p_ref[b] = upd
            return carry

        lax.fori_loop(0, PIVOT, step, 0)
        for b in range(count):
            pneg = p_ref[b]
            col_blk = o_ref[b, :, lo:lo + PIVOT]
            row_blk = o_ref[b, lo:lo + PIVOT, :]
            t = jnp.dot(col_blk, pneg, precision=PRECISE, preferred_element_type=jnp.float32)
            o_ref[b] = o_ref[b] + jnp.dot(t, row_blk, precision=PRECISE, preferred_element_type=jnp.float32)
            o_ref[b, :, lo:lo + PIVOT] = -t
            o_ref[b, lo:lo + PIVOT, :] = -jnp.dot(pneg, row_blk, precision=PRECISE, preferred_element_type=jnp.float32)
            o_ref[b, lo:lo + PIVOT, lo:lo + PIVOT] = pneg


def negated_inverse(mats):
    count, order, _ = mats.shape
    return pl.pallas_call(
        sweep_kernel,
        out_shape=jax.ShapeDtypeStruct(mats.shape, mats.dtype),
        in_specs=[pl.BlockSpec(memory_space=pltpu.VMEM)],
        out_specs=pl.BlockSpec(memory_space=pltpu.VMEM),
        scratch_shapes=[pltpu.VMEM((count, PIVOT, PIVOT), jnp.float32)],
    )(mats)


def eliminate(diagonal, coupling, right_side, next_coupling):
    inverse = -negated_inverse(diagonal)
    ahead = jnp.einsum("bij,bjk->bik", next_coupling, inverse, precision=PRECISE)
    behind = jnp.einsum("bji,bjk->bik", coupling, inverse, precision=PRECISE)
    to_next = (
        jnp.einsum("bik,bjk->bij", ahead, next_coupling, precision=PRECISE),
        jnp.einsum("bik,bkj->bij", ahead, coupling, precision=PRECISE),
        jnp.einsum("bik,bk->bi", ahead, right_side, precision=PRECISE),
    )
    to_prev = (
        jnp.einsum("bik,bkj->bij", behind, coupling, precision=PRECISE),
        jnp.einsum("bik,bk->bi", behind, right_side, precision=PRECISE),
    )
    return (to_next, to_prev)


def local(
    cam_diag, cam_lower, cam_rhs, obs_cam_jac, obs_point_jac, obs_residual, point_prior, knot_start
):
    blocks = cam_diag.shape[1]
    border = (ORDER - 1) * DOF
    local_count = cam_rhs.shape[0]
    schur_mat, schur_vec = batched_terms(
        obs_cam_jac, obs_point_jac, obs_residual, point_prior, knot_start
    )
    schur_mat, schur_vec = lax.psum((schur_mat, schur_vec), "lm")
    arrived_mat, arrived_vec = passed_along(
        (schur_mat[local_count - 1, blocks:, :], schur_vec[local_count - 1, blocks:]), "tm", 1
    )
    spill_mat = jnp.concatenate([arrived_mat[None], schur_mat[:-1, blocks:, :]], 0)
    spill_vec = jnp.concatenate([arrived_vec[None], schur_vec[:-1, blocks:]], 0)
    diagonal = (
        cam_diag.reshape(local_count, blocks, blocks)
        + schur_mat[:, :blocks, :blocks]
        + jnp.pad(spill_mat[:, :, blocks:], ((0, 0), (0, blocks - border), (0, blocks - border)))
    )
    coupling = cam_lower.reshape(local_count, blocks, blocks) + jnp.pad(
        spill_mat[:, :, :blocks], ((0, 0), (0, blocks - border), (0, 0))
    )
    right_side = (
        cam_rhs - schur_vec[:, :blocks] - jnp.pad(spill_vec, ((0, 0), (0, blocks - border)))
    )
    after_coupling = passed_along(coupling[0], "tm", -1)
    pair = eliminate(
        jnp.stack([diagonal[1], diagonal[3]]),
        jnp.stack([coupling[1], coupling[3]]),
        jnp.stack([right_side[1], right_side[3]]),
        jnp.stack([coupling[2], after_coupling]),
    )
    next_first, prev_first = jax.tree.map(lambda x: x[0], pair)
    next_last, prev_last = jax.tree.map(lambda x: x[1], pair)
    mid_diag = diagonal[2] - next_first[0] - prev_last[0]
    mid_coupling = -next_first[1]
    mid_rhs = right_side[2] - next_first[2] - prev_last[1]
    arrived_last = passed_along((next_last[0], next_last[2]), "tm", 1)
    next_mid, prev_mid = jax.tree.map(
        lambda x: x[0],
        eliminate(mid_diag[None], mid_coupling[None], mid_rhs[None], -next_last[1][None]),
    )
    head_diag = diagonal[0] - prev_first[0] - prev_mid[0] - arrived_last[0]
    head_rhs = right_side[0] - prev_first[1] - prev_mid[1] - arrived_last[1]
    arrived = passed_along((next_mid[0], next_mid[1], next_mid[2]), "tm", 1)
    out_diag = head_diag - arrived[0]
    out_coupling = -arrived[1]
    out_rhs = head_rhs - arrived[2]
    return (out_diag, out_coupling, out_rhs[None, :])


def solution(mesh):
    placed = (
        P("tm", None),
        P("tm", None),
        P("tm", None),
        P(None, None, "tm", "lm"),
        P(None, None, "tm", "lm"),
        P(None, "tm", "lm"),
        P("tm", "lm"),
        P("tm", "lm"),
    )
    return jax.shard_map(
        local,
        mesh=mesh,
        in_specs=placed,
        out_specs=(P("tm", None), P("tm", None), P("tm", None)),
        check_vma=False,
    )
```

```python
import jax
import jax.numpy as jnp
from jax import lax
from jax.sharding import PartitionSpec as P
from jax.experimental import pallas as pl
from jax.experimental.pallas import tpu as pltpu

KNOTS = 64
DOF = 6
ORDER = 4


PRECISE = lax.Precision.HIGHEST


def passed_along(block, axis, distance):
    devices = range(lax.axis_size(axis))
    route = [((i - distance) % len(devices), i) for i in devices]
    return lax.ppermute(block, axis, route)


def point_inverse(normal):
    adj_rows = []
    for row_at in range(3):
        entries = []
        for col_at in range(3):
            entries.append(
                normal[(col_at + 1) % 3, (row_at + 1) % 3]
                * normal[(col_at + 2) % 3, (row_at + 2) % 3]
                - normal[(col_at + 1) % 3, (row_at + 2) % 3]
                * normal[(col_at + 2) % 3, (row_at + 1) % 3]
            )
        adj_rows.append(jnp.stack(entries))
    adjugate = jnp.stack(adj_rows)
    determ = (
        normal[0, 0] * adjugate[0, 0]
        + normal[0, 1] * adjugate[1, 0]
        + normal[0, 2] * adjugate[2, 0]
    )
    return adjugate / determ


def landmark_project(cam_jac, point_jac, residual, prior):
    normal = jnp.einsum("rasl,rbsl->absl", point_jac, point_jac, precision=PRECISE)
    normal = normal + prior[None, None] * jnp.eye(3, dtype=jnp.float32)[:, :, None, None]
    inverse = point_inverse(normal)
    cross = jnp.einsum("rasl,rmsl->amsl", point_jac, cam_jac, precision=PRECISE)
    cross_res = jnp.einsum("rasl,rsl->asl", point_jac, residual, precision=PRECISE)
    solved = jnp.einsum("absl,bmsl->amsl", inverse, cross, precision=PRECISE)
    solved_res = jnp.einsum("absl,bsl->asl", inverse, cross_res, precision=PRECISE)
    projected = cam_jac - jnp.einsum("rasl,amsl->rmsl", point_jac, solved, precision=PRECISE)
    projected_res = residual - jnp.einsum("rasl,asl->rsl", point_jac, solved_res, precision=PRECISE)
    return (projected, projected_res)


def place_knots(values, window_start):
    rows_count = values.shape[0]
    seg_count = values.shape[2]
    group_size = values.shape[3]
    knot_span = KNOTS + ORDER - 1
    offsets = jnp.arange(knot_span, dtype=jnp.int32)[:, None, None] - window_start[None]
    onehot = (offsets[:, None] == jnp.arange(ORDER, dtype=jnp.int32)[None, :, None, None]).astype(
        jnp.float32
    )
    shaped = values.reshape(rows_count, ORDER, DOF, seg_count, group_size)
    placed = jnp.einsum("kosl,rodsl->kdrsl", onehot, shaped, precision=PRECISE)
    return placed.reshape(knot_span * DOF, rows_count, seg_count, group_size)


def batched_terms(cam_jac, point_jac, residual, prior, window_start):
    seg_count = window_start.shape[0]
    landmarks = window_start.shape[1]
    group_size = min(128, landmarks)
    extended = (KNOTS + ORDER - 1) * DOF

    def one_group(totals, group_index):
        projected, projected_res = landmark_project(cam_jac, point_jac, residual, prior)
        placed_cam = place_knots(cam_jac, window_start)
        placed_proj = place_knots(projected, window_start)
        new_mat = totals[0] + jnp.einsum(
            "ersl,frsl->sef", placed_cam, placed_proj, precision=PRECISE
        )
        new_vec = totals[1] + jnp.einsum(
            "ersl,rsl->se", placed_cam, projected_res, precision=PRECISE
        )
        return ((new_mat, new_vec), None)

    start_totals = (
        jnp.zeros((seg_count, extended, extended), jnp.float32),
        jnp.zeros((seg_count, extended), jnp.float32),
    )
    totals, _ = lax.scan(
        one_group, start_totals, jnp.arange(landmarks // group_size, dtype=jnp.int32)
    )
    return totals


PIVOT = 128


def sweep_kernel(d_ref, o_ref, p_ref):
    count, order, _ = d_ref.shape
    o_ref[...] = d_ref[...]
    lane_row = lax.broadcasted_iota(jnp.int32, (1, PIVOT), 1)
    for blk in range(order // PIVOT):
        lo = blk * PIVOT
        p_ref[...] = o_ref[:, lo:lo + PIVOT, lo:lo + PIVOT]

        def step(k, carry):
            for b in range(count):
                row = p_ref[b, pl.ds(k, 1), :]
                is_k = lane_row == k
                piv = jnp.sum(jnp.where(is_k, row, 0.0), axis=1, keepdims=True)
                inv = 1.0 / piv
                scaled = row * inv
                col = jnp.broadcast_to(
                    jnp.transpose(jnp.broadcast_to(row, (8, PIVOT)))[:, 0:1], (PIVOT, PIVOT)
                )
                upd = p_ref[b] - col * scaled
                p_ref[b] = jnp.where(is_k, col * inv, upd)
                p_ref[b, pl.ds(k, 1), :] = jnp.where(is_k, -inv, scaled)
            return carry

        lax.fori_loop(0, PIVOT, step, 0)
        for b in range(count):
            pneg = p_ref[b]
            col_blk = o_ref[b, :, lo:lo + PIVOT]
            row_blk = o_ref[b, lo:lo + PIVOT, :]
            t = jnp.dot(col_blk, pneg, precision=PRECISE, preferred_element_type=jnp.float32)
            o_ref[b] = o_ref[b] + jnp.dot(t, row_blk, precision=PRECISE, preferred_element_type=jnp.float32)
            o_ref[b, :, lo:lo + PIVOT] = -t
            o_ref[b, lo:lo + PIVOT, :] = -jnp.dot(pneg, row_blk, precision=PRECISE, preferred_element_type=jnp.float32)
            o_ref[b, lo:lo + PIVOT, lo:lo + PIVOT] = pneg


def negated_inverse(mats):
    count, order, _ = mats.shape
    return pl.pallas_call(
        sweep_kernel,
        out_shape=jax.ShapeDtypeStruct(mats.shape, mats.dtype),
        in_specs=[pl.BlockSpec(memory_space=pltpu.VMEM)],
        out_specs=pl.BlockSpec(memory_space=pltpu.VMEM),
        scratch_shapes=[pltpu.VMEM((count, PIVOT, PIVOT), jnp.float32)],
    )(mats)


def eliminate(diagonal, coupling, right_side, next_coupling):
    inverse = -negated_inverse(diagonal)
    ahead = jnp.einsum("bij,bjk->bik", next_coupling, inverse, precision=PRECISE)
    behind = jnp.einsum("bji,bjk->bik", coupling, inverse, precision=PRECISE)
    to_next = (
        jnp.einsum("bik,bjk->bij", ahead, next_coupling, precision=PRECISE),
        jnp.einsum("bik,bkj->bij", ahead, coupling, precision=PRECISE),
        jnp.einsum("bik,bk->bi", ahead, right_side, precision=PRECISE),
    )
    to_prev = (
        jnp.einsum("bik,bkj->bij", behind, coupling, precision=PRECISE),
        jnp.einsum("bik,bk->bi", behind, right_side, precision=PRECISE),
    )
    return (to_next, to_prev)


def local(
    cam_diag, cam_lower, cam_rhs, obs_cam_jac, obs_point_jac, obs_residual, point_prior, knot_start
):
    blocks = cam_diag.shape[1]
    border = (ORDER - 1) * DOF
    local_count = cam_rhs.shape[0]
    schur_mat, schur_vec = batched_terms(
        obs_cam_jac, obs_point_jac, obs_residual, point_prior, knot_start
    )
    schur_mat, schur_vec = lax.psum((schur_mat, schur_vec), "lm")
    arrived_mat, arrived_vec = passed_along(
        (schur_mat[local_count - 1, blocks:, :], schur_vec[local_count - 1, blocks:]), "tm", 1
    )
    spill_mat = jnp.concatenate([arrived_mat[None], schur_mat[:-1, blocks:, :]], 0)
    spill_vec = jnp.concatenate([arrived_vec[None], schur_vec[:-1, blocks:]], 0)
    diagonal = (
        cam_diag.reshape(local_count, blocks, blocks)
        + schur_mat[:, :blocks, :blocks]
        + jnp.pad(spill_mat[:, :, blocks:], ((0, 0), (0, blocks - border), (0, blocks - border)))
    )
    coupling = cam_lower.reshape(local_count, blocks, blocks) + jnp.pad(
        spill_mat[:, :, :blocks], ((0, 0), (0, blocks - border), (0, 0))
    )
    right_side = (
        cam_rhs - schur_vec[:, :blocks] - jnp.pad(spill_vec, ((0, 0), (0, blocks - border)))
    )
    after_coupling = passed_along(coupling[0], "tm", -1)
    pair = eliminate(
        jnp.stack([diagonal[1], diagonal[3]]),
        jnp.stack([coupling[1], coupling[3]]),
        jnp.stack([right_side[1], right_side[3]]),
        jnp.stack([coupling[2], after_coupling]),
    )
    next_first, prev_first = jax.tree.map(lambda x: x[0], pair)
    next_last, prev_last = jax.tree.map(lambda x: x[1], pair)
    mid_diag = diagonal[2] - next_first[0] - prev_last[0]
    mid_coupling = -next_first[1]
    mid_rhs = right_side[2] - next_first[2] - prev_last[1]
    arrived_last = passed_along((next_last[0], next_last[2]), "tm", 1)
    next_mid, prev_mid = jax.tree.map(
        lambda x: x[0],
        eliminate(mid_diag[None], mid_coupling[None], mid_rhs[None], -next_last[1][None]),
    )
    head_diag = diagonal[0] - prev_first[0] - prev_mid[0] - arrived_last[0]
    head_rhs = right_side[0] - prev_first[1] - prev_mid[1] - arrived_last[1]
    arrived = passed_along((next_mid[0], next_mid[1], next_mid[2]), "tm", 1)
    out_diag = head_diag - arrived[0]
    out_coupling = -arrived[1]
    out_rhs = head_rhs - arrived[2]
    return (out_diag, out_coupling, out_rhs[None, :])


def solution(mesh):
    placed = (
        P("tm", None),
        P("tm", None),
        P("tm", None),
        P(None, None, "tm", "lm"),
        P(None, None, "tm", "lm"),
        P(None, "tm", "lm"),
        P("tm", "lm"),
        P("tm", "lm"),
    )
    return jax.shard_map(
        local,
        mesh=mesh,
        in_specs=placed,
        out_specs=(P("tm", None), P("tm", None), P("tm", None)),
        check_vma=False,
    )
```

```python
import jax
import jax.numpy as jnp
from jax import lax
from jax.sharding import PartitionSpec as P
from jax.experimental import pallas as pl
from jax.experimental.pallas import tpu as pltpu

KNOTS = 64
DOF = 6
ORDER = 4


PRECISE = lax.Precision.HIGHEST


def passed_along(block, axis, distance):
    devices = range(lax.axis_size(axis))
    route = [((i - distance) % len(devices), i) for i in devices]
    return lax.ppermute(block, axis, route)


def point_inverse(normal):
    adj_rows = []
    for row_at in range(3):
        entries = []
        for col_at in range(3):
            entries.append(
                normal[(col_at + 1) % 3, (row_at + 1) % 3]
                * normal[(col_at + 2) % 3, (row_at + 2) % 3]
                - normal[(col_at + 1) % 3, (row_at + 2) % 3]
                * normal[(col_at + 2) % 3, (row_at + 1) % 3]
            )
        adj_rows.append(jnp.stack(entries))
    adjugate = jnp.stack(adj_rows)
    determ = (
        normal[0, 0] * adjugate[0, 0]
        + normal[0, 1] * adjugate[1, 0]
        + normal[0, 2] * adjugate[2, 0]
    )
    return adjugate / determ


def landmark_project(cam_jac, point_jac, residual, prior):
    normal = jnp.einsum("rasl,rbsl->absl", point_jac, point_jac, precision=PRECISE)
    normal = normal + prior[None, None] * jnp.eye(3, dtype=jnp.float32)[:, :, None, None]
    inverse = point_inverse(normal)
    cross = jnp.einsum("rasl,rmsl->amsl", point_jac, cam_jac, precision=PRECISE)
    cross_res = jnp.einsum("rasl,rsl->asl", point_jac, residual, precision=PRECISE)
    solved = jnp.einsum("absl,bmsl->amsl", inverse, cross, precision=PRECISE)
    solved_res = jnp.einsum("absl,bsl->asl", inverse, cross_res, precision=PRECISE)
    projected = cam_jac - jnp.einsum("rasl,amsl->rmsl", point_jac, solved, precision=PRECISE)
    projected_res = residual - jnp.einsum("rasl,asl->rsl", point_jac, solved_res, precision=PRECISE)
    return (projected, projected_res)


def place_knots(values, window_start):
    rows_count = values.shape[0]
    seg_count = values.shape[2]
    group_size = values.shape[3]
    knot_span = KNOTS + ORDER - 1
    offsets = jnp.arange(knot_span, dtype=jnp.int32)[:, None, None] - window_start[None]
    onehot = (offsets[:, None] == jnp.arange(ORDER, dtype=jnp.int32)[None, :, None, None]).astype(
        jnp.float32
    )
    shaped = values.reshape(rows_count, ORDER, DOF, seg_count, group_size)
    placed = jnp.einsum("kosl,rodsl->kdrsl", onehot, shaped, precision=PRECISE)
    return placed.reshape(knot_span * DOF, rows_count, seg_count, group_size)


def batched_terms(cam_jac, point_jac, residual, prior, window_start):
    seg_count = window_start.shape[0]
    landmarks = window_start.shape[1]
    group_size = min(128, landmarks)
    extended = (KNOTS + ORDER - 1) * DOF

    def one_group(totals, group_index):
        projected, projected_res = landmark_project(cam_jac, point_jac, residual, prior)
        placed_cam = place_knots(cam_jac, window_start)
        placed_proj = place_knots(projected, window_start)
        new_mat = totals[0] + jnp.einsum(
            "ersl,frsl->sef", placed_cam, placed_proj, precision=PRECISE
        )
        new_vec = totals[1] + jnp.einsum(
            "ersl,rsl->se", placed_cam, projected_res, precision=PRECISE
        )
        return ((new_mat, new_vec), None)

    start_totals = (
        jnp.zeros((seg_count, extended, extended), jnp.float32),
        jnp.zeros((seg_count, extended), jnp.float32),
    )
    totals, _ = lax.scan(
        one_group, start_totals, jnp.arange(landmarks // group_size, dtype=jnp.int32)
    )
    return totals


PIVOT = 128


def sweep_kernel(d_ref, o_ref, *pivot_refs):
    count, order, _ = d_ref.shape
    o_ref[...] = d_ref[...]
    lane_row = lax.broadcasted_iota(jnp.int32, (1, PIVOT), 1)
    for blk in range(order // PIVOT):
        lo = blk * PIVOT
        for b in range(count):
            pivot_refs[b][...] = o_ref[b, lo:lo + PIVOT, lo:lo + PIVOT]

        def step(k, carry):
            for p_ref in pivot_refs:
                row = p_ref[pl.ds(k, 1), :]
                is_k = lane_row == k
                piv = jnp.sum(jnp.where(is_k, row, 0.0), axis=1, keepdims=True)
                inv = 1.0 / piv
                scaled = row * inv
                col = jnp.broadcast_to(
                    jnp.transpose(jnp.broadcast_to(row, (8, PIVOT)))[:, 0:1], (PIVOT, PIVOT)
                )
                upd = p_ref[...] - col * scaled
                p_ref[...] = jnp.where(is_k, col * inv, upd)
                p_ref[pl.ds(k, 1), :] = jnp.where(is_k, -inv, scaled)
            return carry

        lax.fori_loop(0, PIVOT, step, 0, unroll=2)
        for b in range(count):
            pneg = pivot_refs[b][...]
            col_blk = o_ref[b, :, lo:lo + PIVOT]
            row_blk = o_ref[b, lo:lo + PIVOT, :]
            t = jnp.dot(col_blk, pneg, precision=PRECISE, preferred_element_type=jnp.float32)
            o_ref[b] = o_ref[b] + jnp.dot(t, row_blk, precision=PRECISE, preferred_element_type=jnp.float32)
            o_ref[b, :, lo:lo + PIVOT] = -t
            o_ref[b, lo:lo + PIVOT, :] = -jnp.dot(pneg, row_blk, precision=PRECISE, preferred_element_type=jnp.float32)
            o_ref[b, lo:lo + PIVOT, lo:lo + PIVOT] = pneg


def negated_inverse(mats):
    count, order, _ = mats.shape
    return pl.pallas_call(
        sweep_kernel,
        out_shape=jax.ShapeDtypeStruct(mats.shape, mats.dtype),
        in_specs=[pl.BlockSpec(memory_space=pltpu.VMEM)],
        out_specs=pl.BlockSpec(memory_space=pltpu.VMEM),
        scratch_shapes=[pltpu.VMEM((PIVOT, PIVOT), jnp.float32)] * count,
    )(mats)


def eliminate(diagonal, coupling, right_side, next_coupling):
    inverse = -negated_inverse(diagonal)
    ahead = jnp.einsum("bij,bjk->bik", next_coupling, inverse, precision=PRECISE)
    behind = jnp.einsum("bji,bjk->bik", coupling, inverse, precision=PRECISE)
    to_next = (
        jnp.einsum("bik,bjk->bij", ahead, next_coupling, precision=PRECISE),
        jnp.einsum("bik,bkj->bij", ahead, coupling, precision=PRECISE),
        jnp.einsum("bik,bk->bi", ahead, right_side, precision=PRECISE),
    )
    to_prev = (
        jnp.einsum("bik,bkj->bij", behind, coupling, precision=PRECISE),
        jnp.einsum("bik,bk->bi", behind, right_side, precision=PRECISE),
    )
    return (to_next, to_prev)


def local(
    cam_diag, cam_lower, cam_rhs, obs_cam_jac, obs_point_jac, obs_residual, point_prior, knot_start
):
    blocks = cam_diag.shape[1]
    border = (ORDER - 1) * DOF
    local_count = cam_rhs.shape[0]
    schur_mat, schur_vec = batched_terms(
        obs_cam_jac, obs_point_jac, obs_residual, point_prior, knot_start
    )
    schur_mat, schur_vec = lax.psum((schur_mat, schur_vec), "lm")
    arrived_mat, arrived_vec = passed_along(
        (schur_mat[local_count - 1, blocks:, :], schur_vec[local_count - 1, blocks:]), "tm", 1
    )
    spill_mat = jnp.concatenate([arrived_mat[None], schur_mat[:-1, blocks:, :]], 0)
    spill_vec = jnp.concatenate([arrived_vec[None], schur_vec[:-1, blocks:]], 0)
    diagonal = (
        cam_diag.reshape(local_count, blocks, blocks)
        + schur_mat[:, :blocks, :blocks]
        + jnp.pad(spill_mat[:, :, blocks:], ((0, 0), (0, blocks - border), (0, blocks - border)))
    )
    coupling = cam_lower.reshape(local_count, blocks, blocks) + jnp.pad(
        spill_mat[:, :, :blocks], ((0, 0), (0, blocks - border), (0, 0))
    )
    right_side = (
        cam_rhs - schur_vec[:, :blocks] - jnp.pad(spill_vec, ((0, 0), (0, blocks - border)))
    )
    after_coupling = passed_along(coupling[0], "tm", -1)
    pair = eliminate(
        jnp.stack([diagonal[1], diagonal[3]]),
        jnp.stack([coupling[1], coupling[3]]),
        jnp.stack([right_side[1], right_side[3]]),
        jnp.stack([coupling[2], after_coupling]),
    )
    next_first, prev_first = jax.tree.map(lambda x: x[0], pair)
    next_last, prev_last = jax.tree.map(lambda x: x[1], pair)
    mid_diag = diagonal[2] - next_first[0] - prev_last[0]
    mid_coupling = -next_first[1]
    mid_rhs = right_side[2] - next_first[2] - prev_last[1]
    arrived_last = passed_along((next_last[0], next_last[2]), "tm", 1)
    next_mid, prev_mid = jax.tree.map(
        lambda x: x[0],
        eliminate(mid_diag[None], mid_coupling[None], mid_rhs[None], -next_last[1][None]),
    )
    head_diag = diagonal[0] - prev_first[0] - prev_mid[0] - arrived_last[0]
    head_rhs = right_side[0] - prev_first[1] - prev_mid[1] - arrived_last[1]
    arrived = passed_along((next_mid[0], next_mid[1], next_mid[2]), "tm", 1)
    out_diag = head_diag - arrived[0]
    out_coupling = -arrived[1]
    out_rhs = head_rhs - arrived[2]
    return (out_diag, out_coupling, out_rhs[None, :])


def solution(mesh):
    placed = (
        P("tm", None),
        P("tm", None),
        P("tm", None),
        P(None, None, "tm", "lm"),
        P(None, None, "tm", "lm"),
        P(None, "tm", "lm"),
        P("tm", "lm"),
        P("tm", "lm"),
    )
    return jax.shard_map(
        local,
        mesh=mesh,
        in_specs=placed,
        out_specs=(P("tm", None), P("tm", None), P("tm", None)),
        check_vma=False,
    )
```

```python
import jax
import jax.numpy as jnp
from jax import lax
from jax.sharding import PartitionSpec as P
from jax.experimental import pallas as pl
from jax.experimental.pallas import tpu as pltpu

KNOTS = 64
DOF = 6
ORDER = 4


PRECISE = lax.Precision.HIGHEST


def passed_along(block, axis, distance):
    devices = range(lax.axis_size(axis))
    route = [((i - distance) % len(devices), i) for i in devices]
    return lax.ppermute(block, axis, route)


def point_inverse(normal):
    adj_rows = []
    for row_at in range(3):
        entries = []
        for col_at in range(3):
            entries.append(
                normal[(col_at + 1) % 3, (row_at + 1) % 3]
                * normal[(col_at + 2) % 3, (row_at + 2) % 3]
                - normal[(col_at + 1) % 3, (row_at + 2) % 3]
                * normal[(col_at + 2) % 3, (row_at + 1) % 3]
            )
        adj_rows.append(jnp.stack(entries))
    adjugate = jnp.stack(adj_rows)
    determ = (
        normal[0, 0] * adjugate[0, 0]
        + normal[0, 1] * adjugate[1, 0]
        + normal[0, 2] * adjugate[2, 0]
    )
    return adjugate / determ


def landmark_project(cam_jac, point_jac, residual, prior):
    normal = jnp.einsum("rasl,rbsl->absl", point_jac, point_jac, precision=PRECISE)
    normal = normal + prior[None, None] * jnp.eye(3, dtype=jnp.float32)[:, :, None, None]
    inverse = point_inverse(normal)
    cross = jnp.einsum("rasl,rmsl->amsl", point_jac, cam_jac, precision=PRECISE)
    cross_res = jnp.einsum("rasl,rsl->asl", point_jac, residual, precision=PRECISE)
    solved = jnp.einsum("absl,bmsl->amsl", inverse, cross, precision=PRECISE)
    solved_res = jnp.einsum("absl,bsl->asl", inverse, cross_res, precision=PRECISE)
    projected = cam_jac - jnp.einsum("rasl,amsl->rmsl", point_jac, solved, precision=PRECISE)
    projected_res = residual - jnp.einsum("rasl,asl->rsl", point_jac, solved_res, precision=PRECISE)
    return (projected, projected_res)


def place_knots(values, window_start):
    rows_count = values.shape[0]
    seg_count = values.shape[2]
    group_size = values.shape[3]
    knot_span = KNOTS + ORDER - 1
    offsets = jnp.arange(knot_span, dtype=jnp.int32)[:, None, None] - window_start[None]
    onehot = (offsets[:, None] == jnp.arange(ORDER, dtype=jnp.int32)[None, :, None, None]).astype(
        jnp.float32
    )
    shaped = values.reshape(rows_count, ORDER, DOF, seg_count, group_size)
    placed = jnp.einsum("kosl,rodsl->kdrsl", onehot, shaped, precision=PRECISE)
    return placed.reshape(knot_span * DOF, rows_count, seg_count, group_size)


def batched_terms(cam_jac, point_jac, residual, prior, window_start):
    seg_count = window_start.shape[0]
    landmarks = window_start.shape[1]
    group_size = min(128, landmarks)
    extended = (KNOTS + ORDER - 1) * DOF

    def one_group(totals, group_index):
        projected, projected_res = landmark_project(cam_jac, point_jac, residual, prior)
        placed_cam = place_knots(cam_jac, window_start)
        placed_proj = place_knots(projected, window_start)
        new_mat = totals[0] + jnp.einsum(
            "ersl,frsl->sef", placed_cam, placed_proj, precision=PRECISE
        )
        new_vec = totals[1] + jnp.einsum(
            "ersl,rsl->se", placed_cam, projected_res, precision=PRECISE
        )
        return ((new_mat, new_vec), None)

    start_totals = (
        jnp.zeros((seg_count, extended, extended), jnp.float32),
        jnp.zeros((seg_count, extended), jnp.float32),
    )
    totals, _ = lax.scan(
        one_group, start_totals, jnp.arange(landmarks // group_size, dtype=jnp.int32)
    )
    return totals


PIVOT = 128


def sweep_kernel(d_ref, o_ref, *pivot_refs):
    count, order, _ = d_ref.shape
    o_ref[...] = d_ref[...]
    lane_row = lax.broadcasted_iota(jnp.int32, (1, PIVOT), 1)
    for blk in range(order // PIVOT):
        lo = blk * PIVOT
        for b in range(count):
            pivot_refs[b][...] = o_ref[b, lo:lo + PIVOT, lo:lo + PIVOT]

        def step(k, rows):
            ahead_at = jnp.minimum(k + 1, PIVOT - 1)
            is_k = lane_row == k
            is_ahead = lane_row == ahead_at
            carried = []
            for p_ref, row in zip(pivot_refs, rows):
                piv = jnp.sum(jnp.where(is_k, row, 0.0), axis=1, keepdims=True)
                link = jnp.sum(jnp.where(is_ahead, row, 0.0), axis=1, keepdims=True)
                inv = 1.0 / piv
                scaled = row * inv
                ahead = p_ref[pl.ds(ahead_at, 1), :]
                carried.append(jnp.where(is_k, link * inv, ahead - link * scaled))
                col = jnp.broadcast_to(
                    jnp.transpose(jnp.broadcast_to(row, (8, PIVOT)))[:, 0:1], (PIVOT, PIVOT)
                )
                upd = p_ref[...] - col * scaled
                p_ref[...] = jnp.where(is_k, col * inv, upd)
                p_ref[pl.ds(k, 1), :] = jnp.where(is_k, -inv, scaled)
            return tuple(carried)

        lax.fori_loop(
            0, PIVOT, step, tuple(p_ref[pl.ds(0, 1), :] for p_ref in pivot_refs), unroll=2
        )
        for b in range(count):
            pneg = pivot_refs[b][...]
            col_blk = o_ref[b, :, lo:lo + PIVOT]
            row_blk = o_ref[b, lo:lo + PIVOT, :]
            t = jnp.dot(col_blk, pneg, precision=PRECISE, preferred_element_type=jnp.float32)
            o_ref[b] = o_ref[b] + jnp.dot(t, row_blk, precision=PRECISE, preferred_element_type=jnp.float32)
            o_ref[b, :, lo:lo + PIVOT] = -t
            o_ref[b, lo:lo + PIVOT, :] = -jnp.dot(pneg, row_blk, precision=PRECISE, preferred_element_type=jnp.float32)
            o_ref[b, lo:lo + PIVOT, lo:lo + PIVOT] = pneg


def negated_inverse(mats):
    count, order, _ = mats.shape
    return pl.pallas_call(
        sweep_kernel,
        out_shape=jax.ShapeDtypeStruct(mats.shape, mats.dtype),
        in_specs=[pl.BlockSpec(memory_space=pltpu.VMEM)],
        out_specs=pl.BlockSpec(memory_space=pltpu.VMEM),
        scratch_shapes=[pltpu.VMEM((PIVOT, PIVOT), jnp.float32)] * count,
    )(mats)


def eliminate(diagonal, coupling, right_side, next_coupling):
    inverse = -negated_inverse(diagonal)
    ahead = jnp.einsum("bij,bjk->bik", next_coupling, inverse, precision=PRECISE)
    behind = jnp.einsum("bji,bjk->bik", coupling, inverse, precision=PRECISE)
    to_next = (
        jnp.einsum("bik,bjk->bij", ahead, next_coupling, precision=PRECISE),
        jnp.einsum("bik,bkj->bij", ahead, coupling, precision=PRECISE),
        jnp.einsum("bik,bk->bi", ahead, right_side, precision=PRECISE),
    )
    to_prev = (
        jnp.einsum("bik,bkj->bij", behind, coupling, precision=PRECISE),
        jnp.einsum("bik,bk->bi", behind, right_side, precision=PRECISE),
    )
    return (to_next, to_prev)


def local(
    cam_diag, cam_lower, cam_rhs, obs_cam_jac, obs_point_jac, obs_residual, point_prior, knot_start
):
    blocks = cam_diag.shape[1]
    border = (ORDER - 1) * DOF
    local_count = cam_rhs.shape[0]
    schur_mat, schur_vec = batched_terms(
        obs_cam_jac, obs_point_jac, obs_residual, point_prior, knot_start
    )
    schur_mat, schur_vec = lax.psum((schur_mat, schur_vec), "lm")
    arrived_mat, arrived_vec = passed_along(
        (schur_mat[local_count - 1, blocks:, :], schur_vec[local_count - 1, blocks:]), "tm", 1
    )
    spill_mat = jnp.concatenate([arrived_mat[None], schur_mat[:-1, blocks:, :]], 0)
    spill_vec = jnp.concatenate([arrived_vec[None], schur_vec[:-1, blocks:]], 0)
    diagonal = (
        cam_diag.reshape(local_count, blocks, blocks)
        + schur_mat[:, :blocks, :blocks]
        + jnp.pad(spill_mat[:, :, blocks:], ((0, 0), (0, blocks - border), (0, blocks - border)))
    )
    coupling = cam_lower.reshape(local_count, blocks, blocks) + jnp.pad(
        spill_mat[:, :, :blocks], ((0, 0), (0, blocks - border), (0, 0))
    )
    right_side = (
        cam_rhs - schur_vec[:, :blocks] - jnp.pad(spill_vec, ((0, 0), (0, blocks - border)))
    )
    after_coupling = passed_along(coupling[0], "tm", -1)
    pair = eliminate(
        jnp.stack([diagonal[1], diagonal[3]]),
        jnp.stack([coupling[1], coupling[3]]),
        jnp.stack([right_side[1], right_side[3]]),
        jnp.stack([coupling[2], after_coupling]),
    )
    next_first, prev_first = jax.tree.map(lambda x: x[0], pair)
    next_last, prev_last = jax.tree.map(lambda x: x[1], pair)
    mid_diag = diagonal[2] - next_first[0] - prev_last[0]
    mid_coupling = -next_first[1]
    mid_rhs = right_side[2] - next_first[2] - prev_last[1]
    arrived_last = passed_along((next_last[0], next_last[2]), "tm", 1)
    next_mid, prev_mid = jax.tree.map(
        lambda x: x[0],
        eliminate(mid_diag[None], mid_coupling[None], mid_rhs[None], -next_last[1][None]),
    )
    head_diag = diagonal[0] - prev_first[0] - prev_mid[0] - arrived_last[0]
    head_rhs = right_side[0] - prev_first[1] - prev_mid[1] - arrived_last[1]
    arrived = passed_along((next_mid[0], next_mid[1], next_mid[2]), "tm", 1)
    out_diag = head_diag - arrived[0]
    out_coupling = -arrived[1]
    out_rhs = head_rhs - arrived[2]
    return (out_diag, out_coupling, out_rhs[None, :])


def solution(mesh):
    placed = (
        P("tm", None),
        P("tm", None),
        P("tm", None),
        P(None, None, "tm", "lm"),
        P(None, None, "tm", "lm"),
        P(None, "tm", "lm"),
        P("tm", "lm"),
        P("tm", "lm"),
    )
    return jax.shard_map(
        local,
        mesh=mesh,
        in_specs=placed,
        out_specs=(P("tm", None), P("tm", None), P("tm", None)),
        check_vma=False,
    )
```

```python
import jax
import jax.numpy as jnp
from jax import lax
from jax.sharding import PartitionSpec as P
from jax.experimental import pallas as pl
from jax.experimental.pallas import tpu as pltpu

KNOTS = 64
DOF = 6
ORDER = 4


PRECISE = lax.Precision.HIGHEST


def passed_along(block, axis, distance):
    devices = range(lax.axis_size(axis))
    route = [((i - distance) % len(devices), i) for i in devices]
    return lax.ppermute(block, axis, route)


def point_inverse(normal):
    adj_rows = []
    for row_at in range(3):
        entries = []
        for col_at in range(3):
            entries.append(
                normal[(col_at + 1) % 3, (row_at + 1) % 3]
                * normal[(col_at + 2) % 3, (row_at + 2) % 3]
                - normal[(col_at + 1) % 3, (row_at + 2) % 3]
                * normal[(col_at + 2) % 3, (row_at + 1) % 3]
            )
        adj_rows.append(jnp.stack(entries))
    adjugate = jnp.stack(adj_rows)
    determ = (
        normal[0, 0] * adjugate[0, 0]
        + normal[0, 1] * adjugate[1, 0]
        + normal[0, 2] * adjugate[2, 0]
    )
    return adjugate / determ


def landmark_project(cam_jac, point_jac, residual, prior):
    normal = jnp.einsum("rasl,rbsl->absl", point_jac, point_jac, precision=PRECISE)
    normal = normal + prior[None, None] * jnp.eye(3, dtype=jnp.float32)[:, :, None, None]
    inverse = point_inverse(normal)
    cross = jnp.einsum("rasl,rmsl->amsl", point_jac, cam_jac, precision=PRECISE)
    cross_res = jnp.einsum("rasl,rsl->asl", point_jac, residual, precision=PRECISE)
    solved = jnp.einsum("absl,bmsl->amsl", inverse, cross, precision=PRECISE)
    solved_res = jnp.einsum("absl,bsl->asl", inverse, cross_res, precision=PRECISE)
    projected = cam_jac - jnp.einsum("rasl,amsl->rmsl", point_jac, solved, precision=PRECISE)
    projected_res = residual - jnp.einsum("rasl,asl->rsl", point_jac, solved_res, precision=PRECISE)
    return (projected, projected_res)


def place_knots(values, window_start):
    rows_count = values.shape[0]
    seg_count = values.shape[2]
    group_size = values.shape[3]
    knot_span = KNOTS + ORDER - 1
    offsets = jnp.arange(knot_span, dtype=jnp.int32)[:, None, None] - window_start[None]
    onehot = (offsets[:, None] == jnp.arange(ORDER, dtype=jnp.int32)[None, :, None, None]).astype(
        jnp.float32
    )
    shaped = values.reshape(rows_count, ORDER, DOF, seg_count, group_size)
    placed = jnp.einsum("kosl,rodsl->kdrsl", onehot, shaped, precision=PRECISE)
    return placed.reshape(knot_span * DOF, rows_count, seg_count, group_size)


def batched_terms(cam_jac, point_jac, residual, prior, window_start):
    seg_count = window_start.shape[0]
    landmarks = window_start.shape[1]
    group_size = min(128, landmarks)
    extended = (KNOTS + ORDER - 1) * DOF

    def one_group(totals, group_index):
        projected, projected_res = landmark_project(cam_jac, point_jac, residual, prior)
        placed_cam = place_knots(cam_jac, window_start)
        placed_proj = place_knots(projected, window_start)
        new_mat = totals[0] + jnp.einsum(
            "ersl,frsl->sef", placed_cam, placed_proj, precision=PRECISE
        )
        new_vec = totals[1] + jnp.einsum(
            "ersl,rsl->se", placed_cam, projected_res, precision=PRECISE
        )
        return ((new_mat, new_vec), None)

    start_totals = (
        jnp.zeros((seg_count, extended, extended), jnp.float32),
        jnp.zeros((seg_count, extended), jnp.float32),
    )
    totals, _ = lax.scan(
        one_group, start_totals, jnp.arange(landmarks // group_size, dtype=jnp.int32)
    )
    return totals


def band_terms(cam_jac, point_jac, residual, prior, window_start):
    projected, projected_res = landmark_project(cam_jac, point_jac, residual, prior)
    pair = jnp.einsum("rmsl,rnsl->slmn", cam_jac, projected, precision=PRECISE)
    vec = jnp.einsum("rmsl,rsl->slm", cam_jac, projected_res, precision=PRECISE)
    seg_count, landmarks = pair.shape[:2]
    blocks = pair.reshape(seg_count, landmarks, ORDER, DOF, ORDER, DOF)
    zero = jnp.zeros((seg_count, landmarks, DOF, DOF), pair.dtype)
    width = 2 * ORDER - 1
    by_start = []
    for a in range(ORDER):
        per_offset = []
        for d in range(width):
            b = a + d - (ORDER - 1)
            per_offset.append(blocks[:, :, a, :, b, :] if 0 <= b < ORDER else zero)
        by_start.append(jnp.stack(per_offset, 2))
    spread = jnp.stack(by_start, 2)
    knot_span = KNOTS + ORDER - 1
    onehot = (
        jnp.arange(knot_span, dtype=jnp.int32)[None, :, None, None]
        == window_start[:, None, :, None] + jnp.arange(ORDER, dtype=jnp.int32)[None, None, None, :]
    ).astype(jnp.float32)
    band = jnp.einsum("sila,sladxy->sidxy", onehot, spread, precision=PRECISE)
    vec_blocks = vec.reshape(seg_count, landmarks, ORDER, DOF)
    dense_vec = jnp.einsum("sila,slax->six", onehot, vec_blocks, precision=PRECISE)
    return band, dense_vec.reshape(seg_count, knot_span * DOF)


def dense_from_band(band):
    seg_count, knot_span, width = band.shape[:3]
    extended = knot_span * DOF
    rows = jnp.transpose(band, (1, 0, 3, 2, 4)).reshape(knot_span, seg_count * DOF, width * DOF)
    within = jnp.arange(width * DOF, dtype=jnp.int32)
    column = jnp.arange(extended, dtype=jnp.int32)
    knot = jnp.arange(knot_span, dtype=jnp.int32)
    select = (
        column[None, None, :]
        == DOF * (knot[:, None, None] - (ORDER - 1)) + within[None, :, None]
    ).astype(jnp.float32)
    placed = jnp.einsum("iak,ikc->iac", rows, select, precision=PRECISE)
    placed = jnp.transpose(placed.reshape(knot_span, seg_count, DOF, extended), (1, 0, 2, 3))
    return placed.reshape(seg_count, extended, extended)


PIVOT = 128


def sweep_kernel(d_ref, o_ref, *pivot_refs):
    count, order, _ = d_ref.shape
    o_ref[...] = d_ref[...]
    lane_row = lax.broadcasted_iota(jnp.int32, (1, PIVOT), 1)
    for blk in range(order // PIVOT):
        lo = blk * PIVOT
        for b in range(count):
            pivot_refs[b][...] = o_ref[b, lo:lo + PIVOT, lo:lo + PIVOT]

        def step(k, rows):
            ahead_at = jnp.minimum(k + 1, PIVOT - 1)
            is_k = lane_row == k
            is_ahead = lane_row == ahead_at
            carried = []
            for p_ref, row in zip(pivot_refs, rows):
                piv = jnp.sum(jnp.where(is_k, row, 0.0), axis=1, keepdims=True)
                link = jnp.sum(jnp.where(is_ahead, row, 0.0), axis=1, keepdims=True)
                inv = 1.0 / piv
                scaled = row * inv
                ahead = p_ref[pl.ds(ahead_at, 1), :]
                carried.append(jnp.where(is_k, link * inv, ahead - link * scaled))
                col = jnp.broadcast_to(
                    jnp.transpose(jnp.broadcast_to(row, (8, PIVOT)))[:, 0:1], (PIVOT, PIVOT)
                )
                upd = p_ref[...] - col * scaled
                p_ref[...] = jnp.where(is_k, col * inv, upd)
                p_ref[pl.ds(k, 1), :] = jnp.where(is_k, -inv, scaled)
            return tuple(carried)

        lax.fori_loop(
            0, PIVOT, step, tuple(p_ref[pl.ds(0, 1), :] for p_ref in pivot_refs), unroll=2
        )
        for b in range(count):
            pneg = pivot_refs[b][...]
            col_blk = o_ref[b, :, lo:lo + PIVOT]
            row_blk = o_ref[b, lo:lo + PIVOT, :]
            t = jnp.dot(col_blk, pneg, precision=PRECISE, preferred_element_type=jnp.float32)
            o_ref[b] = o_ref[b] + jnp.dot(t, row_blk, precision=PRECISE, preferred_element_type=jnp.float32)
            o_ref[b, :, lo:lo + PIVOT] = -t
            o_ref[b, lo:lo + PIVOT, :] = -jnp.dot(pneg, row_blk, precision=PRECISE, preferred_element_type=jnp.float32)
            o_ref[b, lo:lo + PIVOT, lo:lo + PIVOT] = pneg


def negated_inverse(mats):
    count, order, _ = mats.shape
    return pl.pallas_call(
        sweep_kernel,
        out_shape=jax.ShapeDtypeStruct(mats.shape, mats.dtype),
        in_specs=[pl.BlockSpec(memory_space=pltpu.VMEM)],
        out_specs=pl.BlockSpec(memory_space=pltpu.VMEM),
        scratch_shapes=[pltpu.VMEM((PIVOT, PIVOT), jnp.float32)] * count,
    )(mats)


def eliminate(diagonal, coupling, right_side, next_coupling):
    inverse = -negated_inverse(diagonal)
    ahead = jnp.einsum("bij,bjk->bik", next_coupling, inverse, precision=PRECISE)
    behind = jnp.einsum("bji,bjk->bik", coupling, inverse, precision=PRECISE)
    to_next = (
        jnp.einsum("bik,bjk->bij", ahead, next_coupling, precision=PRECISE),
        jnp.einsum("bik,bkj->bij", ahead, coupling, precision=PRECISE),
        jnp.einsum("bik,bk->bi", ahead, right_side, precision=PRECISE),
    )
    to_prev = (
        jnp.einsum("bik,bkj->bij", behind, coupling, precision=PRECISE),
        jnp.einsum("bik,bk->bi", behind, right_side, precision=PRECISE),
    )
    return (to_next, to_prev)


def local(
    cam_diag, cam_lower, cam_rhs, obs_cam_jac, obs_point_jac, obs_residual, point_prior, knot_start
):
    blocks = cam_diag.shape[1]
    border = (ORDER - 1) * DOF
    local_count = cam_rhs.shape[0]
    band, schur_vec = band_terms(
        obs_cam_jac, obs_point_jac, obs_residual, point_prior, knot_start
    )
    band, schur_vec = lax.psum((band, schur_vec), "lm")
    schur_mat = dense_from_band(band)
    arrived_mat, arrived_vec = passed_along(
        (schur_mat[local_count - 1, blocks:, :], schur_vec[local_count - 1, blocks:]), "tm", 1
    )
    spill_mat = jnp.concatenate([arrived_mat[None], schur_mat[:-1, blocks:, :]], 0)
    spill_vec = jnp.concatenate([arrived_vec[None], schur_vec[:-1, blocks:]], 0)
    diagonal = (
        cam_diag.reshape(local_count, blocks, blocks)
        + schur_mat[:, :blocks, :blocks]
        + jnp.pad(spill_mat[:, :, blocks:], ((0, 0), (0, blocks - border), (0, blocks - border)))
    )
    coupling = cam_lower.reshape(local_count, blocks, blocks) + jnp.pad(
        spill_mat[:, :, :blocks], ((0, 0), (0, blocks - border), (0, 0))
    )
    right_side = (
        cam_rhs - schur_vec[:, :blocks] - jnp.pad(spill_vec, ((0, 0), (0, blocks - border)))
    )
    after_coupling = passed_along(coupling[0], "tm", -1)
    pair = eliminate(
        jnp.stack([diagonal[1], diagonal[3]]),
        jnp.stack([coupling[1], coupling[3]]),
        jnp.stack([right_side[1], right_side[3]]),
        jnp.stack([coupling[2], after_coupling]),
    )
    next_first, prev_first = jax.tree.map(lambda x: x[0], pair)
    next_last, prev_last = jax.tree.map(lambda x: x[1], pair)
    mid_diag = diagonal[2] - next_first[0] - prev_last[0]
    mid_coupling = -next_first[1]
    mid_rhs = right_side[2] - next_first[2] - prev_last[1]
    arrived_last = passed_along((next_last[0], next_last[2]), "tm", 1)
    next_mid, prev_mid = jax.tree.map(
        lambda x: x[0],
        eliminate(mid_diag[None], mid_coupling[None], mid_rhs[None], -next_last[1][None]),
    )
    head_diag = diagonal[0] - prev_first[0] - prev_mid[0] - arrived_last[0]
    head_rhs = right_side[0] - prev_first[1] - prev_mid[1] - arrived_last[1]
    arrived = passed_along((next_mid[0], next_mid[1], next_mid[2]), "tm", 1)
    out_diag = head_diag - arrived[0]
    out_coupling = -arrived[1]
    out_rhs = head_rhs - arrived[2]
    return (out_diag, out_coupling, out_rhs[None, :])


def solution(mesh):
    placed = (
        P("tm", None),
        P("tm", None),
        P("tm", None),
        P(None, None, "tm", "lm"),
        P(None, None, "tm", "lm"),
        P(None, "tm", "lm"),
        P("tm", "lm"),
        P("tm", "lm"),
    )
    return jax.shard_map(
        local,
        mesh=mesh,
        in_specs=placed,
        out_specs=(P("tm", None), P("tm", None), P("tm", None)),
        check_vma=False,
    )
```

```python
import jax
import jax.numpy as jnp
from jax import lax
from jax.sharding import PartitionSpec as P
from jax.experimental import pallas as pl
from jax.experimental.pallas import tpu as pltpu

KNOTS = 64
DOF = 6
ORDER = 4


PRECISE = lax.Precision.HIGHEST


def passed_along(block, axis, distance):
    devices = range(lax.axis_size(axis))
    route = [((i - distance) % len(devices), i) for i in devices]
    return lax.ppermute(block, axis, route)


def point_inverse(normal):
    adj_rows = []
    for row_at in range(3):
        entries = []
        for col_at in range(3):
            entries.append(
                normal[(col_at + 1) % 3, (row_at + 1) % 3]
                * normal[(col_at + 2) % 3, (row_at + 2) % 3]
                - normal[(col_at + 1) % 3, (row_at + 2) % 3]
                * normal[(col_at + 2) % 3, (row_at + 1) % 3]
            )
        adj_rows.append(jnp.stack(entries))
    adjugate = jnp.stack(adj_rows)
    determ = (
        normal[0, 0] * adjugate[0, 0]
        + normal[0, 1] * adjugate[1, 0]
        + normal[0, 2] * adjugate[2, 0]
    )
    return adjugate / determ


def landmark_project(cam_jac, point_jac, residual, prior):
    normal = jnp.einsum("rasl,rbsl->absl", point_jac, point_jac, precision=PRECISE)
    normal = normal + prior[None, None] * jnp.eye(3, dtype=jnp.float32)[:, :, None, None]
    inverse = point_inverse(normal)
    cross = jnp.einsum("rasl,rmsl->amsl", point_jac, cam_jac, precision=PRECISE)
    cross_res = jnp.einsum("rasl,rsl->asl", point_jac, residual, precision=PRECISE)
    solved = jnp.einsum("absl,bmsl->amsl", inverse, cross, precision=PRECISE)
    solved_res = jnp.einsum("absl,bsl->asl", inverse, cross_res, precision=PRECISE)
    projected = cam_jac - jnp.einsum("rasl,amsl->rmsl", point_jac, solved, precision=PRECISE)
    projected_res = residual - jnp.einsum("rasl,asl->rsl", point_jac, solved_res, precision=PRECISE)
    return (projected, projected_res)


def place_knots(values, window_start):
    rows_count = values.shape[0]
    seg_count = values.shape[2]
    group_size = values.shape[3]
    knot_span = KNOTS + ORDER - 1
    offsets = jnp.arange(knot_span, dtype=jnp.int32)[:, None, None] - window_start[None]
    onehot = (offsets[:, None] == jnp.arange(ORDER, dtype=jnp.int32)[None, :, None, None]).astype(
        jnp.float32
    )
    shaped = values.reshape(rows_count, ORDER, DOF, seg_count, group_size)
    placed = jnp.einsum("kosl,rodsl->kdrsl", onehot, shaped, precision=PRECISE)
    return placed.reshape(knot_span * DOF, rows_count, seg_count, group_size)


def batched_terms(cam_jac, point_jac, residual, prior, window_start):
    seg_count = window_start.shape[0]
    landmarks = window_start.shape[1]
    group_size = min(128, landmarks)
    extended = (KNOTS + ORDER - 1) * DOF

    def one_group(totals, group_index):
        projected, projected_res = landmark_project(cam_jac, point_jac, residual, prior)
        placed_cam = place_knots(cam_jac, window_start)
        placed_proj = place_knots(projected, window_start)
        new_mat = totals[0] + jnp.einsum(
            "ersl,frsl->sef", placed_cam, placed_proj, precision=PRECISE
        )
        new_vec = totals[1] + jnp.einsum(
            "ersl,rsl->se", placed_cam, projected_res, precision=PRECISE
        )
        return ((new_mat, new_vec), None)

    start_totals = (
        jnp.zeros((seg_count, extended, extended), jnp.float32),
        jnp.zeros((seg_count, extended), jnp.float32),
    )
    totals, _ = lax.scan(
        one_group, start_totals, jnp.arange(landmarks // group_size, dtype=jnp.int32)
    )
    return totals


def band_terms(cam_jac, point_jac, residual, prior, window_start):
    projected, projected_res = landmark_project(cam_jac, point_jac, residual, prior)
    pair = jnp.einsum("rmsl,rnsl->slmn", cam_jac, projected, precision=PRECISE)
    vec = jnp.einsum("rmsl,rsl->slm", cam_jac, projected_res, precision=PRECISE)
    seg_count, landmarks = pair.shape[:2]
    blocks = pair.reshape(seg_count, landmarks, ORDER, DOF, ORDER, DOF)
    zero = jnp.zeros((seg_count, landmarks, DOF, DOF), pair.dtype)
    width = 2 * ORDER - 1
    by_start = []
    for a in range(ORDER):
        per_offset = []
        for d in range(width):
            b = a + d - (ORDER - 1)
            per_offset.append(blocks[:, :, a, :, b, :] if 0 <= b < ORDER else zero)
        by_start.append(jnp.stack(per_offset, 2))
    spread = jnp.stack(by_start, 2)
    knot_span = KNOTS + ORDER - 1
    onehot = (
        jnp.arange(knot_span, dtype=jnp.int32)[None, :, None, None]
        == window_start[:, None, :, None] + jnp.arange(ORDER, dtype=jnp.int32)[None, None, None, :]
    ).astype(jnp.float32)
    band = jnp.einsum("sila,sladxy->sidxy", onehot, spread, precision=PRECISE)
    vec_blocks = vec.reshape(seg_count, landmarks, ORDER, DOF)
    dense_vec = jnp.einsum("sila,slax->six", onehot, vec_blocks, precision=PRECISE)
    return band, dense_vec.reshape(seg_count, knot_span * DOF)


def summed_over(band, vec, axis):
    size = lax.axis_size(axis)
    assert size & (size - 1) == 0
    seg_count = vec.shape[0]
    packed = jnp.concatenate([band.reshape(seg_count, -1), vec], 1)
    bit = 1
    while bit < size:
        packed = packed + lax.ppermute(packed, axis, [(i, i ^ bit) for i in range(size)])
        bit *= 2
    return packed[:, : band[0].size].reshape(band.shape), packed[:, band[0].size :]


def dense_from_band(band):
    seg_count, knot_span, width = band.shape[:3]
    extended = knot_span * DOF
    rows = jnp.transpose(band, (1, 0, 3, 2, 4)).reshape(knot_span, seg_count * DOF, width * DOF)
    within = jnp.arange(width * DOF, dtype=jnp.int32)
    column = jnp.arange(extended, dtype=jnp.int32)
    knot = jnp.arange(knot_span, dtype=jnp.int32)
    select = (
        column[None, None, :]
        == DOF * (knot[:, None, None] - (ORDER - 1)) + within[None, :, None]
    ).astype(jnp.float32)
    placed = jnp.einsum("iak,ikc->iac", rows, select, precision=PRECISE)
    placed = jnp.transpose(placed.reshape(knot_span, seg_count, DOF, extended), (1, 0, 2, 3))
    return placed.reshape(seg_count, extended, extended)


PIVOT = 128


def sweep_kernel(d_ref, o_ref, *pivot_refs):
    count, order, _ = d_ref.shape
    o_ref[...] = d_ref[...]
    lane_row = lax.broadcasted_iota(jnp.int32, (1, PIVOT), 1)
    for blk in range(order // PIVOT):
        lo = blk * PIVOT
        for b in range(count):
            pivot_refs[b][...] = o_ref[b, lo:lo + PIVOT, lo:lo + PIVOT]

        def step(k, rows):
            ahead_at = jnp.minimum(k + 1, PIVOT - 1)
            is_k = lane_row == k
            is_ahead = lane_row == ahead_at
            carried = []
            for p_ref, row in zip(pivot_refs, rows):
                piv = jnp.sum(jnp.where(is_k, row, 0.0), axis=1, keepdims=True)
                link = jnp.sum(jnp.where(is_ahead, row, 0.0), axis=1, keepdims=True)
                inv = 1.0 / piv
                scaled = row * inv
                ahead = p_ref[pl.ds(ahead_at, 1), :]
                carried.append(jnp.where(is_k, link * inv, ahead - link * scaled))
                col = jnp.broadcast_to(
                    jnp.transpose(jnp.broadcast_to(row, (8, PIVOT)))[:, 0:1], (PIVOT, PIVOT)
                )
                upd = p_ref[...] - col * scaled
                p_ref[...] = jnp.where(is_k, col * inv, upd)
                p_ref[pl.ds(k, 1), :] = jnp.where(is_k, -inv, scaled)
            return tuple(carried)

        lax.fori_loop(
            0, PIVOT, step, tuple(p_ref[pl.ds(0, 1), :] for p_ref in pivot_refs), unroll=2
        )
        for b in range(count):
            pneg = pivot_refs[b][...]
            col_blk = o_ref[b, :, lo:lo + PIVOT]
            row_blk = o_ref[b, lo:lo + PIVOT, :]
            t = jnp.dot(col_blk, pneg, precision=PRECISE, preferred_element_type=jnp.float32)
            o_ref[b] = o_ref[b] + jnp.dot(t, row_blk, precision=PRECISE, preferred_element_type=jnp.float32)
            o_ref[b, :, lo:lo + PIVOT] = -t
            o_ref[b, lo:lo + PIVOT, :] = -jnp.dot(pneg, row_blk, precision=PRECISE, preferred_element_type=jnp.float32)
            o_ref[b, lo:lo + PIVOT, lo:lo + PIVOT] = pneg


def negated_inverse(mats):
    count, order, _ = mats.shape
    return pl.pallas_call(
        sweep_kernel,
        out_shape=jax.ShapeDtypeStruct(mats.shape, mats.dtype),
        in_specs=[pl.BlockSpec(memory_space=pltpu.VMEM)],
        out_specs=pl.BlockSpec(memory_space=pltpu.VMEM),
        scratch_shapes=[pltpu.VMEM((PIVOT, PIVOT), jnp.float32)] * count,
    )(mats)


def eliminate(diagonal, coupling, right_side, next_coupling):
    inverse = -negated_inverse(diagonal)
    ahead = jnp.einsum("bij,bjk->bik", next_coupling, inverse, precision=PRECISE)
    behind = jnp.einsum("bji,bjk->bik", coupling, inverse, precision=PRECISE)
    to_next = (
        jnp.einsum("bik,bjk->bij", ahead, next_coupling, precision=PRECISE),
        jnp.einsum("bik,bkj->bij", ahead, coupling, precision=PRECISE),
        jnp.einsum("bik,bk->bi", ahead, right_side, precision=PRECISE),
    )
    to_prev = (
        jnp.einsum("bik,bkj->bij", behind, coupling, precision=PRECISE),
        jnp.einsum("bik,bk->bi", behind, right_side, precision=PRECISE),
    )
    return (to_next, to_prev)


def local(
    cam_diag, cam_lower, cam_rhs, obs_cam_jac, obs_point_jac, obs_residual, point_prior, knot_start
):
    blocks = cam_diag.shape[1]
    border = (ORDER - 1) * DOF
    local_count = cam_rhs.shape[0]
    band, schur_vec = band_terms(
        obs_cam_jac, obs_point_jac, obs_residual, point_prior, knot_start
    )
    band, schur_vec = summed_over(band, schur_vec, "lm")
    schur_mat = dense_from_band(band)
    arrived_mat, arrived_vec = passed_along(
        (schur_mat[local_count - 1, blocks:, :], schur_vec[local_count - 1, blocks:]), "tm", 1
    )
    spill_mat = jnp.concatenate([arrived_mat[None], schur_mat[:-1, blocks:, :]], 0)
    spill_vec = jnp.concatenate([arrived_vec[None], schur_vec[:-1, blocks:]], 0)
    diagonal = (
        cam_diag.reshape(local_count, blocks, blocks)
        + schur_mat[:, :blocks, :blocks]
        + jnp.pad(spill_mat[:, :, blocks:], ((0, 0), (0, blocks - border), (0, blocks - border)))
    )
    coupling = cam_lower.reshape(local_count, blocks, blocks) + jnp.pad(
        spill_mat[:, :, :blocks], ((0, 0), (0, blocks - border), (0, 0))
    )
    right_side = (
        cam_rhs - schur_vec[:, :blocks] - jnp.pad(spill_vec, ((0, 0), (0, blocks - border)))
    )
    after_coupling = passed_along(coupling[0], "tm", -1)
    pair = eliminate(
        jnp.stack([diagonal[1], diagonal[3]]),
        jnp.stack([coupling[1], coupling[3]]),
        jnp.stack([right_side[1], right_side[3]]),
        jnp.stack([coupling[2], after_coupling]),
    )
    next_first, prev_first = jax.tree.map(lambda x: x[0], pair)
    next_last, prev_last = jax.tree.map(lambda x: x[1], pair)
    mid_diag = diagonal[2] - next_first[0] - prev_last[0]
    mid_coupling = -next_first[1]
    mid_rhs = right_side[2] - next_first[2] - prev_last[1]
    arrived_last = passed_along((next_last[0], next_last[2]), "tm", 1)
    next_mid, prev_mid = jax.tree.map(
        lambda x: x[0],
        eliminate(mid_diag[None], mid_coupling[None], mid_rhs[None], -next_last[1][None]),
    )
    head_diag = diagonal[0] - prev_first[0] - prev_mid[0] - arrived_last[0]
    head_rhs = right_side[0] - prev_first[1] - prev_mid[1] - arrived_last[1]
    arrived = passed_along((next_mid[0], next_mid[1], next_mid[2]), "tm", 1)
    out_diag = head_diag - arrived[0]
    out_coupling = -arrived[1]
    out_rhs = head_rhs - arrived[2]
    return (out_diag, out_coupling, out_rhs[None, :])


def solution(mesh):
    placed = (
        P("tm", None),
        P("tm", None),
        P("tm", None),
        P(None, None, "tm", "lm"),
        P(None, None, "tm", "lm"),
        P(None, "tm", "lm"),
        P("tm", "lm"),
        P("tm", "lm"),
    )
    return jax.shard_map(
        local,
        mesh=mesh,
        in_specs=placed,
        out_specs=(P("tm", None), P("tm", None), P("tm", None)),
        check_vma=False,
    )
```

```python
import jax
import jax.numpy as jnp
from jax import lax
from jax.sharding import PartitionSpec as P
from jax.experimental import pallas as pl
from jax.experimental.pallas import tpu as pltpu

KNOTS = 64
DOF = 6
ORDER = 4


PRECISE = lax.Precision.HIGHEST


def passed_along(block, axis, distance):
    devices = range(lax.axis_size(axis))
    route = [((i - distance) % len(devices), i) for i in devices]
    return lax.ppermute(block, axis, route)


def point_inverse(normal):
    adj_rows = []
    for row_at in range(3):
        entries = []
        for col_at in range(3):
            entries.append(
                normal[(col_at + 1) % 3, (row_at + 1) % 3]
                * normal[(col_at + 2) % 3, (row_at + 2) % 3]
                - normal[(col_at + 1) % 3, (row_at + 2) % 3]
                * normal[(col_at + 2) % 3, (row_at + 1) % 3]
            )
        adj_rows.append(jnp.stack(entries))
    adjugate = jnp.stack(adj_rows)
    determ = (
        normal[0, 0] * adjugate[0, 0]
        + normal[0, 1] * adjugate[1, 0]
        + normal[0, 2] * adjugate[2, 0]
    )
    return adjugate / determ


def landmark_project(cam_jac, point_jac, residual, prior):
    normal = jnp.einsum("rasl,rbsl->absl", point_jac, point_jac, precision=PRECISE)
    normal = normal + prior[None, None] * jnp.eye(3, dtype=jnp.float32)[:, :, None, None]
    inverse = point_inverse(normal)
    cross = jnp.einsum("rasl,rmsl->amsl", point_jac, cam_jac, precision=PRECISE)
    cross_res = jnp.einsum("rasl,rsl->asl", point_jac, residual, precision=PRECISE)
    solved = jnp.einsum("absl,bmsl->amsl", inverse, cross, precision=PRECISE)
    solved_res = jnp.einsum("absl,bsl->asl", inverse, cross_res, precision=PRECISE)
    projected = cam_jac - jnp.einsum("rasl,amsl->rmsl", point_jac, solved, precision=PRECISE)
    projected_res = residual - jnp.einsum("rasl,asl->rsl", point_jac, solved_res, precision=PRECISE)
    return (projected, projected_res)


def place_knots(values, window_start):
    rows_count = values.shape[0]
    seg_count = values.shape[2]
    group_size = values.shape[3]
    knot_span = KNOTS + ORDER - 1
    offsets = jnp.arange(knot_span, dtype=jnp.int32)[:, None, None] - window_start[None]
    onehot = (offsets[:, None] == jnp.arange(ORDER, dtype=jnp.int32)[None, :, None, None]).astype(
        jnp.float32
    )
    shaped = values.reshape(rows_count, ORDER, DOF, seg_count, group_size)
    placed = jnp.einsum("kosl,rodsl->kdrsl", onehot, shaped, precision=PRECISE)
    return placed.reshape(knot_span * DOF, rows_count, seg_count, group_size)


def batched_terms(cam_jac, point_jac, residual, prior, window_start):
    seg_count = window_start.shape[0]
    landmarks = window_start.shape[1]
    group_size = min(128, landmarks)
    extended = (KNOTS + ORDER - 1) * DOF

    def one_group(totals, group_index):
        projected, projected_res = landmark_project(cam_jac, point_jac, residual, prior)
        placed_cam = place_knots(cam_jac, window_start)
        placed_proj = place_knots(projected, window_start)
        new_mat = totals[0] + jnp.einsum(
            "ersl,frsl->sef", placed_cam, placed_proj, precision=PRECISE
        )
        new_vec = totals[1] + jnp.einsum(
            "ersl,rsl->se", placed_cam, projected_res, precision=PRECISE
        )
        return ((new_mat, new_vec), None)

    start_totals = (
        jnp.zeros((seg_count, extended, extended), jnp.float32),
        jnp.zeros((seg_count, extended), jnp.float32),
    )
    totals, _ = lax.scan(
        one_group, start_totals, jnp.arange(landmarks // group_size, dtype=jnp.int32)
    )
    return totals


def band_terms(cam_jac, point_jac, residual, prior, window_start):
    projected, projected_res = landmark_project(cam_jac, point_jac, residual, prior)
    pair = jnp.einsum("rmsl,rnsl->slmn", cam_jac, projected, precision=PRECISE)
    vec = jnp.einsum("rmsl,rsl->slm", cam_jac, projected_res, precision=PRECISE)
    seg_count, landmarks = pair.shape[:2]
    blocks = pair.reshape(seg_count, landmarks, ORDER, DOF, ORDER, DOF)
    zero = jnp.zeros((seg_count, landmarks, DOF, DOF), pair.dtype)
    width = 2 * ORDER - 1
    by_start = []
    for a in range(ORDER):
        per_offset = []
        for d in range(width):
            b = a + d - (ORDER - 1)
            per_offset.append(blocks[:, :, a, :, b, :] if 0 <= b < ORDER else zero)
        by_start.append(jnp.stack(per_offset, 2))
    spread = jnp.stack(by_start, 2)
    knot_span = KNOTS + ORDER - 1
    onehot = (
        jnp.arange(knot_span, dtype=jnp.int32)[None, :, None, None]
        == window_start[:, None, :, None] + jnp.arange(ORDER, dtype=jnp.int32)[None, None, None, :]
    ).astype(jnp.float32)
    band = jnp.einsum("sila,sladxy->sidxy", onehot, spread, precision=PRECISE)
    vec_blocks = vec.reshape(seg_count, landmarks, ORDER, DOF)
    dense_vec = jnp.einsum("sila,slax->six", onehot, vec_blocks, precision=PRECISE)
    return band, dense_vec.reshape(seg_count, knot_span * DOF)


def summed_over(band, vec, axis):
    size = lax.axis_size(axis)
    assert size & (size - 1) == 0
    seg_count = vec.shape[0]
    packed = jnp.concatenate([band.reshape(seg_count, -1), vec], 1)
    bit = 1
    while bit < size:
        packed = packed + lax.ppermute(packed, axis, [(i, i ^ bit) for i in range(size)])
        bit *= 2
    return packed[:, : band[0].size].reshape(band.shape), packed[:, band[0].size :]


def dense_from_band(band):
    seg_count, knot_span, width = band.shape[:3]
    extended = knot_span * DOF
    rows = jnp.transpose(band, (1, 0, 3, 2, 4)).reshape(knot_span, seg_count * DOF, width * DOF)
    within = jnp.arange(width * DOF, dtype=jnp.int32)
    column = jnp.arange(extended, dtype=jnp.int32)
    knot = jnp.arange(knot_span, dtype=jnp.int32)
    select = (
        column[None, None, :]
        == DOF * (knot[:, None, None] - (ORDER - 1)) + within[None, :, None]
    ).astype(jnp.float32)
    placed = jnp.einsum("iak,ikc->iac", rows, select, precision=PRECISE)
    placed = jnp.transpose(placed.reshape(knot_span, seg_count, DOF, extended), (1, 0, 2, 3))
    return placed.reshape(seg_count, extended, extended)


PIVOT = 128


def sweep_kernel(d_ref, o_ref, *pivot_refs):
    count, order, _ = d_ref.shape
    o_ref[...] = d_ref[...]
    lane_row = lax.broadcasted_iota(jnp.int32, (1, PIVOT), 1)
    for blk in range(order // PIVOT):
        lo = blk * PIVOT
        for b in range(count):
            pivot_refs[b][...] = o_ref[b, lo:lo + PIVOT, lo:lo + PIVOT]

        def lane_value(row, at):
            return jnp.sum(jnp.where(lane_row == at, row, 0.0), axis=1, keepdims=True)

        def pivot_step(row, ahead, k, ahead_at):
            inv = 1.0 / lane_value(row, k)
            scaled = row * inv
            link = lane_value(row, ahead_at)
            return jnp.where(lane_row == k, link * inv, ahead - link * scaled), scaled, inv

        def full_update(p_ref, row, scaled, inv, k):
            is_k = lane_row == k
            col = jnp.broadcast_to(
                jnp.transpose(jnp.broadcast_to(row, (8, PIVOT)))[:, 0:1], (PIVOT, PIVOT)
            )
            upd = p_ref[...] - col * scaled
            p_ref[...] = jnp.where(is_k, col * inv, upd)
            p_ref[pl.ds(k, 1), :] = jnp.where(is_k, -inv, scaled)

        def step(k, carried):
            ahead_at = jnp.minimum(k + 1, PIVOT - 1)
            out = []
            for p_ref, (row, prev_row, prev_scaled, prev_inv) in zip(pivot_refs, carried):
                ahead = p_ref[pl.ds(ahead_at, 1), :]
                link = lane_value(prev_row, ahead_at)
                ahead = jnp.where(
                    lane_row == k - 1, link * prev_inv, ahead - link * prev_scaled
                )
                next_row, scaled, inv = pivot_step(row, ahead, k, ahead_at)
                full_update(p_ref, prev_row, prev_scaled, prev_inv, k - 1)
                out.append((next_row, row, scaled, inv))
            return tuple(out)

        first = []
        for p_ref in pivot_refs:
            row = p_ref[pl.ds(0, 1), :]
            next_row, scaled, inv = pivot_step(row, p_ref[pl.ds(1, 1), :], 0, 1)
            first.append((next_row, row, scaled, inv))
        last = lax.fori_loop(1, PIVOT, step, tuple(first), unroll=2)
        for p_ref, (_, prev_row, prev_scaled, prev_inv) in zip(pivot_refs, last):
            full_update(p_ref, prev_row, prev_scaled, prev_inv, PIVOT - 1)
        for b in range(count):
            pneg = pivot_refs[b][...]
            col_blk = o_ref[b, :, lo:lo + PIVOT]
            row_blk = o_ref[b, lo:lo + PIVOT, :]
            t = jnp.dot(col_blk, pneg, precision=PRECISE, preferred_element_type=jnp.float32)
            o_ref[b] = o_ref[b] + jnp.dot(t, row_blk, precision=PRECISE, preferred_element_type=jnp.float32)
            o_ref[b, :, lo:lo + PIVOT] = -t
            o_ref[b, lo:lo + PIVOT, :] = -jnp.dot(pneg, row_blk, precision=PRECISE, preferred_element_type=jnp.float32)
            o_ref[b, lo:lo + PIVOT, lo:lo + PIVOT] = pneg


def negated_inverse(mats):
    count, order, _ = mats.shape
    return pl.pallas_call(
        sweep_kernel,
        out_shape=jax.ShapeDtypeStruct(mats.shape, mats.dtype),
        in_specs=[pl.BlockSpec(memory_space=pltpu.VMEM)],
        out_specs=pl.BlockSpec(memory_space=pltpu.VMEM),
        scratch_shapes=[pltpu.VMEM((PIVOT, PIVOT), jnp.float32)] * count,
    )(mats)


def eliminate(diagonal, coupling, right_side, next_coupling):
    inverse = -negated_inverse(diagonal)
    ahead = jnp.einsum("bij,bjk->bik", next_coupling, inverse, precision=PRECISE)
    behind = jnp.einsum("bji,bjk->bik", coupling, inverse, precision=PRECISE)
    to_next = (
        jnp.einsum("bik,bjk->bij", ahead, next_coupling, precision=PRECISE),
        jnp.einsum("bik,bkj->bij", ahead, coupling, precision=PRECISE),
        jnp.einsum("bik,bk->bi", ahead, right_side, precision=PRECISE),
    )
    to_prev = (
        jnp.einsum("bik,bkj->bij", behind, coupling, precision=PRECISE),
        jnp.einsum("bik,bk->bi", behind, right_side, precision=PRECISE),
    )
    return (to_next, to_prev)


def local(
    cam_diag, cam_lower, cam_rhs, obs_cam_jac, obs_point_jac, obs_residual, point_prior, knot_start
):
    blocks = cam_diag.shape[1]
    border = (ORDER - 1) * DOF
    local_count = cam_rhs.shape[0]
    band, schur_vec = band_terms(
        obs_cam_jac, obs_point_jac, obs_residual, point_prior, knot_start
    )
    band, schur_vec = summed_over(band, schur_vec, "lm")
    schur_mat = dense_from_band(band)
    arrived_mat, arrived_vec = passed_along(
        (schur_mat[local_count - 1, blocks:, :], schur_vec[local_count - 1, blocks:]), "tm", 1
    )
    spill_mat = jnp.concatenate([arrived_mat[None], schur_mat[:-1, blocks:, :]], 0)
    spill_vec = jnp.concatenate([arrived_vec[None], schur_vec[:-1, blocks:]], 0)
    diagonal = (
        cam_diag.reshape(local_count, blocks, blocks)
        + schur_mat[:, :blocks, :blocks]
        + jnp.pad(spill_mat[:, :, blocks:], ((0, 0), (0, blocks - border), (0, blocks - border)))
    )
    coupling = cam_lower.reshape(local_count, blocks, blocks) + jnp.pad(
        spill_mat[:, :, :blocks], ((0, 0), (0, blocks - border), (0, 0))
    )
    right_side = (
        cam_rhs - schur_vec[:, :blocks] - jnp.pad(spill_vec, ((0, 0), (0, blocks - border)))
    )
    after_coupling = passed_along(coupling[0], "tm", -1)
    pair = eliminate(
        jnp.stack([diagonal[1], diagonal[3]]),
        jnp.stack([coupling[1], coupling[3]]),
        jnp.stack([right_side[1], right_side[3]]),
        jnp.stack([coupling[2], after_coupling]),
    )
    next_first, prev_first = jax.tree.map(lambda x: x[0], pair)
    next_last, prev_last = jax.tree.map(lambda x: x[1], pair)
    mid_diag = diagonal[2] - next_first[0] - prev_last[0]
    mid_coupling = -next_first[1]
    mid_rhs = right_side[2] - next_first[2] - prev_last[1]
    arrived_last = passed_along((next_last[0], next_last[2]), "tm", 1)
    next_mid, prev_mid = jax.tree.map(
        lambda x: x[0],
        eliminate(mid_diag[None], mid_coupling[None], mid_rhs[None], -next_last[1][None]),
    )
    head_diag = diagonal[0] - prev_first[0] - prev_mid[0] - arrived_last[0]
    head_rhs = right_side[0] - prev_first[1] - prev_mid[1] - arrived_last[1]
    arrived = passed_along((next_mid[0], next_mid[1], next_mid[2]), "tm", 1)
    out_diag = head_diag - arrived[0]
    out_coupling = -arrived[1]
    out_rhs = head_rhs - arrived[2]
    return (out_diag, out_coupling, out_rhs[None, :])


def solution(mesh):
    placed = (
        P("tm", None),
        P("tm", None),
        P("tm", None),
        P(None, None, "tm", "lm"),
        P(None, None, "tm", "lm"),
        P(None, "tm", "lm"),
        P("tm", "lm"),
        P("tm", "lm"),
    )
    return jax.shard_map(
        local,
        mesh=mesh,
        in_specs=placed,
        out_specs=(P("tm", None), P("tm", None), P("tm", None)),
        check_vma=False,
    )
```

```python
import jax
import jax.numpy as jnp
from jax import lax
from jax.sharding import PartitionSpec as P
from jax.experimental import pallas as pl
from jax.experimental.pallas import tpu as pltpu

KNOTS = 64
DOF = 6
ORDER = 4


PRECISE = lax.Precision.HIGHEST


def passed_along(block, axis, distance):
    devices = range(lax.axis_size(axis))
    route = [((i - distance) % len(devices), i) for i in devices]
    return lax.ppermute(block, axis, route)


def point_inverse(normal):
    adj_rows = []
    for row_at in range(3):
        entries = []
        for col_at in range(3):
            entries.append(
                normal[(col_at + 1) % 3, (row_at + 1) % 3]
                * normal[(col_at + 2) % 3, (row_at + 2) % 3]
                - normal[(col_at + 1) % 3, (row_at + 2) % 3]
                * normal[(col_at + 2) % 3, (row_at + 1) % 3]
            )
        adj_rows.append(jnp.stack(entries))
    adjugate = jnp.stack(adj_rows)
    determ = (
        normal[0, 0] * adjugate[0, 0]
        + normal[0, 1] * adjugate[1, 0]
        + normal[0, 2] * adjugate[2, 0]
    )
    return adjugate / determ


def landmark_project(cam_jac, point_jac, residual, prior):
    normal = jnp.einsum("rasl,rbsl->absl", point_jac, point_jac, precision=PRECISE)
    normal = normal + prior[None, None] * jnp.eye(3, dtype=jnp.float32)[:, :, None, None]
    inverse = point_inverse(normal)
    cross = jnp.einsum("rasl,rmsl->amsl", point_jac, cam_jac, precision=PRECISE)
    cross_res = jnp.einsum("rasl,rsl->asl", point_jac, residual, precision=PRECISE)
    solved = jnp.einsum("absl,bmsl->amsl", inverse, cross, precision=PRECISE)
    solved_res = jnp.einsum("absl,bsl->asl", inverse, cross_res, precision=PRECISE)
    projected = cam_jac - jnp.einsum("rasl,amsl->rmsl", point_jac, solved, precision=PRECISE)
    projected_res = residual - jnp.einsum("rasl,asl->rsl", point_jac, solved_res, precision=PRECISE)
    return (projected, projected_res)


def place_knots(values, window_start):
    rows_count = values.shape[0]
    seg_count = values.shape[2]
    group_size = values.shape[3]
    knot_span = KNOTS + ORDER - 1
    offsets = jnp.arange(knot_span, dtype=jnp.int32)[:, None, None] - window_start[None]
    onehot = (offsets[:, None] == jnp.arange(ORDER, dtype=jnp.int32)[None, :, None, None]).astype(
        jnp.float32
    )
    shaped = values.reshape(rows_count, ORDER, DOF, seg_count, group_size)
    placed = jnp.einsum("kosl,rodsl->kdrsl", onehot, shaped, precision=PRECISE)
    return placed.reshape(knot_span * DOF, rows_count, seg_count, group_size)


def batched_terms(cam_jac, point_jac, residual, prior, window_start):
    seg_count = window_start.shape[0]
    landmarks = window_start.shape[1]
    group_size = min(128, landmarks)
    extended = (KNOTS + ORDER - 1) * DOF

    def one_group(totals, group_index):
        projected, projected_res = landmark_project(cam_jac, point_jac, residual, prior)
        placed_cam = place_knots(cam_jac, window_start)
        placed_proj = place_knots(projected, window_start)
        new_mat = totals[0] + jnp.einsum(
            "ersl,frsl->sef", placed_cam, placed_proj, precision=PRECISE
        )
        new_vec = totals[1] + jnp.einsum(
            "ersl,rsl->se", placed_cam, projected_res, precision=PRECISE
        )
        return ((new_mat, new_vec), None)

    start_totals = (
        jnp.zeros((seg_count, extended, extended), jnp.float32),
        jnp.zeros((seg_count, extended), jnp.float32),
    )
    totals, _ = lax.scan(
        one_group, start_totals, jnp.arange(landmarks // group_size, dtype=jnp.int32)
    )
    return totals


def band_terms(cam_jac, point_jac, residual, prior, window_start):
    projected, projected_res = landmark_project(cam_jac, point_jac, residual, prior)
    pair = jnp.einsum("rmsl,rnsl->slmn", cam_jac, projected, precision=PRECISE)
    vec = jnp.einsum("rmsl,rsl->slm", cam_jac, projected_res, precision=PRECISE)
    seg_count, landmarks = pair.shape[:2]
    blocks = pair.reshape(seg_count, landmarks, ORDER, DOF, ORDER, DOF)
    zero = jnp.zeros((seg_count, landmarks, DOF, DOF), pair.dtype)
    width = 2 * ORDER - 1
    by_start = []
    for a in range(ORDER):
        per_offset = []
        for d in range(width):
            b = a + d - (ORDER - 1)
            per_offset.append(blocks[:, :, a, :, b, :] if 0 <= b < ORDER else zero)
        by_start.append(jnp.stack(per_offset, 2))
    spread = jnp.stack(by_start, 2)
    knot_span = KNOTS + ORDER - 1
    onehot = (
        jnp.arange(knot_span, dtype=jnp.int32)[None, :, None, None]
        == window_start[:, None, :, None] + jnp.arange(ORDER, dtype=jnp.int32)[None, None, None, :]
    ).astype(jnp.float32)
    band = jnp.einsum("sila,sladxy->sidxy", onehot, spread, precision=PRECISE)
    vec_blocks = vec.reshape(seg_count, landmarks, ORDER, DOF)
    dense_vec = jnp.einsum("sila,slax->six", onehot, vec_blocks, precision=PRECISE)
    return band, dense_vec.reshape(seg_count, knot_span * DOF)


def summed_over(band, vec, axis):
    size = lax.axis_size(axis)
    assert size & (size - 1) == 0
    seg_count = vec.shape[0]
    packed = jnp.concatenate([band.reshape(seg_count, -1), vec], 1)
    bit = 1
    while bit < size:
        packed = packed + lax.ppermute(packed, axis, [(i, i ^ bit) for i in range(size)])
        bit *= 2
    return packed[:, : band[0].size].reshape(band.shape), packed[:, band[0].size :]


def dense_from_band(band):
    seg_count, knot_span, width = band.shape[:3]
    extended = knot_span * DOF
    rows = jnp.transpose(band, (1, 0, 3, 2, 4)).reshape(knot_span, seg_count * DOF, width * DOF)
    within = jnp.arange(width * DOF, dtype=jnp.int32)
    column = jnp.arange(extended, dtype=jnp.int32)
    knot = jnp.arange(knot_span, dtype=jnp.int32)
    select = (
        column[None, None, :]
        == DOF * (knot[:, None, None] - (ORDER - 1)) + within[None, :, None]
    ).astype(jnp.float32)
    placed = jnp.einsum("iak,ikc->iac", rows, select, precision=PRECISE)
    placed = jnp.transpose(placed.reshape(knot_span, seg_count, DOF, extended), (1, 0, 2, 3))
    return placed.reshape(seg_count, extended, extended)


PIVOT = 128


def sweep_kernel(d_ref, o_ref, *pivot_refs):
    count, order, _ = d_ref.shape
    o_ref[...] = d_ref[...]
    lane_row = lax.broadcasted_iota(jnp.int32, (1, PIVOT), 1)
    for blk in range(order // PIVOT):
        lo = blk * PIVOT
        for b in range(count):
            pivot_refs[b][...] = o_ref[b, lo:lo + PIVOT, lo:lo + PIVOT]

        def lane_value(row, at):
            return jnp.sum(jnp.where(lane_row == at, row, 0.0), axis=1, keepdims=True)

        def pivot_step(row, ahead, k, ahead_at):
            inv = 1.0 / lane_value(row, k)
            scaled = row * inv
            link = lane_value(row, ahead_at)
            return jnp.where(lane_row == k, link * inv, ahead - link * scaled), scaled, inv

        def full_update(p_ref, row, scaled, inv, k):
            is_k = lane_row == k
            col = jnp.broadcast_to(
                jnp.transpose(jnp.broadcast_to(row, (8, PIVOT)))[:, 0:1], (PIVOT, PIVOT)
            )
            upd = p_ref[...] - col * scaled
            p_ref[...] = jnp.where(is_k, col * inv, upd)
            p_ref[pl.ds(k, 1), :] = jnp.where(is_k, -inv, scaled)

        def step(k, carried):
            ahead_at = jnp.minimum(k + 1, PIVOT - 1)
            out = []
            for p_ref, (row, prev_row, prev_scaled, prev_inv) in zip(pivot_refs, carried):
                ahead = p_ref[pl.ds(ahead_at, 1), :]
                link = lane_value(prev_row, ahead_at)
                ahead = jnp.where(
                    lane_row == k - 1, link * prev_inv, ahead - link * prev_scaled
                )
                next_row, scaled, inv = pivot_step(row, ahead, k, ahead_at)
                full_update(p_ref, prev_row, prev_scaled, prev_inv, k - 1)
                out.append((next_row, row, scaled, inv))
            return tuple(out)

        first = []
        for p_ref in pivot_refs:
            row = p_ref[pl.ds(0, 1), :]
            next_row, scaled, inv = pivot_step(row, p_ref[pl.ds(1, 1), :], 0, 1)
            first.append((next_row, row, scaled, inv))
        last = lax.fori_loop(1, PIVOT, step, tuple(first), unroll=2)
        for p_ref, (_, prev_row, prev_scaled, prev_inv) in zip(pivot_refs, last):
            full_update(p_ref, prev_row, prev_scaled, prev_inv, PIVOT - 1)
        for b in range(count):
            pneg = pivot_refs[b][...]
            col_blk = o_ref[b, :, lo:lo + PIVOT]
            row_blk = o_ref[b, lo:lo + PIVOT, :]
            t = jnp.dot(col_blk, pneg, precision=PRECISE, preferred_element_type=jnp.float32)
            o_ref[b] = o_ref[b] + jnp.dot(t, row_blk, precision=PRECISE, preferred_element_type=jnp.float32)
            o_ref[b, :, lo:lo + PIVOT] = -t
            o_ref[b, lo:lo + PIVOT, :] = -jnp.dot(pneg, row_blk, precision=PRECISE, preferred_element_type=jnp.float32)
            o_ref[b, lo:lo + PIVOT, lo:lo + PIVOT] = pneg


def negated_inverse(mats):
    count, order, _ = mats.shape
    return pl.pallas_call(
        sweep_kernel,
        out_shape=jax.ShapeDtypeStruct(mats.shape, mats.dtype),
        in_specs=[pl.BlockSpec(memory_space=pltpu.VMEM)],
        out_specs=pl.BlockSpec(memory_space=pltpu.VMEM),
        scratch_shapes=[pltpu.VMEM((PIVOT, PIVOT), jnp.float32)] * count,
    )(mats)


def eliminate(inverse, coupling, right_side, next_coupling):
    ahead = jnp.einsum("bij,bjk->bik", next_coupling, inverse, precision=PRECISE)
    behind = jnp.einsum("bji,bjk->bik", coupling, inverse, precision=PRECISE)
    to_next = (
        jnp.einsum("bik,bjk->bij", ahead, next_coupling, precision=PRECISE),
        jnp.einsum("bik,bkj->bij", ahead, coupling, precision=PRECISE),
        jnp.einsum("bik,bk->bi", ahead, right_side, precision=PRECISE),
    )
    to_prev = (
        jnp.einsum("bik,bkj->bij", behind, coupling, precision=PRECISE),
        jnp.einsum("bik,bk->bi", behind, right_side, precision=PRECISE),
    )
    return (to_next, to_prev)


def local(
    cam_diag, cam_lower, cam_rhs, obs_cam_jac, obs_point_jac, obs_residual, point_prior, knot_start
):
    blocks = cam_diag.shape[1]
    border = (ORDER - 1) * DOF
    local_count = cam_rhs.shape[0]
    band, schur_vec = band_terms(
        obs_cam_jac, obs_point_jac, obs_residual, point_prior, knot_start
    )
    band, schur_vec = summed_over(band, schur_vec, "lm")
    schur_mat = dense_from_band(band)
    arrived_mat, arrived_vec = passed_along(
        (schur_mat[local_count - 1, blocks:, :], schur_vec[local_count - 1, blocks:]), "tm", 1
    )
    spill_mat = jnp.concatenate([arrived_mat[None], schur_mat[:-1, blocks:, :]], 0)
    spill_vec = jnp.concatenate([arrived_vec[None], schur_vec[:-1, blocks:]], 0)
    diagonal = (
        cam_diag.reshape(local_count, blocks, blocks)
        + schur_mat[:, :blocks, :blocks]
        + jnp.pad(spill_mat[:, :, blocks:], ((0, 0), (0, blocks - border), (0, blocks - border)))
    )
    coupling = cam_lower.reshape(local_count, blocks, blocks) + jnp.pad(
        spill_mat[:, :, :blocks], ((0, 0), (0, blocks - border), (0, 0))
    )
    right_side = (
        cam_rhs - schur_vec[:, :blocks] - jnp.pad(spill_vec, ((0, 0), (0, blocks - border)))
    )
    after_coupling = passed_along(coupling[0], "tm", -1)
    level_one = jnp.stack([diagonal[1], diagonal[3]])
    lm_size = lax.axis_size("lm")
    if lm_size % 2 == 0:
        parity = lax.axis_index("lm") % 2
        mine = -negated_inverse(lax.dynamic_index_in_dim(level_one, parity, 0, keepdims=True))[0]
        other = lax.ppermute(mine, "lm", [(i, i ^ 1) for i in range(lm_size)])
        inverses = jnp.where(parity == 0, jnp.stack([mine, other]), jnp.stack([other, mine]))
    else:
        inverses = -negated_inverse(level_one)
    pair = eliminate(
        inverses,
        jnp.stack([coupling[1], coupling[3]]),
        jnp.stack([right_side[1], right_side[3]]),
        jnp.stack([coupling[2], after_coupling]),
    )
    next_first, prev_first = jax.tree.map(lambda x: x[0], pair)
    next_last, prev_last = jax.tree.map(lambda x: x[1], pair)
    mid_diag = diagonal[2] - next_first[0] - prev_last[0]
    mid_coupling = -next_first[1]
    mid_rhs = right_side[2] - next_first[2] - prev_last[1]
    arrived_last = passed_along((next_last[0], next_last[2]), "tm", 1)
    next_mid, prev_mid = jax.tree.map(
        lambda x: x[0],
        eliminate(
            -negated_inverse(mid_diag[None]), mid_coupling[None], mid_rhs[None], -next_last[1][None]
        ),
    )
    head_diag = diagonal[0] - prev_first[0] - prev_mid[0] - arrived_last[0]
    head_rhs = right_side[0] - prev_first[1] - prev_mid[1] - arrived_last[1]
    arrived = passed_along((next_mid[0], next_mid[1], next_mid[2]), "tm", 1)
    out_diag = head_diag - arrived[0]
    out_coupling = -arrived[1]
    out_rhs = head_rhs - arrived[2]
    return (out_diag, out_coupling, out_rhs[None, :])


def solution(mesh):
    placed = (
        P("tm", None),
        P("tm", None),
        P("tm", None),
        P(None, None, "tm", "lm"),
        P(None, None, "tm", "lm"),
        P(None, "tm", "lm"),
        P("tm", "lm"),
        P("tm", "lm"),
    )
    return jax.shard_map(
        local,
        mesh=mesh,
        in_specs=placed,
        out_specs=(P("tm", None), P("tm", None), P("tm", None)),
        check_vma=False,
    )
```

```python
import jax
import jax.numpy as jnp
from jax import lax
from jax.sharding import PartitionSpec as P
from jax.experimental import pallas as pl
from jax.experimental.pallas import tpu as pltpu

KNOTS = 64
DOF = 6
ORDER = 4


PRECISE = lax.Precision.HIGHEST


def passed_along(block, axis, distance):
    devices = range(lax.axis_size(axis))
    route = [((i - distance) % len(devices), i) for i in devices]
    return lax.ppermute(block, axis, route)


def passed_in_halves(arrays, distance):
    lm_size = lax.axis_size("lm")
    if lm_size % 2:
        return passed_along(arrays, "tm", distance)
    parity = lax.axis_index("lm") % 2

    def own_half(x):
        half = x.shape[0] // 2
        return lax.dynamic_slice_in_dim(x, parity * half, half, 0)

    got = passed_along(tuple(own_half(x) for x in arrays), "tm", distance)
    partner = lax.ppermute(got, "lm", [(i, i ^ 1) for i in range(lm_size)])
    return tuple(
        jnp.where(parity == 0, jnp.concatenate([g, p]), jnp.concatenate([p, g]))
        for g, p in zip(got, partner)
    )


def point_inverse(normal):
    adj_rows = []
    for row_at in range(3):
        entries = []
        for col_at in range(3):
            entries.append(
                normal[(col_at + 1) % 3, (row_at + 1) % 3]
                * normal[(col_at + 2) % 3, (row_at + 2) % 3]
                - normal[(col_at + 1) % 3, (row_at + 2) % 3]
                * normal[(col_at + 2) % 3, (row_at + 1) % 3]
            )
        adj_rows.append(jnp.stack(entries))
    adjugate = jnp.stack(adj_rows)
    determ = (
        normal[0, 0] * adjugate[0, 0]
        + normal[0, 1] * adjugate[1, 0]
        + normal[0, 2] * adjugate[2, 0]
    )
    return adjugate / determ


def landmark_project(cam_jac, point_jac, residual, prior):
    normal = jnp.einsum("rasl,rbsl->absl", point_jac, point_jac, precision=PRECISE)
    normal = normal + prior[None, None] * jnp.eye(3, dtype=jnp.float32)[:, :, None, None]
    inverse = point_inverse(normal)
    cross = jnp.einsum("rasl,rmsl->amsl", point_jac, cam_jac, precision=PRECISE)
    cross_res = jnp.einsum("rasl,rsl->asl", point_jac, residual, precision=PRECISE)
    solved = jnp.einsum("absl,bmsl->amsl", inverse, cross, precision=PRECISE)
    solved_res = jnp.einsum("absl,bsl->asl", inverse, cross_res, precision=PRECISE)
    projected = cam_jac - jnp.einsum("rasl,amsl->rmsl", point_jac, solved, precision=PRECISE)
    projected_res = residual - jnp.einsum("rasl,asl->rsl", point_jac, solved_res, precision=PRECISE)
    return (projected, projected_res)


def place_knots(values, window_start):
    rows_count = values.shape[0]
    seg_count = values.shape[2]
    group_size = values.shape[3]
    knot_span = KNOTS + ORDER - 1
    offsets = jnp.arange(knot_span, dtype=jnp.int32)[:, None, None] - window_start[None]
    onehot = (offsets[:, None] == jnp.arange(ORDER, dtype=jnp.int32)[None, :, None, None]).astype(
        jnp.float32
    )
    shaped = values.reshape(rows_count, ORDER, DOF, seg_count, group_size)
    placed = jnp.einsum("kosl,rodsl->kdrsl", onehot, shaped, precision=PRECISE)
    return placed.reshape(knot_span * DOF, rows_count, seg_count, group_size)


def batched_terms(cam_jac, point_jac, residual, prior, window_start):
    seg_count = window_start.shape[0]
    landmarks = window_start.shape[1]
    group_size = min(128, landmarks)
    extended = (KNOTS + ORDER - 1) * DOF

    def one_group(totals, group_index):
        projected, projected_res = landmark_project(cam_jac, point_jac, residual, prior)
        placed_cam = place_knots(cam_jac, window_start)
        placed_proj = place_knots(projected, window_start)
        new_mat = totals[0] + jnp.einsum(
            "ersl,frsl->sef", placed_cam, placed_proj, precision=PRECISE
        )
        new_vec = totals[1] + jnp.einsum(
            "ersl,rsl->se", placed_cam, projected_res, precision=PRECISE
        )
        return ((new_mat, new_vec), None)

    start_totals = (
        jnp.zeros((seg_count, extended, extended), jnp.float32),
        jnp.zeros((seg_count, extended), jnp.float32),
    )
    totals, _ = lax.scan(
        one_group, start_totals, jnp.arange(landmarks // group_size, dtype=jnp.int32)
    )
    return totals


def band_terms(cam_jac, point_jac, residual, prior, window_start):
    projected, projected_res = landmark_project(cam_jac, point_jac, residual, prior)
    pair = jnp.einsum("rmsl,rnsl->slmn", cam_jac, projected, precision=PRECISE)
    vec = jnp.einsum("rmsl,rsl->slm", cam_jac, projected_res, precision=PRECISE)
    seg_count, landmarks = pair.shape[:2]
    blocks = pair.reshape(seg_count, landmarks, ORDER, DOF, ORDER, DOF)
    zero = jnp.zeros((seg_count, landmarks, DOF, DOF), pair.dtype)
    width = 2 * ORDER - 1
    by_start = []
    for a in range(ORDER):
        per_offset = []
        for d in range(width):
            b = a + d - (ORDER - 1)
            per_offset.append(blocks[:, :, a, :, b, :] if 0 <= b < ORDER else zero)
        by_start.append(jnp.stack(per_offset, 2))
    spread = jnp.stack(by_start, 2)
    knot_span = KNOTS + ORDER - 1
    onehot = (
        jnp.arange(knot_span, dtype=jnp.int32)[None, :, None, None]
        == window_start[:, None, :, None] + jnp.arange(ORDER, dtype=jnp.int32)[None, None, None, :]
    ).astype(jnp.float32)
    band = jnp.einsum("sila,sladxy->sidxy", onehot, spread, precision=PRECISE)
    vec_blocks = vec.reshape(seg_count, landmarks, ORDER, DOF)
    dense_vec = jnp.einsum("sila,slax->six", onehot, vec_blocks, precision=PRECISE)
    return band, dense_vec.reshape(seg_count, knot_span * DOF)


def summed_over(band, vec, axis):
    size = lax.axis_size(axis)
    assert size & (size - 1) == 0
    seg_count = vec.shape[0]
    packed = jnp.concatenate([band.reshape(seg_count, -1), vec], 1)
    bit = 1
    while bit < size:
        packed = packed + lax.ppermute(packed, axis, [(i, i ^ bit) for i in range(size)])
        bit *= 2
    return packed[:, : band[0].size].reshape(band.shape), packed[:, band[0].size :]


def dense_from_band(band):
    seg_count, knot_span, width = band.shape[:3]
    extended = knot_span * DOF
    rows = jnp.transpose(band, (1, 0, 3, 2, 4)).reshape(knot_span, seg_count * DOF, width * DOF)
    within = jnp.arange(width * DOF, dtype=jnp.int32)
    column = jnp.arange(extended, dtype=jnp.int32)
    knot = jnp.arange(knot_span, dtype=jnp.int32)
    select = (
        column[None, None, :]
        == DOF * (knot[:, None, None] - (ORDER - 1)) + within[None, :, None]
    ).astype(jnp.float32)
    placed = jnp.einsum("iak,ikc->iac", rows, select, precision=PRECISE)
    placed = jnp.transpose(placed.reshape(knot_span, seg_count, DOF, extended), (1, 0, 2, 3))
    return placed.reshape(seg_count, extended, extended)


PIVOT = 128


def sweep_kernel(d_ref, o_ref, *pivot_refs):
    count, order, _ = d_ref.shape
    o_ref[...] = d_ref[...]
    lane_row = lax.broadcasted_iota(jnp.int32, (1, PIVOT), 1)
    for blk in range(order // PIVOT):
        lo = blk * PIVOT
        for b in range(count):
            pivot_refs[b][...] = o_ref[b, lo:lo + PIVOT, lo:lo + PIVOT]

        def lane_value(row, at):
            return jnp.sum(jnp.where(lane_row == at, row, 0.0), axis=1, keepdims=True)

        def pivot_step(row, ahead, k, ahead_at):
            inv = 1.0 / lane_value(row, k)
            scaled = row * inv
            link = lane_value(row, ahead_at)
            return jnp.where(lane_row == k, link * inv, ahead - link * scaled), scaled, inv

        def full_update(p_ref, row, scaled, inv, k):
            is_k = lane_row == k
            col = jnp.broadcast_to(
                jnp.transpose(jnp.broadcast_to(row, (8, PIVOT)))[:, 0:1], (PIVOT, PIVOT)
            )
            upd = p_ref[...] - col * scaled
            p_ref[...] = jnp.where(is_k, col * inv, upd)
            p_ref[pl.ds(k, 1), :] = jnp.where(is_k, -inv, scaled)

        def step(k, carried):
            ahead_at = jnp.minimum(k + 1, PIVOT - 1)
            out = []
            for p_ref, (row, prev_row, prev_scaled, prev_inv) in zip(pivot_refs, carried):
                ahead = p_ref[pl.ds(ahead_at, 1), :]
                link = lane_value(prev_row, ahead_at)
                ahead = jnp.where(
                    lane_row == k - 1, link * prev_inv, ahead - link * prev_scaled
                )
                next_row, scaled, inv = pivot_step(row, ahead, k, ahead_at)
                full_update(p_ref, prev_row, prev_scaled, prev_inv, k - 1)
                out.append((next_row, row, scaled, inv))
            return tuple(out)

        first = []
        for p_ref in pivot_refs:
            row = p_ref[pl.ds(0, 1), :]
            next_row, scaled, inv = pivot_step(row, p_ref[pl.ds(1, 1), :], 0, 1)
            first.append((next_row, row, scaled, inv))
        last = lax.fori_loop(1, PIVOT, step, tuple(first), unroll=2)
        for p_ref, (_, prev_row, prev_scaled, prev_inv) in zip(pivot_refs, last):
            full_update(p_ref, prev_row, prev_scaled, prev_inv, PIVOT - 1)
        for b in range(count):
            pneg = pivot_refs[b][...]
            col_blk = o_ref[b, :, lo:lo + PIVOT]
            row_blk = o_ref[b, lo:lo + PIVOT, :]
            t = jnp.dot(col_blk, pneg, precision=PRECISE, preferred_element_type=jnp.float32)
            o_ref[b] = o_ref[b] + jnp.dot(t, row_blk, precision=PRECISE, preferred_element_type=jnp.float32)
            o_ref[b, :, lo:lo + PIVOT] = -t
            o_ref[b, lo:lo + PIVOT, :] = -jnp.dot(pneg, row_blk, precision=PRECISE, preferred_element_type=jnp.float32)
            o_ref[b, lo:lo + PIVOT, lo:lo + PIVOT] = pneg


def negated_inverse(mats):
    count, order, _ = mats.shape
    return pl.pallas_call(
        sweep_kernel,
        out_shape=jax.ShapeDtypeStruct(mats.shape, mats.dtype),
        in_specs=[pl.BlockSpec(memory_space=pltpu.VMEM)],
        out_specs=pl.BlockSpec(memory_space=pltpu.VMEM),
        scratch_shapes=[pltpu.VMEM((PIVOT, PIVOT), jnp.float32)] * count,
    )(mats)


def eliminate(inverse, coupling, right_side, next_coupling):
    ahead = jnp.einsum("bij,bjk->bik", next_coupling, inverse, precision=PRECISE)
    behind = jnp.einsum("bji,bjk->bik", coupling, inverse, precision=PRECISE)
    to_next = (
        jnp.einsum("bik,bjk->bij", ahead, next_coupling, precision=PRECISE),
        jnp.einsum("bik,bkj->bij", ahead, coupling, precision=PRECISE),
        jnp.einsum("bik,bk->bi", ahead, right_side, precision=PRECISE),
    )
    to_prev = (
        jnp.einsum("bik,bkj->bij", behind, coupling, precision=PRECISE),
        jnp.einsum("bik,bk->bi", behind, right_side, precision=PRECISE),
    )
    return (to_next, to_prev)


def local(
    cam_diag, cam_lower, cam_rhs, obs_cam_jac, obs_point_jac, obs_residual, point_prior, knot_start
):
    blocks = cam_diag.shape[1]
    border = (ORDER - 1) * DOF
    local_count = cam_rhs.shape[0]
    band, schur_vec = band_terms(
        obs_cam_jac, obs_point_jac, obs_residual, point_prior, knot_start
    )
    band, schur_vec = summed_over(band, schur_vec, "lm")
    schur_mat = dense_from_band(band)
    arrived_mat, arrived_vec = passed_along(
        (schur_mat[local_count - 1, blocks:, :], schur_vec[local_count - 1, blocks:]), "tm", 1
    )
    spill_mat = jnp.concatenate([arrived_mat[None], schur_mat[:-1, blocks:, :]], 0)
    spill_vec = jnp.concatenate([arrived_vec[None], schur_vec[:-1, blocks:]], 0)
    diagonal = (
        cam_diag.reshape(local_count, blocks, blocks)
        + schur_mat[:, :blocks, :blocks]
        + jnp.pad(spill_mat[:, :, blocks:], ((0, 0), (0, blocks - border), (0, blocks - border)))
    )
    coupling = cam_lower.reshape(local_count, blocks, blocks) + jnp.pad(
        spill_mat[:, :, :blocks], ((0, 0), (0, blocks - border), (0, 0))
    )
    right_side = (
        cam_rhs - schur_vec[:, :blocks] - jnp.pad(spill_vec, ((0, 0), (0, blocks - border)))
    )
    after_coupling = passed_along(coupling[0], "tm", -1)
    level_one = jnp.stack([diagonal[1], diagonal[3]])
    lm_size = lax.axis_size("lm")
    if lm_size % 2 == 0:
        parity = lax.axis_index("lm") % 2
        mine = -negated_inverse(lax.dynamic_index_in_dim(level_one, parity, 0, keepdims=True))[0]
        other = lax.ppermute(mine, "lm", [(i, i ^ 1) for i in range(lm_size)])
        inverses = jnp.where(parity == 0, jnp.stack([mine, other]), jnp.stack([other, mine]))
    else:
        inverses = -negated_inverse(level_one)
    pair = eliminate(
        inverses,
        jnp.stack([coupling[1], coupling[3]]),
        jnp.stack([right_side[1], right_side[3]]),
        jnp.stack([coupling[2], after_coupling]),
    )
    next_first, prev_first = jax.tree.map(lambda x: x[0], pair)
    next_last, prev_last = jax.tree.map(lambda x: x[1], pair)
    mid_diag = diagonal[2] - next_first[0] - prev_last[0]
    mid_coupling = -next_first[1]
    mid_rhs = right_side[2] - next_first[2] - prev_last[1]
    arrived_last = passed_in_halves((next_last[0], next_last[2]), 1)
    next_mid, prev_mid = jax.tree.map(
        lambda x: x[0],
        eliminate(
            -negated_inverse(mid_diag[None]), mid_coupling[None], mid_rhs[None], -next_last[1][None]
        ),
    )
    head_diag = diagonal[0] - prev_first[0] - prev_mid[0] - arrived_last[0]
    head_rhs = right_side[0] - prev_first[1] - prev_mid[1] - arrived_last[1]
    arrived = passed_in_halves((next_mid[0], next_mid[1], next_mid[2]), 1)
    out_diag = head_diag - arrived[0]
    out_coupling = -arrived[1]
    out_rhs = head_rhs - arrived[2]
    return (out_diag, out_coupling, out_rhs[None, :])


def solution(mesh):
    placed = (
        P("tm", None),
        P("tm", None),
        P("tm", None),
        P(None, None, "tm", "lm"),
        P(None, None, "tm", "lm"),
        P(None, "tm", "lm"),
        P("tm", "lm"),
        P("tm", "lm"),
    )
    return jax.shard_map(
        local,
        mesh=mesh,
        in_specs=placed,
        out_specs=(P("tm", None), P("tm", None), P("tm", None)),
        check_vma=False,
    )
```

```python
import jax
import jax.numpy as jnp
from jax import lax
from jax.sharding import PartitionSpec as P
from jax.experimental import pallas as pl
from jax.experimental.pallas import tpu as pltpu

KNOTS = 64
DOF = 6
ORDER = 4


PRECISE = lax.Precision.HIGHEST
PRODUCT = lax.Precision.HIGH


def passed_along(block, axis, distance):
    devices = range(lax.axis_size(axis))
    route = [((i - distance) % len(devices), i) for i in devices]
    return lax.ppermute(block, axis, route)


def passed_in_halves(arrays, distance):
    lm_size = lax.axis_size("lm")
    if lm_size % 2:
        return passed_along(arrays, "tm", distance)
    parity = lax.axis_index("lm") % 2

    def own_half(x):
        half = x.shape[0] // 2
        return lax.dynamic_slice_in_dim(x, parity * half, half, 0)

    got = passed_along(tuple(own_half(x) for x in arrays), "tm", distance)
    partner = lax.ppermute(got, "lm", [(i, i ^ 1) for i in range(lm_size)])
    return tuple(
        jnp.where(parity == 0, jnp.concatenate([g, p]), jnp.concatenate([p, g]))
        for g, p in zip(got, partner)
    )


def point_inverse(normal):
    adj_rows = []
    for row_at in range(3):
        entries = []
        for col_at in range(3):
            entries.append(
                normal[(col_at + 1) % 3, (row_at + 1) % 3]
                * normal[(col_at + 2) % 3, (row_at + 2) % 3]
                - normal[(col_at + 1) % 3, (row_at + 2) % 3]
                * normal[(col_at + 2) % 3, (row_at + 1) % 3]
            )
        adj_rows.append(jnp.stack(entries))
    adjugate = jnp.stack(adj_rows)
    determ = (
        normal[0, 0] * adjugate[0, 0]
        + normal[0, 1] * adjugate[1, 0]
        + normal[0, 2] * adjugate[2, 0]
    )
    return adjugate / determ


def landmark_project(cam_jac, point_jac, residual, prior):
    normal = jnp.einsum("rasl,rbsl->absl", point_jac, point_jac, precision=PRECISE)
    normal = normal + prior[None, None] * jnp.eye(3, dtype=jnp.float32)[:, :, None, None]
    inverse = point_inverse(normal)
    cross = jnp.einsum("rasl,rmsl->amsl", point_jac, cam_jac, precision=PRECISE)
    cross_res = jnp.einsum("rasl,rsl->asl", point_jac, residual, precision=PRECISE)
    solved = jnp.einsum("absl,bmsl->amsl", inverse, cross, precision=PRECISE)
    solved_res = jnp.einsum("absl,bsl->asl", inverse, cross_res, precision=PRECISE)
    projected = cam_jac - jnp.einsum("rasl,amsl->rmsl", point_jac, solved, precision=PRECISE)
    projected_res = residual - jnp.einsum("rasl,asl->rsl", point_jac, solved_res, precision=PRECISE)
    return (projected, projected_res)


def place_knots(values, window_start):
    rows_count = values.shape[0]
    seg_count = values.shape[2]
    group_size = values.shape[3]
    knot_span = KNOTS + ORDER - 1
    offsets = jnp.arange(knot_span, dtype=jnp.int32)[:, None, None] - window_start[None]
    onehot = (offsets[:, None] == jnp.arange(ORDER, dtype=jnp.int32)[None, :, None, None]).astype(
        jnp.float32
    )
    shaped = values.reshape(rows_count, ORDER, DOF, seg_count, group_size)
    placed = jnp.einsum("kosl,rodsl->kdrsl", onehot, shaped, precision=PRECISE)
    return placed.reshape(knot_span * DOF, rows_count, seg_count, group_size)


def batched_terms(cam_jac, point_jac, residual, prior, window_start):
    seg_count = window_start.shape[0]
    landmarks = window_start.shape[1]
    group_size = min(128, landmarks)
    extended = (KNOTS + ORDER - 1) * DOF

    def one_group(totals, group_index):
        projected, projected_res = landmark_project(cam_jac, point_jac, residual, prior)
        placed_cam = place_knots(cam_jac, window_start)
        placed_proj = place_knots(projected, window_start)
        new_mat = totals[0] + jnp.einsum(
            "ersl,frsl->sef", placed_cam, placed_proj, precision=PRECISE
        )
        new_vec = totals[1] + jnp.einsum(
            "ersl,rsl->se", placed_cam, projected_res, precision=PRECISE
        )
        return ((new_mat, new_vec), None)

    start_totals = (
        jnp.zeros((seg_count, extended, extended), jnp.float32),
        jnp.zeros((seg_count, extended), jnp.float32),
    )
    totals, _ = lax.scan(
        one_group, start_totals, jnp.arange(landmarks // group_size, dtype=jnp.int32)
    )
    return totals


def band_terms(cam_jac, point_jac, residual, prior, window_start):
    projected, projected_res = landmark_project(cam_jac, point_jac, residual, prior)
    pair = jnp.einsum("rmsl,rnsl->slmn", cam_jac, projected, precision=PRECISE)
    vec = jnp.einsum("rmsl,rsl->slm", cam_jac, projected_res, precision=PRECISE)
    seg_count, landmarks = pair.shape[:2]
    blocks = pair.reshape(seg_count, landmarks, ORDER, DOF, ORDER, DOF)
    zero = jnp.zeros((seg_count, landmarks, DOF, DOF), pair.dtype)
    width = 2 * ORDER - 1
    by_start = []
    for a in range(ORDER):
        per_offset = []
        for d in range(width):
            b = a + d - (ORDER - 1)
            per_offset.append(blocks[:, :, a, :, b, :] if 0 <= b < ORDER else zero)
        by_start.append(jnp.stack(per_offset, 2))
    spread = jnp.stack(by_start, 2)
    knot_span = KNOTS + ORDER - 1
    onehot = (
        jnp.arange(knot_span, dtype=jnp.int32)[None, :, None, None]
        == window_start[:, None, :, None] + jnp.arange(ORDER, dtype=jnp.int32)[None, None, None, :]
    ).astype(jnp.float32)
    band = jnp.einsum("sila,sladxy->sidxy", onehot, spread, precision=PRECISE)
    vec_blocks = vec.reshape(seg_count, landmarks, ORDER, DOF)
    dense_vec = jnp.einsum("sila,slax->six", onehot, vec_blocks, precision=PRECISE)
    return band, dense_vec.reshape(seg_count, knot_span * DOF)


def summed_over(band, vec, axis):
    size = lax.axis_size(axis)
    assert size & (size - 1) == 0
    seg_count = vec.shape[0]
    packed = jnp.concatenate([band.reshape(seg_count, -1), vec], 1)
    bit = 1
    while bit < size:
        packed = packed + lax.ppermute(packed, axis, [(i, i ^ bit) for i in range(size)])
        bit *= 2
    return packed[:, : band[0].size].reshape(band.shape), packed[:, band[0].size :]


def dense_from_band(band):
    seg_count, knot_span, width = band.shape[:3]
    extended = knot_span * DOF
    rows = jnp.transpose(band, (1, 0, 3, 2, 4)).reshape(knot_span, seg_count * DOF, width * DOF)
    within = jnp.arange(width * DOF, dtype=jnp.int32)
    column = jnp.arange(extended, dtype=jnp.int32)
    knot = jnp.arange(knot_span, dtype=jnp.int32)
    select = (
        column[None, None, :]
        == DOF * (knot[:, None, None] - (ORDER - 1)) + within[None, :, None]
    ).astype(jnp.float32)
    placed = jnp.einsum("iak,ikc->iac", rows, select, precision=PRECISE)
    placed = jnp.transpose(placed.reshape(knot_span, seg_count, DOF, extended), (1, 0, 2, 3))
    return placed.reshape(seg_count, extended, extended)


PIVOT = 128


def sweep_kernel(d_ref, o_ref, *pivot_refs):
    count, order, _ = d_ref.shape
    o_ref[...] = d_ref[...]
    lane_row = lax.broadcasted_iota(jnp.int32, (1, PIVOT), 1)
    for blk in range(order // PIVOT):
        lo = blk * PIVOT
        for b in range(count):
            pivot_refs[b][...] = o_ref[b, lo:lo + PIVOT, lo:lo + PIVOT]

        def lane_value(row, at):
            return jnp.sum(jnp.where(lane_row == at, row, 0.0), axis=1, keepdims=True)

        def pivot_step(row, ahead, k, ahead_at):
            inv = 1.0 / lane_value(row, k)
            scaled = row * inv
            link = lane_value(row, ahead_at)
            return jnp.where(lane_row == k, link * inv, ahead - link * scaled), scaled, inv

        def full_update(p_ref, row, scaled, inv, k):
            is_k = lane_row == k
            col = jnp.broadcast_to(
                jnp.transpose(jnp.broadcast_to(row, (8, PIVOT)))[:, 0:1], (PIVOT, PIVOT)
            )
            upd = p_ref[...] - col * scaled
            p_ref[...] = jnp.where(is_k, col * inv, upd)
            p_ref[pl.ds(k, 1), :] = jnp.where(is_k, -inv, scaled)

        def step(k, carried):
            ahead_at = jnp.minimum(k + 1, PIVOT - 1)
            out = []
            for p_ref, (row, prev_row, prev_scaled, prev_inv) in zip(pivot_refs, carried):
                ahead = p_ref[pl.ds(ahead_at, 1), :]
                link = lane_value(prev_row, ahead_at)
                ahead = jnp.where(
                    lane_row == k - 1, link * prev_inv, ahead - link * prev_scaled
                )
                next_row, scaled, inv = pivot_step(row, ahead, k, ahead_at)
                full_update(p_ref, prev_row, prev_scaled, prev_inv, k - 1)
                out.append((next_row, row, scaled, inv))
            return tuple(out)

        first = []
        for p_ref in pivot_refs:
            row = p_ref[pl.ds(0, 1), :]
            next_row, scaled, inv = pivot_step(row, p_ref[pl.ds(1, 1), :], 0, 1)
            first.append((next_row, row, scaled, inv))
        last = lax.fori_loop(1, PIVOT, step, tuple(first), unroll=2)
        for p_ref, (_, prev_row, prev_scaled, prev_inv) in zip(pivot_refs, last):
            full_update(p_ref, prev_row, prev_scaled, prev_inv, PIVOT - 1)
        for b in range(count):
            pneg = pivot_refs[b][...]
            col_blk = o_ref[b, :, lo:lo + PIVOT]
            row_blk = o_ref[b, lo:lo + PIVOT, :]
            t = jnp.dot(col_blk, pneg, precision=PRECISE, preferred_element_type=jnp.float32)
            o_ref[b] = o_ref[b] + jnp.dot(t, row_blk, precision=PRECISE, preferred_element_type=jnp.float32)
            o_ref[b, :, lo:lo + PIVOT] = -t
            o_ref[b, lo:lo + PIVOT, :] = -jnp.dot(pneg, row_blk, precision=PRECISE, preferred_element_type=jnp.float32)
            o_ref[b, lo:lo + PIVOT, lo:lo + PIVOT] = pneg


def negated_inverse(mats):
    count, order, _ = mats.shape
    return pl.pallas_call(
        sweep_kernel,
        out_shape=jax.ShapeDtypeStruct(mats.shape, mats.dtype),
        in_specs=[pl.BlockSpec(memory_space=pltpu.VMEM)],
        out_specs=pl.BlockSpec(memory_space=pltpu.VMEM),
        scratch_shapes=[pltpu.VMEM((PIVOT, PIVOT), jnp.float32)] * count,
    )(mats)


def eliminate(inverse, coupling, right_side, next_coupling):
    ahead = jnp.einsum("bij,bjk->bik", next_coupling, inverse, precision=PRODUCT)
    behind = jnp.einsum("bji,bjk->bik", coupling, inverse, precision=PRODUCT)
    to_next = (
        jnp.einsum("bik,bjk->bij", ahead, next_coupling, precision=PRODUCT),
        jnp.einsum("bik,bkj->bij", ahead, coupling, precision=PRODUCT),
        jnp.einsum("bik,bk->bi", ahead, right_side, precision=PRODUCT),
    )
    to_prev = (
        jnp.einsum("bik,bkj->bij", behind, coupling, precision=PRODUCT),
        jnp.einsum("bik,bk->bi", behind, right_side, precision=PRODUCT),
    )
    return (to_next, to_prev)


def local(
    cam_diag, cam_lower, cam_rhs, obs_cam_jac, obs_point_jac, obs_residual, point_prior, knot_start
):
    blocks = cam_diag.shape[1]
    border = (ORDER - 1) * DOF
    local_count = cam_rhs.shape[0]
    band, schur_vec = band_terms(
        obs_cam_jac, obs_point_jac, obs_residual, point_prior, knot_start
    )
    band, schur_vec = summed_over(band, schur_vec, "lm")
    schur_mat = dense_from_band(band)
    arrived_mat, arrived_vec = passed_along(
        (schur_mat[local_count - 1, blocks:, :], schur_vec[local_count - 1, blocks:]), "tm", 1
    )
    spill_mat = jnp.concatenate([arrived_mat[None], schur_mat[:-1, blocks:, :]], 0)
    spill_vec = jnp.concatenate([arrived_vec[None], schur_vec[:-1, blocks:]], 0)
    diagonal = (
        cam_diag.reshape(local_count, blocks, blocks)
        + schur_mat[:, :blocks, :blocks]
        + jnp.pad(spill_mat[:, :, blocks:], ((0, 0), (0, blocks - border), (0, blocks - border)))
    )
    coupling = cam_lower.reshape(local_count, blocks, blocks) + jnp.pad(
        spill_mat[:, :, :blocks], ((0, 0), (0, blocks - border), (0, 0))
    )
    right_side = (
        cam_rhs - schur_vec[:, :blocks] - jnp.pad(spill_vec, ((0, 0), (0, blocks - border)))
    )
    after_coupling = passed_along(coupling[0], "tm", -1)
    level_one = jnp.stack([diagonal[1], diagonal[3]])
    lm_size = lax.axis_size("lm")
    if lm_size % 2 == 0:
        parity = lax.axis_index("lm") % 2
        mine = -negated_inverse(lax.dynamic_index_in_dim(level_one, parity, 0, keepdims=True))[0]
        other = lax.ppermute(mine, "lm", [(i, i ^ 1) for i in range(lm_size)])
        inverses = jnp.where(parity == 0, jnp.stack([mine, other]), jnp.stack([other, mine]))
    else:
        inverses = -negated_inverse(level_one)
    pair = eliminate(
        inverses,
        jnp.stack([coupling[1], coupling[3]]),
        jnp.stack([right_side[1], right_side[3]]),
        jnp.stack([coupling[2], after_coupling]),
    )
    next_first, prev_first = jax.tree.map(lambda x: x[0], pair)
    next_last, prev_last = jax.tree.map(lambda x: x[1], pair)
    mid_diag = diagonal[2] - next_first[0] - prev_last[0]
    mid_coupling = -next_first[1]
    mid_rhs = right_side[2] - next_first[2] - prev_last[1]
    arrived_last = passed_in_halves((next_last[0], next_last[2]), 1)
    next_mid, prev_mid = jax.tree.map(
        lambda x: x[0],
        eliminate(
            -negated_inverse(mid_diag[None]), mid_coupling[None], mid_rhs[None], -next_last[1][None]
        ),
    )
    head_diag = diagonal[0] - prev_first[0] - prev_mid[0] - arrived_last[0]
    head_rhs = right_side[0] - prev_first[1] - prev_mid[1] - arrived_last[1]
    arrived = passed_in_halves((next_mid[0], next_mid[1], next_mid[2]), 1)
    out_diag = head_diag - arrived[0]
    out_coupling = -arrived[1]
    out_rhs = head_rhs - arrived[2]
    return (out_diag, out_coupling, out_rhs[None, :])


def solution(mesh):
    placed = (
        P("tm", None),
        P("tm", None),
        P("tm", None),
        P(None, None, "tm", "lm"),
        P(None, None, "tm", "lm"),
        P(None, "tm", "lm"),
        P("tm", "lm"),
        P("tm", "lm"),
    )
    return jax.shard_map(
        local,
        mesh=mesh,
        in_specs=placed,
        out_specs=(P("tm", None), P("tm", None), P("tm", None)),
        check_vma=False,
    )
```

```python
import jax
import jax.numpy as jnp
from jax import lax
from jax.sharding import PartitionSpec as P
from jax.experimental import pallas as pl
from jax.experimental.pallas import tpu as pltpu

KNOTS = 64
DOF = 6
ORDER = 4


PRECISE = lax.Precision.HIGHEST


def passed_along(block, axis, distance):
    devices = range(lax.axis_size(axis))
    route = [((i - distance) % len(devices), i) for i in devices]
    return lax.ppermute(block, axis, route)


def passed_in_halves(arrays, distance):
    lm_size = lax.axis_size("lm")
    if lm_size % 2:
        return passed_along(arrays, "tm", distance)
    parity = lax.axis_index("lm") % 2

    def own_half(x):
        half = x.shape[0] // 2
        return lax.dynamic_slice_in_dim(x, parity * half, half, 0)

    got = passed_along(tuple(own_half(x) for x in arrays), "tm", distance)
    partner = lax.ppermute(got, "lm", [(i, i ^ 1) for i in range(lm_size)])
    return tuple(
        jnp.where(parity == 0, jnp.concatenate([g, p]), jnp.concatenate([p, g]))
        for g, p in zip(got, partner)
    )


def point_inverse(normal):
    adj_rows = []
    for row_at in range(3):
        entries = []
        for col_at in range(3):
            entries.append(
                normal[(col_at + 1) % 3, (row_at + 1) % 3]
                * normal[(col_at + 2) % 3, (row_at + 2) % 3]
                - normal[(col_at + 1) % 3, (row_at + 2) % 3]
                * normal[(col_at + 2) % 3, (row_at + 1) % 3]
            )
        adj_rows.append(jnp.stack(entries))
    adjugate = jnp.stack(adj_rows)
    determ = (
        normal[0, 0] * adjugate[0, 0]
        + normal[0, 1] * adjugate[1, 0]
        + normal[0, 2] * adjugate[2, 0]
    )
    return adjugate / determ


def landmark_project(cam_jac, point_jac, residual, prior):
    normal = jnp.einsum("rasl,rbsl->absl", point_jac, point_jac, precision=PRECISE)
    normal = normal + prior[None, None] * jnp.eye(3, dtype=jnp.float32)[:, :, None, None]
    inverse = point_inverse(normal)
    cross = jnp.einsum("rasl,rmsl->amsl", point_jac, cam_jac, precision=PRECISE)
    cross_res = jnp.einsum("rasl,rsl->asl", point_jac, residual, precision=PRECISE)
    solved = jnp.einsum("absl,bmsl->amsl", inverse, cross, precision=PRECISE)
    solved_res = jnp.einsum("absl,bsl->asl", inverse, cross_res, precision=PRECISE)
    projected = cam_jac - jnp.einsum("rasl,amsl->rmsl", point_jac, solved, precision=PRECISE)
    projected_res = residual - jnp.einsum("rasl,asl->rsl", point_jac, solved_res, precision=PRECISE)
    return (projected, projected_res)


def place_knots(values, window_start):
    rows_count = values.shape[0]
    seg_count = values.shape[2]
    group_size = values.shape[3]
    knot_span = KNOTS + ORDER - 1
    offsets = jnp.arange(knot_span, dtype=jnp.int32)[:, None, None] - window_start[None]
    onehot = (offsets[:, None] == jnp.arange(ORDER, dtype=jnp.int32)[None, :, None, None]).astype(
        jnp.float32
    )
    shaped = values.reshape(rows_count, ORDER, DOF, seg_count, group_size)
    placed = jnp.einsum("kosl,rodsl->kdrsl", onehot, shaped, precision=PRECISE)
    return placed.reshape(knot_span * DOF, rows_count, seg_count, group_size)


def batched_terms(cam_jac, point_jac, residual, prior, window_start):
    seg_count = window_start.shape[0]
    landmarks = window_start.shape[1]
    group_size = min(128, landmarks)
    extended = (KNOTS + ORDER - 1) * DOF

    def one_group(totals, group_index):
        projected, projected_res = landmark_project(cam_jac, point_jac, residual, prior)
        placed_cam = place_knots(cam_jac, window_start)
        placed_proj = place_knots(projected, window_start)
        new_mat = totals[0] + jnp.einsum(
            "ersl,frsl->sef", placed_cam, placed_proj, precision=PRECISE
        )
        new_vec = totals[1] + jnp.einsum(
            "ersl,rsl->se", placed_cam, projected_res, precision=PRECISE
        )
        return ((new_mat, new_vec), None)

    start_totals = (
        jnp.zeros((seg_count, extended, extended), jnp.float32),
        jnp.zeros((seg_count, extended), jnp.float32),
    )
    totals, _ = lax.scan(
        one_group, start_totals, jnp.arange(landmarks // group_size, dtype=jnp.int32)
    )
    return totals


def band_terms(cam_jac, point_jac, residual, prior, window_start):
    projected, projected_res = landmark_project(cam_jac, point_jac, residual, prior)
    pair = jnp.einsum("rmsl,rnsl->slmn", cam_jac, projected, precision=PRECISE)
    vec = jnp.einsum("rmsl,rsl->slm", cam_jac, projected_res, precision=PRECISE)
    seg_count, landmarks = pair.shape[:2]
    blocks = pair.reshape(seg_count, landmarks, ORDER, DOF, ORDER, DOF)
    zero = jnp.zeros((seg_count, landmarks, DOF, DOF), pair.dtype)
    width = 2 * ORDER - 1
    by_start = []
    for a in range(ORDER):
        per_offset = []
        for d in range(width):
            b = a + d - (ORDER - 1)
            per_offset.append(blocks[:, :, a, :, b, :] if 0 <= b < ORDER else zero)
        by_start.append(jnp.stack(per_offset, 2))
    spread = jnp.stack(by_start, 2)
    knot_span = KNOTS + ORDER - 1
    onehot = (
        jnp.arange(knot_span, dtype=jnp.int32)[None, :, None, None]
        == window_start[:, None, :, None] + jnp.arange(ORDER, dtype=jnp.int32)[None, None, None, :]
    ).astype(jnp.float32)
    band = jnp.einsum("sila,sladxy->isxdy", onehot, spread, precision=PRECISE)
    band = band.reshape(knot_span, seg_count * DOF, width * DOF)
    vec_blocks = vec.reshape(seg_count, landmarks, ORDER, DOF)
    dense_vec = jnp.einsum("sila,slax->isx", onehot, vec_blocks, precision=PRECISE)
    return jnp.concatenate([band, dense_vec.reshape(knot_span, seg_count * DOF, 1)], 2)


def summed_over(packed, axis):
    size = lax.axis_size(axis)
    assert size & (size - 1) == 0
    bit = 1
    while bit < size:
        packed = packed + lax.ppermute(packed, axis, [(i, i ^ bit) for i in range(size)])
        bit *= 2
    return packed


def dense_from_band(rows, seg_count):
    knot_span = rows.shape[0]
    width = rows.shape[2] // DOF
    extended = knot_span * DOF
    within = jnp.arange(width * DOF, dtype=jnp.int32)
    column = jnp.arange(extended, dtype=jnp.int32)
    knot = jnp.arange(knot_span, dtype=jnp.int32)
    select = (
        column[None, None, :]
        == DOF * (knot[:, None, None] - (ORDER - 1)) + within[None, :, None]
    ).astype(jnp.float32)
    placed = jnp.einsum("iak,ikc->iac", rows, select, precision=PRECISE)
    placed = jnp.transpose(placed.reshape(knot_span, seg_count, DOF, extended), (1, 0, 2, 3))
    return placed.reshape(seg_count, extended, extended)


PIVOT = 128


def sweep_kernel(d_ref, o_ref, *pivot_refs):
    count, order, _ = d_ref.shape
    o_ref[...] = d_ref[...]
    lane_row = lax.broadcasted_iota(jnp.int32, (1, PIVOT), 1)
    for blk in range(order // PIVOT):
        lo = blk * PIVOT
        for b in range(count):
            pivot_refs[b][...] = o_ref[b, lo:lo + PIVOT, lo:lo + PIVOT]

        def lane_value(row, at):
            return jnp.sum(jnp.where(lane_row == at, row, 0.0), axis=1, keepdims=True)

        def pivot_step(row, ahead, k, ahead_at):
            inv = 1.0 / lane_value(row, k)
            scaled = row * inv
            link = lane_value(row, ahead_at)
            return jnp.where(lane_row == k, link * inv, ahead - link * scaled), scaled, inv

        def full_update(p_ref, row, scaled, inv, k):
            is_k = lane_row == k
            col = jnp.broadcast_to(
                jnp.transpose(jnp.broadcast_to(row, (8, PIVOT)))[:, 0:1], (PIVOT, PIVOT)
            )
            upd = p_ref[...] - col * scaled
            p_ref[...] = jnp.where(is_k, col * inv, upd)
            p_ref[pl.ds(k, 1), :] = jnp.where(is_k, -inv, scaled)

        def step(k, carried):
            ahead_at = jnp.minimum(k + 1, PIVOT - 1)
            out = []
            for p_ref, (row, prev_row, prev_scaled, prev_inv) in zip(pivot_refs, carried):
                ahead = p_ref[pl.ds(ahead_at, 1), :]
                link = lane_value(prev_row, ahead_at)
                ahead = jnp.where(
                    lane_row == k - 1, link * prev_inv, ahead - link * prev_scaled
                )
                next_row, scaled, inv = pivot_step(row, ahead, k, ahead_at)
                full_update(p_ref, prev_row, prev_scaled, prev_inv, k - 1)
                out.append((next_row, row, scaled, inv))
            return tuple(out)

        first = []
        for p_ref in pivot_refs:
            row = p_ref[pl.ds(0, 1), :]
            next_row, scaled, inv = pivot_step(row, p_ref[pl.ds(1, 1), :], 0, 1)
            first.append((next_row, row, scaled, inv))
        last = lax.fori_loop(1, PIVOT, step, tuple(first), unroll=2)
        for p_ref, (_, prev_row, prev_scaled, prev_inv) in zip(pivot_refs, last):
            full_update(p_ref, prev_row, prev_scaled, prev_inv, PIVOT - 1)
        for b in range(count):
            pneg = pivot_refs[b][...]
            col_blk = o_ref[b, :, lo:lo + PIVOT]
            row_blk = o_ref[b, lo:lo + PIVOT, :]
            t = jnp.dot(col_blk, pneg, precision=PRECISE, preferred_element_type=jnp.float32)
            o_ref[b] = o_ref[b] + jnp.dot(t, row_blk, precision=PRECISE, preferred_element_type=jnp.float32)
            o_ref[b, :, lo:lo + PIVOT] = -t
            o_ref[b, lo:lo + PIVOT, :] = -jnp.dot(pneg, row_blk, precision=PRECISE, preferred_element_type=jnp.float32)
            o_ref[b, lo:lo + PIVOT, lo:lo + PIVOT] = pneg


def negated_inverse(mats):
    count, order, _ = mats.shape
    return pl.pallas_call(
        sweep_kernel,
        out_shape=jax.ShapeDtypeStruct(mats.shape, mats.dtype),
        in_specs=[pl.BlockSpec(memory_space=pltpu.VMEM)],
        out_specs=pl.BlockSpec(memory_space=pltpu.VMEM),
        scratch_shapes=[pltpu.VMEM((PIVOT, PIVOT), jnp.float32)] * count,
    )(mats)


def eliminate(inverse, coupling, right_side, next_coupling):
    ahead = jnp.einsum("bij,bjk->bik", next_coupling, inverse, precision=PRECISE)
    behind = jnp.einsum("bji,bjk->bik", coupling, inverse, precision=PRECISE)
    to_next = (
        jnp.einsum("bik,bjk->bij", ahead, next_coupling, precision=PRECISE),
        jnp.einsum("bik,bkj->bij", ahead, coupling, precision=PRECISE),
        jnp.einsum("bik,bk->bi", ahead, right_side, precision=PRECISE),
    )
    to_prev = (
        jnp.einsum("bik,bkj->bij", behind, coupling, precision=PRECISE),
        jnp.einsum("bik,bk->bi", behind, right_side, precision=PRECISE),
    )
    return (to_next, to_prev)


def local(
    cam_diag, cam_lower, cam_rhs, obs_cam_jac, obs_point_jac, obs_residual, point_prior, knot_start
):
    blocks = cam_diag.shape[1]
    border = (ORDER - 1) * DOF
    local_count = cam_rhs.shape[0]
    packed = summed_over(
        band_terms(obs_cam_jac, obs_point_jac, obs_residual, point_prior, knot_start), "lm"
    )
    schur_mat = dense_from_band(packed[:, :, :-1], local_count)
    schur_vec = jnp.transpose(
        packed[:, :, -1].reshape(packed.shape[0], local_count, DOF), (1, 0, 2)
    ).reshape(local_count, -1)
    arrived_mat, arrived_vec = passed_along(
        (schur_mat[local_count - 1, blocks:, :], schur_vec[local_count - 1, blocks:]), "tm", 1
    )
    spill_mat = jnp.concatenate([arrived_mat[None], schur_mat[:-1, blocks:, :]], 0)
    spill_vec = jnp.concatenate([arrived_vec[None], schur_vec[:-1, blocks:]], 0)
    diagonal = (
        cam_diag.reshape(local_count, blocks, blocks)
        + schur_mat[:, :blocks, :blocks]
        + jnp.pad(spill_mat[:, :, blocks:], ((0, 0), (0, blocks - border), (0, blocks - border)))
    )
    coupling = cam_lower.reshape(local_count, blocks, blocks) + jnp.pad(
        spill_mat[:, :, :blocks], ((0, 0), (0, blocks - border), (0, 0))
    )
    right_side = (
        cam_rhs - schur_vec[:, :blocks] - jnp.pad(spill_vec, ((0, 0), (0, blocks - border)))
    )
    after_coupling = passed_along(coupling[0], "tm", -1)
    level_one = jnp.stack([diagonal[1], diagonal[3]])
    lm_size = lax.axis_size("lm")
    if lm_size % 2 == 0:
        parity = lax.axis_index("lm") % 2
        mine = -negated_inverse(lax.dynamic_index_in_dim(level_one, parity, 0, keepdims=True))[0]
        other = lax.ppermute(mine, "lm", [(i, i ^ 1) for i in range(lm_size)])
        inverses = jnp.where(parity == 0, jnp.stack([mine, other]), jnp.stack([other, mine]))
    else:
        inverses = -negated_inverse(level_one)
    pair = eliminate(
        inverses,
        jnp.stack([coupling[1], coupling[3]]),
        jnp.stack([right_side[1], right_side[3]]),
        jnp.stack([coupling[2], after_coupling]),
    )
    next_first, prev_first = jax.tree.map(lambda x: x[0], pair)
    next_last, prev_last = jax.tree.map(lambda x: x[1], pair)
    mid_diag = diagonal[2] - next_first[0] - prev_last[0]
    mid_coupling = -next_first[1]
    mid_rhs = right_side[2] - next_first[2] - prev_last[1]
    arrived_last = passed_in_halves((next_last[0], next_last[2]), 1)
    next_mid, prev_mid = jax.tree.map(
        lambda x: x[0],
        eliminate(
            -negated_inverse(mid_diag[None]), mid_coupling[None], mid_rhs[None], -next_last[1][None]
        ),
    )
    head_diag = diagonal[0] - prev_first[0] - prev_mid[0] - arrived_last[0]
    head_rhs = right_side[0] - prev_first[1] - prev_mid[1] - arrived_last[1]
    arrived = passed_in_halves((next_mid[0], next_mid[1], next_mid[2]), 1)
    out_diag = head_diag - arrived[0]
    out_coupling = -arrived[1]
    out_rhs = head_rhs - arrived[2]
    return (out_diag, out_coupling, out_rhs[None, :])


def solution(mesh):
    placed = (
        P("tm", None),
        P("tm", None),
        P("tm", None),
        P(None, None, "tm", "lm"),
        P(None, None, "tm", "lm"),
        P(None, "tm", "lm"),
        P("tm", "lm"),
        P("tm", "lm"),
    )
    return jax.shard_map(
        local,
        mesh=mesh,
        in_specs=placed,
        out_specs=(P("tm", None), P("tm", None), P("tm", None)),
        check_vma=False,
    )
```

```python
import jax
import jax.numpy as jnp
from jax import lax
from jax.sharding import PartitionSpec as P
from jax.experimental import pallas as pl
from jax.experimental.pallas import tpu as pltpu

KNOTS = 64
DOF = 6
ORDER = 4


PRECISE = lax.Precision.HIGHEST


def passed_along(block, axis, distance):
    devices = range(lax.axis_size(axis))
    route = [((i - distance) % len(devices), i) for i in devices]
    return lax.ppermute(block, axis, route)


def passed_in_halves(arrays, distance):
    lm_size = lax.axis_size("lm")
    if lm_size % 2:
        return passed_along(arrays, "tm", distance)
    parity = lax.axis_index("lm") % 2

    def own_half(x):
        half = x.shape[0] // 2
        return lax.dynamic_slice_in_dim(x, parity * half, half, 0)

    got = passed_along(tuple(own_half(x) for x in arrays), "tm", distance)
    partner = lax.ppermute(got, "lm", [(i, i ^ 1) for i in range(lm_size)])
    return tuple(
        jnp.where(parity == 0, jnp.concatenate([g, p]), jnp.concatenate([p, g]))
        for g, p in zip(got, partner)
    )


def point_inverse(normal):
    adj_rows = []
    for row_at in range(3):
        entries = []
        for col_at in range(3):
            entries.append(
                normal[(col_at + 1) % 3, (row_at + 1) % 3]
                * normal[(col_at + 2) % 3, (row_at + 2) % 3]
                - normal[(col_at + 1) % 3, (row_at + 2) % 3]
                * normal[(col_at + 2) % 3, (row_at + 1) % 3]
            )
        adj_rows.append(jnp.stack(entries))
    adjugate = jnp.stack(adj_rows)
    determ = (
        normal[0, 0] * adjugate[0, 0]
        + normal[0, 1] * adjugate[1, 0]
        + normal[0, 2] * adjugate[2, 0]
    )
    return adjugate / determ


def landmark_project(cam_jac, point_jac, residual, prior):
    normal = jnp.einsum("rasl,rbsl->absl", point_jac, point_jac, precision=PRECISE)
    normal = normal + prior[None, None] * jnp.eye(3, dtype=jnp.float32)[:, :, None, None]
    inverse = point_inverse(normal)
    cross = jnp.einsum("rasl,rmsl->amsl", point_jac, cam_jac, precision=PRECISE)
    cross_res = jnp.einsum("rasl,rsl->asl", point_jac, residual, precision=PRECISE)
    solved = jnp.einsum("absl,bmsl->amsl", inverse, cross, precision=PRECISE)
    solved_res = jnp.einsum("absl,bsl->asl", inverse, cross_res, precision=PRECISE)
    projected = cam_jac - jnp.einsum("rasl,amsl->rmsl", point_jac, solved, precision=PRECISE)
    projected_res = residual - jnp.einsum("rasl,asl->rsl", point_jac, solved_res, precision=PRECISE)
    return (projected, projected_res)


def place_knots(values, window_start):
    rows_count = values.shape[0]
    seg_count = values.shape[2]
    group_size = values.shape[3]
    knot_span = KNOTS + ORDER - 1
    offsets = jnp.arange(knot_span, dtype=jnp.int32)[:, None, None] - window_start[None]
    onehot = (offsets[:, None] == jnp.arange(ORDER, dtype=jnp.int32)[None, :, None, None]).astype(
        jnp.float32
    )
    shaped = values.reshape(rows_count, ORDER, DOF, seg_count, group_size)
    placed = jnp.einsum("kosl,rodsl->kdrsl", onehot, shaped, precision=PRECISE)
    return placed.reshape(knot_span * DOF, rows_count, seg_count, group_size)


def batched_terms(cam_jac, point_jac, residual, prior, window_start):
    seg_count = window_start.shape[0]
    landmarks = window_start.shape[1]
    group_size = min(128, landmarks)
    extended = (KNOTS + ORDER - 1) * DOF

    def one_group(totals, group_index):
        projected, projected_res = landmark_project(cam_jac, point_jac, residual, prior)
        placed_cam = place_knots(cam_jac, window_start)
        placed_proj = place_knots(projected, window_start)
        new_mat = totals[0] + jnp.einsum(
            "ersl,frsl->sef", placed_cam, placed_proj, precision=PRECISE
        )
        new_vec = totals[1] + jnp.einsum(
            "ersl,rsl->se", placed_cam, projected_res, precision=PRECISE
        )
        return ((new_mat, new_vec), None)

    start_totals = (
        jnp.zeros((seg_count, extended, extended), jnp.float32),
        jnp.zeros((seg_count, extended), jnp.float32),
    )
    totals, _ = lax.scan(
        one_group, start_totals, jnp.arange(landmarks // group_size, dtype=jnp.int32)
    )
    return totals


def band_terms(cam_jac, point_jac, residual, prior, window_start):
    projected, projected_res = landmark_project(cam_jac, point_jac, residual, prior)
    pair = jnp.einsum("rmsl,rnsl->slmn", cam_jac, projected, precision=PRECISE)
    vec = jnp.einsum("rmsl,rsl->slm", cam_jac, projected_res, precision=PRECISE)
    seg_count, landmarks = pair.shape[:2]
    blocks = pair.reshape(seg_count, landmarks, ORDER, DOF, ORDER, DOF)
    zero = jnp.zeros((seg_count, landmarks, DOF, DOF), pair.dtype)
    width = 2 * ORDER - 1
    by_start = []
    for a in range(ORDER):
        per_offset = []
        for d in range(width):
            b = a + d - (ORDER - 1)
            per_offset.append(blocks[:, :, a, :, b, :] if 0 <= b < ORDER else zero)
        by_start.append(jnp.stack(per_offset, 2))
    spread = jnp.stack(by_start, 2)
    knot_span = KNOTS + ORDER - 1
    onehot = (
        jnp.arange(knot_span, dtype=jnp.int32)[None, :, None, None]
        == window_start[:, None, :, None] + jnp.arange(ORDER, dtype=jnp.int32)[None, None, None, :]
    ).astype(jnp.float32)
    band = jnp.einsum("sila,sladxy->isxdy", onehot, spread, precision=PRECISE)
    band = band.reshape(knot_span, seg_count * DOF, width * DOF)
    vec_blocks = vec.reshape(seg_count, landmarks, ORDER, DOF)
    dense_vec = jnp.einsum("sila,slax->isx", onehot, vec_blocks, precision=PRECISE)
    return jnp.concatenate([band, dense_vec.reshape(knot_span, seg_count * DOF, 1)], 2)


def summed_over(packed, axis):
    size = lax.axis_size(axis)
    assert size & (size - 1) == 0
    bit = 1
    while bit < size:
        packed = packed + lax.ppermute(packed, axis, [(i, i ^ bit) for i in range(size)])
        bit *= 2
    return packed


def dense_from_band(rows, seg_count):
    knot_span = rows.shape[0]
    width = rows.shape[2] // DOF
    extended = knot_span * DOF
    within = jnp.arange(width * DOF, dtype=jnp.int32)
    column = jnp.arange(extended, dtype=jnp.int32)
    knot = jnp.arange(knot_span, dtype=jnp.int32)
    select = (
        column[None, None, :]
        == DOF * (knot[:, None, None] - (ORDER - 1)) + within[None, :, None]
    ).astype(jnp.float32)
    placed = jnp.einsum("iak,ikc->iac", rows, select, precision=PRECISE)
    placed = jnp.transpose(placed.reshape(knot_span, seg_count, DOF, extended), (1, 0, 2, 3))
    return placed.reshape(seg_count, extended, extended)


PIVOT = 128


def sweep_kernel(d_ref, o_ref, *pivot_refs):
    count, order, _ = d_ref.shape
    o_ref[...] = d_ref[...]
    lane_row = lax.broadcasted_iota(jnp.int32, (1, PIVOT), 1)
    for blk in range(order // PIVOT):
        lo = blk * PIVOT
        for b in range(count):
            pivot_refs[b][...] = o_ref[b, lo:lo + PIVOT, lo:lo + PIVOT]

        def lane_value(row, at):
            return jnp.sum(jnp.where(lane_row == at, row, 0.0), axis=1, keepdims=True)

        def pivot_step(row, ahead, k, ahead_at):
            inv = 1.0 / lane_value(row, k)
            scaled = row * inv
            link = lane_value(row, ahead_at)
            return jnp.where(lane_row == k, link * inv, ahead - link * scaled), scaled, inv

        def full_update(p_ref, row, scaled, inv, k):
            is_k = lane_row == k
            col = jnp.broadcast_to(
                jnp.transpose(jnp.broadcast_to(row, (8, PIVOT)))[:, 0:1], (PIVOT, PIVOT)
            )
            upd = p_ref[...] - col * scaled
            p_ref[...] = jnp.where(is_k, col * inv, upd)
            p_ref[pl.ds(k, 1), :] = jnp.where(is_k, -inv, scaled)

        def step(k, carried):
            ahead_at = jnp.minimum(k + 1, PIVOT - 1)
            out = []
            for p_ref, (row, prev_row, prev_scaled, prev_inv) in zip(pivot_refs, carried):
                ahead = p_ref[pl.ds(ahead_at, 1), :]
                link = lane_value(prev_row, ahead_at)
                ahead = jnp.where(
                    lane_row == k - 1, link * prev_inv, ahead - link * prev_scaled
                )
                next_row, scaled, inv = pivot_step(row, ahead, k, ahead_at)
                full_update(p_ref, prev_row, prev_scaled, prev_inv, k - 1)
                out.append((next_row, row, scaled, inv))
            return tuple(out)

        first = []
        for p_ref in pivot_refs:
            row = p_ref[pl.ds(0, 1), :]
            next_row, scaled, inv = pivot_step(row, p_ref[pl.ds(1, 1), :], 0, 1)
            first.append((next_row, row, scaled, inv))
        last = lax.fori_loop(1, PIVOT, step, tuple(first), unroll=4)
        for p_ref, (_, prev_row, prev_scaled, prev_inv) in zip(pivot_refs, last):
            full_update(p_ref, prev_row, prev_scaled, prev_inv, PIVOT - 1)
        for b in range(count):
            pneg = pivot_refs[b][...]
            col_blk = o_ref[b, :, lo:lo + PIVOT]
            row_blk = o_ref[b, lo:lo + PIVOT, :]
            t = jnp.dot(col_blk, pneg, precision=PRECISE, preferred_element_type=jnp.float32)
            o_ref[b] = o_ref[b] + jnp.dot(t, row_blk, precision=PRECISE, preferred_element_type=jnp.float32)
            o_ref[b, :, lo:lo + PIVOT] = -t
            o_ref[b, lo:lo + PIVOT, :] = -jnp.dot(pneg, row_blk, precision=PRECISE, preferred_element_type=jnp.float32)
            o_ref[b, lo:lo + PIVOT, lo:lo + PIVOT] = pneg


def negated_inverse(mats):
    count, order, _ = mats.shape
    return pl.pallas_call(
        sweep_kernel,
        out_shape=jax.ShapeDtypeStruct(mats.shape, mats.dtype),
        in_specs=[pl.BlockSpec(memory_space=pltpu.VMEM)],
        out_specs=pl.BlockSpec(memory_space=pltpu.VMEM),
        scratch_shapes=[pltpu.VMEM((PIVOT, PIVOT), jnp.float32)] * count,
    )(mats)


def eliminate(inverse, coupling, right_side, next_coupling):
    ahead = jnp.einsum("bij,bjk->bik", next_coupling, inverse, precision=PRECISE)
    behind = jnp.einsum("bji,bjk->bik", coupling, inverse, precision=PRECISE)
    to_next = (
        jnp.einsum("bik,bjk->bij", ahead, next_coupling, precision=PRECISE),
        jnp.einsum("bik,bkj->bij", ahead, coupling, precision=PRECISE),
        jnp.einsum("bik,bk->bi", ahead, right_side, precision=PRECISE),
    )
    to_prev = (
        jnp.einsum("bik,bkj->bij", behind, coupling, precision=PRECISE),
        jnp.einsum("bik,bk->bi", behind, right_side, precision=PRECISE),
    )
    return (to_next, to_prev)


def local(
    cam_diag, cam_lower, cam_rhs, obs_cam_jac, obs_point_jac, obs_residual, point_prior, knot_start
):
    blocks = cam_diag.shape[1]
    border = (ORDER - 1) * DOF
    local_count = cam_rhs.shape[0]
    packed = summed_over(
        band_terms(obs_cam_jac, obs_point_jac, obs_residual, point_prior, knot_start), "lm"
    )
    schur_mat = dense_from_band(packed[:, :, :-1], local_count)
    schur_vec = jnp.transpose(
        packed[:, :, -1].reshape(packed.shape[0], local_count, DOF), (1, 0, 2)
    ).reshape(local_count, -1)
    arrived_mat, arrived_vec = passed_along(
        (schur_mat[local_count - 1, blocks:, :], schur_vec[local_count - 1, blocks:]), "tm", 1
    )
    spill_mat = jnp.concatenate([arrived_mat[None], schur_mat[:-1, blocks:, :]], 0)
    spill_vec = jnp.concatenate([arrived_vec[None], schur_vec[:-1, blocks:]], 0)
    diagonal = (
        cam_diag.reshape(local_count, blocks, blocks)
        + schur_mat[:, :blocks, :blocks]
        + jnp.pad(spill_mat[:, :, blocks:], ((0, 0), (0, blocks - border), (0, blocks - border)))
    )
    coupling = cam_lower.reshape(local_count, blocks, blocks) + jnp.pad(
        spill_mat[:, :, :blocks], ((0, 0), (0, blocks - border), (0, 0))
    )
    right_side = (
        cam_rhs - schur_vec[:, :blocks] - jnp.pad(spill_vec, ((0, 0), (0, blocks - border)))
    )
    after_coupling = passed_along(coupling[0], "tm", -1)
    level_one = jnp.stack([diagonal[1], diagonal[3]])
    lm_size = lax.axis_size("lm")
    if lm_size % 2 == 0:
        parity = lax.axis_index("lm") % 2
        mine = -negated_inverse(lax.dynamic_index_in_dim(level_one, parity, 0, keepdims=True))[0]
        other = lax.ppermute(mine, "lm", [(i, i ^ 1) for i in range(lm_size)])
        inverses = jnp.where(parity == 0, jnp.stack([mine, other]), jnp.stack([other, mine]))
    else:
        inverses = -negated_inverse(level_one)
    pair = eliminate(
        inverses,
        jnp.stack([coupling[1], coupling[3]]),
        jnp.stack([right_side[1], right_side[3]]),
        jnp.stack([coupling[2], after_coupling]),
    )
    next_first, prev_first = jax.tree.map(lambda x: x[0], pair)
    next_last, prev_last = jax.tree.map(lambda x: x[1], pair)
    mid_diag = diagonal[2] - next_first[0] - prev_last[0]
    mid_coupling = -next_first[1]
    mid_rhs = right_side[2] - next_first[2] - prev_last[1]
    arrived_last = passed_in_halves((next_last[0], next_last[2]), 1)
    next_mid, prev_mid = jax.tree.map(
        lambda x: x[0],
        eliminate(
            -negated_inverse(mid_diag[None]), mid_coupling[None], mid_rhs[None], -next_last[1][None]
        ),
    )
    head_diag = diagonal[0] - prev_first[0] - prev_mid[0] - arrived_last[0]
    head_rhs = right_side[0] - prev_first[1] - prev_mid[1] - arrived_last[1]
    arrived = passed_in_halves((next_mid[0], next_mid[1], next_mid[2]), 1)
    out_diag = head_diag - arrived[0]
    out_coupling = -arrived[1]
    out_rhs = head_rhs - arrived[2]
    return (out_diag, out_coupling, out_rhs[None, :])


def solution(mesh):
    placed = (
        P("tm", None),
        P("tm", None),
        P("tm", None),
        P(None, None, "tm", "lm"),
        P(None, None, "tm", "lm"),
        P(None, "tm", "lm"),
        P("tm", "lm"),
        P("tm", "lm"),
    )
    return jax.shard_map(
        local,
        mesh=mesh,
        in_specs=placed,
        out_specs=(P("tm", None), P("tm", None), P("tm", None)),
        check_vma=False,
    )
```

```python
import jax
import jax.numpy as jnp
from jax import lax
from jax.sharding import PartitionSpec as P
from jax.experimental import pallas as pl
from jax.experimental.pallas import tpu as pltpu

KNOTS = 64
DOF = 6
ORDER = 4


PRECISE = lax.Precision.HIGHEST


def passed_along(block, axis, distance):
    devices = range(lax.axis_size(axis))
    route = [((i - distance) % len(devices), i) for i in devices]
    return lax.ppermute(block, axis, route)


def passed_in_halves(arrays, distance):
    lm_size = lax.axis_size("lm")
    if lm_size % 2:
        return passed_along(arrays, "tm", distance)
    parity = lax.axis_index("lm") % 2

    def own_half(x):
        half = x.shape[0] // 2
        return lax.dynamic_slice_in_dim(x, parity * half, half, 0)

    got = passed_along(tuple(own_half(x) for x in arrays), "tm", distance)
    partner = lax.ppermute(got, "lm", [(i, i ^ 1) for i in range(lm_size)])
    return tuple(
        jnp.where(parity == 0, jnp.concatenate([g, p]), jnp.concatenate([p, g]))
        for g, p in zip(got, partner)
    )


def point_inverse(normal):
    adj_rows = []
    for row_at in range(3):
        entries = []
        for col_at in range(3):
            entries.append(
                normal[(col_at + 1) % 3, (row_at + 1) % 3]
                * normal[(col_at + 2) % 3, (row_at + 2) % 3]
                - normal[(col_at + 1) % 3, (row_at + 2) % 3]
                * normal[(col_at + 2) % 3, (row_at + 1) % 3]
            )
        adj_rows.append(jnp.stack(entries))
    adjugate = jnp.stack(adj_rows)
    determ = (
        normal[0, 0] * adjugate[0, 0]
        + normal[0, 1] * adjugate[1, 0]
        + normal[0, 2] * adjugate[2, 0]
    )
    return adjugate / determ


def landmark_project(cam_jac, point_jac, residual, prior):
    normal = jnp.einsum("rasl,rbsl->absl", point_jac, point_jac, precision=PRECISE)
    normal = normal + prior[None, None] * jnp.eye(3, dtype=jnp.float32)[:, :, None, None]
    inverse = point_inverse(normal)
    cross = jnp.einsum("rasl,rmsl->amsl", point_jac, cam_jac, precision=PRECISE)
    cross_res = jnp.einsum("rasl,rsl->asl", point_jac, residual, precision=PRECISE)
    solved = jnp.einsum("absl,bmsl->amsl", inverse, cross, precision=PRECISE)
    solved_res = jnp.einsum("absl,bsl->asl", inverse, cross_res, precision=PRECISE)
    projected = cam_jac - jnp.einsum("rasl,amsl->rmsl", point_jac, solved, precision=PRECISE)
    projected_res = residual - jnp.einsum("rasl,asl->rsl", point_jac, solved_res, precision=PRECISE)
    return (projected, projected_res)


def place_knots(values, window_start):
    rows_count = values.shape[0]
    seg_count = values.shape[2]
    group_size = values.shape[3]
    knot_span = KNOTS + ORDER - 1
    offsets = jnp.arange(knot_span, dtype=jnp.int32)[:, None, None] - window_start[None]
    onehot = (offsets[:, None] == jnp.arange(ORDER, dtype=jnp.int32)[None, :, None, None]).astype(
        jnp.float32
    )
    shaped = values.reshape(rows_count, ORDER, DOF, seg_count, group_size)
    placed = jnp.einsum("kosl,rodsl->kdrsl", onehot, shaped, precision=PRECISE)
    return placed.reshape(knot_span * DOF, rows_count, seg_count, group_size)


def batched_terms(cam_jac, point_jac, residual, prior, window_start):
    seg_count = window_start.shape[0]
    landmarks = window_start.shape[1]
    group_size = min(128, landmarks)
    extended = (KNOTS + ORDER - 1) * DOF

    def one_group(totals, group_index):
        projected, projected_res = landmark_project(cam_jac, point_jac, residual, prior)
        placed_cam = place_knots(cam_jac, window_start)
        placed_proj = place_knots(projected, window_start)
        new_mat = totals[0] + jnp.einsum(
            "ersl,frsl->sef", placed_cam, placed_proj, precision=PRECISE
        )
        new_vec = totals[1] + jnp.einsum(
            "ersl,rsl->se", placed_cam, projected_res, precision=PRECISE
        )
        return ((new_mat, new_vec), None)

    start_totals = (
        jnp.zeros((seg_count, extended, extended), jnp.float32),
        jnp.zeros((seg_count, extended), jnp.float32),
    )
    totals, _ = lax.scan(
        one_group, start_totals, jnp.arange(landmarks // group_size, dtype=jnp.int32)
    )
    return totals


def band_terms(cam_jac, point_jac, residual, prior, window_start):
    projected, projected_res = landmark_project(cam_jac, point_jac, residual, prior)
    pair = jnp.einsum("rmsl,rnsl->slmn", cam_jac, projected, precision=PRECISE)
    vec = jnp.einsum("rmsl,rsl->slm", cam_jac, projected_res, precision=PRECISE)
    seg_count, landmarks = pair.shape[:2]
    blocks = pair.reshape(seg_count, landmarks, ORDER, DOF, ORDER, DOF)
    zero = jnp.zeros((seg_count, landmarks, DOF, DOF), pair.dtype)
    width = 2 * ORDER - 1
    by_start = []
    for a in range(ORDER):
        per_offset = []
        for d in range(width):
            b = a + d - (ORDER - 1)
            per_offset.append(blocks[:, :, a, :, b, :] if 0 <= b < ORDER else zero)
        by_start.append(jnp.stack(per_offset, 2))
    spread = jnp.stack(by_start, 2)
    knot_span = KNOTS + ORDER - 1
    onehot = (
        jnp.arange(knot_span, dtype=jnp.int32)[None, :, None, None]
        == window_start[:, None, :, None] + jnp.arange(ORDER, dtype=jnp.int32)[None, None, None, :]
    ).astype(jnp.float32)
    band = jnp.einsum("sila,sladxy->isxdy", onehot, spread, precision=PRECISE)
    band = band.reshape(knot_span, seg_count * DOF * width * DOF)
    vec_blocks = vec.reshape(seg_count, landmarks, ORDER, DOF)
    dense_vec = jnp.einsum("sila,slax->isx", onehot, vec_blocks, precision=PRECISE)
    return jnp.concatenate([band, dense_vec.reshape(knot_span, seg_count * DOF)], 1)


def summed_over(packed, axis):
    size = lax.axis_size(axis)
    assert size & (size - 1) == 0
    bit = 1
    while bit < size:
        packed = packed + lax.ppermute(packed, axis, [(i, i ^ bit) for i in range(size)])
        bit *= 2
    return packed


def dense_from_band(rows, seg_count):
    knot_span = rows.shape[0]
    width = rows.shape[2] // DOF
    extended = knot_span * DOF
    within = jnp.arange(width * DOF, dtype=jnp.int32)
    column = jnp.arange(extended, dtype=jnp.int32)
    knot = jnp.arange(knot_span, dtype=jnp.int32)
    select = (
        column[None, None, :]
        == DOF * (knot[:, None, None] - (ORDER - 1)) + within[None, :, None]
    ).astype(jnp.float32)
    placed = jnp.einsum("iak,ikc->iac", rows, select, precision=PRECISE)
    placed = jnp.transpose(placed.reshape(knot_span, seg_count, DOF, extended), (1, 0, 2, 3))
    return placed.reshape(seg_count, extended, extended)


PIVOT = 128


def sweep_kernel(d_ref, o_ref, *pivot_refs):
    count, order, _ = d_ref.shape
    o_ref[...] = d_ref[...]
    lane_row = lax.broadcasted_iota(jnp.int32, (1, PIVOT), 1)
    for blk in range(order // PIVOT):
        lo = blk * PIVOT
        for b in range(count):
            pivot_refs[b][...] = o_ref[b, lo:lo + PIVOT, lo:lo + PIVOT]

        def lane_value(row, at):
            return jnp.sum(jnp.where(lane_row == at, row, 0.0), axis=1, keepdims=True)

        def pivot_step(row, ahead, k, ahead_at):
            inv = 1.0 / lane_value(row, k)
            scaled = row * inv
            link = lane_value(row, ahead_at)
            return jnp.where(lane_row == k, link * inv, ahead - link * scaled), scaled, inv

        def full_update(p_ref, row, scaled, inv, k):
            is_k = lane_row == k
            col = jnp.broadcast_to(
                jnp.transpose(jnp.broadcast_to(row, (8, PIVOT)))[:, 0:1], (PIVOT, PIVOT)
            )
            upd = p_ref[...] - col * scaled
            p_ref[...] = jnp.where(is_k, col * inv, upd)
            p_ref[pl.ds(k, 1), :] = jnp.where(is_k, -inv, scaled)

        def step(k, carried):
            ahead_at = jnp.minimum(k + 1, PIVOT - 1)
            out = []
            for p_ref, (row, prev_row, prev_scaled, prev_inv) in zip(pivot_refs, carried):
                ahead = p_ref[pl.ds(ahead_at, 1), :]
                link = lane_value(prev_row, ahead_at)
                ahead = jnp.where(
                    lane_row == k - 1, link * prev_inv, ahead - link * prev_scaled
                )
                next_row, scaled, inv = pivot_step(row, ahead, k, ahead_at)
                full_update(p_ref, prev_row, prev_scaled, prev_inv, k - 1)
                out.append((next_row, row, scaled, inv))
            return tuple(out)

        first = []
        for p_ref in pivot_refs:
            row = p_ref[pl.ds(0, 1), :]
            next_row, scaled, inv = pivot_step(row, p_ref[pl.ds(1, 1), :], 0, 1)
            first.append((next_row, row, scaled, inv))
        last = lax.fori_loop(1, PIVOT, step, tuple(first), unroll=2)
        for p_ref, (_, prev_row, prev_scaled, prev_inv) in zip(pivot_refs, last):
            full_update(p_ref, prev_row, prev_scaled, prev_inv, PIVOT - 1)
        for b in range(count):
            pneg = pivot_refs[b][...]
            col_blk = o_ref[b, :, lo:lo + PIVOT]
            row_blk = o_ref[b, lo:lo + PIVOT, :]
            t = jnp.dot(col_blk, pneg, precision=PRECISE, preferred_element_type=jnp.float32)
            o_ref[b] = o_ref[b] + jnp.dot(t, row_blk, precision=PRECISE, preferred_element_type=jnp.float32)
            o_ref[b, :, lo:lo + PIVOT] = -t
            o_ref[b, lo:lo + PIVOT, :] = -jnp.dot(pneg, row_blk, precision=PRECISE, preferred_element_type=jnp.float32)
            o_ref[b, lo:lo + PIVOT, lo:lo + PIVOT] = pneg


def negated_inverse(mats):
    count, order, _ = mats.shape
    return pl.pallas_call(
        sweep_kernel,
        out_shape=jax.ShapeDtypeStruct(mats.shape, mats.dtype),
        in_specs=[pl.BlockSpec(memory_space=pltpu.VMEM)],
        out_specs=pl.BlockSpec(memory_space=pltpu.VMEM),
        scratch_shapes=[pltpu.VMEM((PIVOT, PIVOT), jnp.float32)] * count,
    )(mats)


def eliminate(inverse, coupling, right_side, next_coupling):
    ahead = jnp.einsum("bij,bjk->bik", next_coupling, inverse, precision=PRECISE)
    behind = jnp.einsum("bji,bjk->bik", coupling, inverse, precision=PRECISE)
    to_next = (
        jnp.einsum("bik,bjk->bij", ahead, next_coupling, precision=PRECISE),
        jnp.einsum("bik,bkj->bij", ahead, coupling, precision=PRECISE),
        jnp.einsum("bik,bk->bi", ahead, right_side, precision=PRECISE),
    )
    to_prev = (
        jnp.einsum("bik,bkj->bij", behind, coupling, precision=PRECISE),
        jnp.einsum("bik,bk->bi", behind, right_side, precision=PRECISE),
    )
    return (to_next, to_prev)


def local(
    cam_diag, cam_lower, cam_rhs, obs_cam_jac, obs_point_jac, obs_residual, point_prior, knot_start
):
    blocks = cam_diag.shape[1]
    border = (ORDER - 1) * DOF
    local_count = cam_rhs.shape[0]
    packed = summed_over(
        band_terms(obs_cam_jac, obs_point_jac, obs_residual, point_prior, knot_start), "lm"
    )
    knot_span = packed.shape[0]
    rows = local_count * DOF
    schur_mat = dense_from_band(
        packed[:, : rows * (2 * ORDER - 1) * DOF].reshape(knot_span, rows, -1), local_count
    )
    schur_vec = jnp.transpose(
        packed[:, rows * (2 * ORDER - 1) * DOF :].reshape(knot_span, local_count, DOF), (1, 0, 2)
    ).reshape(local_count, -1)
    arrived_mat, arrived_vec = passed_along(
        (schur_mat[local_count - 1, blocks:, :], schur_vec[local_count - 1, blocks:]), "tm", 1
    )
    spill_mat = jnp.concatenate([arrived_mat[None], schur_mat[:-1, blocks:, :]], 0)
    spill_vec = jnp.concatenate([arrived_vec[None], schur_vec[:-1, blocks:]], 0)
    diagonal = (
        cam_diag.reshape(local_count, blocks, blocks)
        + schur_mat[:, :blocks, :blocks]
        + jnp.pad(spill_mat[:, :, blocks:], ((0, 0), (0, blocks - border), (0, blocks - border)))
    )
    coupling = cam_lower.reshape(local_count, blocks, blocks) + jnp.pad(
        spill_mat[:, :, :blocks], ((0, 0), (0, blocks - border), (0, 0))
    )
    right_side = (
        cam_rhs - schur_vec[:, :blocks] - jnp.pad(spill_vec, ((0, 0), (0, blocks - border)))
    )
    after_coupling = passed_along(coupling[0], "tm", -1)
    level_one = jnp.stack([diagonal[1], diagonal[3]])
    lm_size = lax.axis_size("lm")
    if lm_size % 2 == 0:
        parity = lax.axis_index("lm") % 2
        mine = -negated_inverse(lax.dynamic_index_in_dim(level_one, parity, 0, keepdims=True))[0]
        other = lax.ppermute(mine, "lm", [(i, i ^ 1) for i in range(lm_size)])
        inverses = jnp.where(parity == 0, jnp.stack([mine, other]), jnp.stack([other, mine]))
    else:
        inverses = -negated_inverse(level_one)
    pair = eliminate(
        inverses,
        jnp.stack([coupling[1], coupling[3]]),
        jnp.stack([right_side[1], right_side[3]]),
        jnp.stack([coupling[2], after_coupling]),
    )
    next_first, prev_first = jax.tree.map(lambda x: x[0], pair)
    next_last, prev_last = jax.tree.map(lambda x: x[1], pair)
    mid_diag = diagonal[2] - next_first[0] - prev_last[0]
    mid_coupling = -next_first[1]
    mid_rhs = right_side[2] - next_first[2] - prev_last[1]
    arrived_last = passed_in_halves((next_last[0], next_last[2]), 1)
    next_mid, prev_mid = jax.tree.map(
        lambda x: x[0],
        eliminate(
            -negated_inverse(mid_diag[None]), mid_coupling[None], mid_rhs[None], -next_last[1][None]
        ),
    )
    head_diag = diagonal[0] - prev_first[0] - prev_mid[0] - arrived_last[0]
    head_rhs = right_side[0] - prev_first[1] - prev_mid[1] - arrived_last[1]
    arrived = passed_in_halves((next_mid[0], next_mid[1], next_mid[2]), 1)
    out_diag = head_diag - arrived[0]
    out_coupling = -arrived[1]
    out_rhs = head_rhs - arrived[2]
    return (out_diag, out_coupling, out_rhs[None, :])


def solution(mesh):
    placed = (
        P("tm", None),
        P("tm", None),
        P("tm", None),
        P(None, None, "tm", "lm"),
        P(None, None, "tm", "lm"),
        P(None, "tm", "lm"),
        P("tm", "lm"),
        P("tm", "lm"),
    )
    return jax.shard_map(
        local,
        mesh=mesh,
        in_specs=placed,
        out_specs=(P("tm", None), P("tm", None), P("tm", None)),
        check_vma=False,
    )
```

```python
import jax
import jax.numpy as jnp
from jax import lax
from jax.sharding import PartitionSpec as P
from jax.experimental import pallas as pl
from jax.experimental.pallas import tpu as pltpu

KNOTS = 64
DOF = 6
ORDER = 4


PRECISE = lax.Precision.HIGHEST


def passed_along(block, axis, distance):
    devices = range(lax.axis_size(axis))
    route = [((i - distance) % len(devices), i) for i in devices]
    return lax.ppermute(block, axis, route)


def passed_in_halves(arrays, distance):
    lm_size = lax.axis_size("lm")
    if lm_size % 2:
        return passed_along(arrays, "tm", distance)
    parity = lax.axis_index("lm") % 2

    def own_half(x):
        half = x.shape[0] // 2
        return lax.dynamic_slice_in_dim(x, parity * half, half, 0)

    got = passed_along(tuple(own_half(x) for x in arrays), "tm", distance)
    partner = lax.ppermute(got, "lm", [(i, i ^ 1) for i in range(lm_size)])
    return tuple(
        jnp.where(parity == 0, jnp.concatenate([g, p]), jnp.concatenate([p, g]))
        for g, p in zip(got, partner)
    )


def point_inverse(normal):
    adj_rows = []
    for row_at in range(3):
        entries = []
        for col_at in range(3):
            entries.append(
                normal[(col_at + 1) % 3, (row_at + 1) % 3]
                * normal[(col_at + 2) % 3, (row_at + 2) % 3]
                - normal[(col_at + 1) % 3, (row_at + 2) % 3]
                * normal[(col_at + 2) % 3, (row_at + 1) % 3]
            )
        adj_rows.append(jnp.stack(entries))
    adjugate = jnp.stack(adj_rows)
    determ = (
        normal[0, 0] * adjugate[0, 0]
        + normal[0, 1] * adjugate[1, 0]
        + normal[0, 2] * adjugate[2, 0]
    )
    return adjugate / determ


def landmark_project(cam_jac, point_jac, residual, prior):
    normal = jnp.einsum("rasl,rbsl->absl", point_jac, point_jac, precision=PRECISE)
    normal = normal + prior[None, None] * jnp.eye(3, dtype=jnp.float32)[:, :, None, None]
    inverse = point_inverse(normal)
    cross = jnp.einsum("rasl,rmsl->amsl", point_jac, cam_jac, precision=PRECISE)
    cross_res = jnp.einsum("rasl,rsl->asl", point_jac, residual, precision=PRECISE)
    solved = jnp.einsum("absl,bmsl->amsl", inverse, cross, precision=PRECISE)
    solved_res = jnp.einsum("absl,bsl->asl", inverse, cross_res, precision=PRECISE)
    projected = cam_jac - jnp.einsum("rasl,amsl->rmsl", point_jac, solved, precision=PRECISE)
    projected_res = residual - jnp.einsum("rasl,asl->rsl", point_jac, solved_res, precision=PRECISE)
    return (projected, projected_res)


def place_knots(values, window_start):
    rows_count = values.shape[0]
    seg_count = values.shape[2]
    group_size = values.shape[3]
    knot_span = KNOTS + ORDER - 1
    offsets = jnp.arange(knot_span, dtype=jnp.int32)[:, None, None] - window_start[None]
    onehot = (offsets[:, None] == jnp.arange(ORDER, dtype=jnp.int32)[None, :, None, None]).astype(
        jnp.float32
    )
    shaped = values.reshape(rows_count, ORDER, DOF, seg_count, group_size)
    placed = jnp.einsum("kosl,rodsl->kdrsl", onehot, shaped, precision=PRECISE)
    return placed.reshape(knot_span * DOF, rows_count, seg_count, group_size)


def batched_terms(cam_jac, point_jac, residual, prior, window_start):
    seg_count = window_start.shape[0]
    landmarks = window_start.shape[1]
    group_size = min(128, landmarks)
    extended = (KNOTS + ORDER - 1) * DOF

    def one_group(totals, group_index):
        projected, projected_res = landmark_project(cam_jac, point_jac, residual, prior)
        placed_cam = place_knots(cam_jac, window_start)
        placed_proj = place_knots(projected, window_start)
        new_mat = totals[0] + jnp.einsum(
            "ersl,frsl->sef", placed_cam, placed_proj, precision=PRECISE
        )
        new_vec = totals[1] + jnp.einsum(
            "ersl,rsl->se", placed_cam, projected_res, precision=PRECISE
        )
        return ((new_mat, new_vec), None)

    start_totals = (
        jnp.zeros((seg_count, extended, extended), jnp.float32),
        jnp.zeros((seg_count, extended), jnp.float32),
    )
    totals, _ = lax.scan(
        one_group, start_totals, jnp.arange(landmarks // group_size, dtype=jnp.int32)
    )
    return totals


def band_terms(cam_jac, point_jac, residual, prior, window_start):
    projected, projected_res = landmark_project(cam_jac, point_jac, residual, prior)
    pair = jnp.einsum("rmsl,rnsl->slmn", cam_jac, projected, precision=PRECISE)
    vec = jnp.einsum("rmsl,rsl->slm", cam_jac, projected_res, precision=PRECISE)
    seg_count, landmarks = pair.shape[:2]
    blocks = pair.reshape(seg_count, landmarks, ORDER, DOF, ORDER, DOF)
    zero = jnp.zeros((seg_count, landmarks, DOF, DOF), pair.dtype)
    width = 2 * ORDER - 1
    by_start = []
    for a in range(ORDER):
        per_offset = []
        for d in range(width):
            b = a + d - (ORDER - 1)
            per_offset.append(blocks[:, :, a, :, b, :] if 0 <= b < ORDER else zero)
        by_start.append(jnp.stack(per_offset, 2))
    spread = jnp.stack(by_start, 2)
    knot_span = KNOTS + ORDER - 1
    onehot = (
        jnp.arange(knot_span, dtype=jnp.int32)[None, :, None, None]
        == window_start[:, None, :, None] + jnp.arange(ORDER, dtype=jnp.int32)[None, None, None, :]
    ).astype(jnp.float32)
    band = jnp.einsum("sila,sladxy->isxdy", onehot, spread, precision=PRECISE)
    band = band.reshape(knot_span, seg_count * DOF * width * DOF)
    vec_blocks = vec.reshape(seg_count, landmarks, ORDER, DOF)
    dense_vec = jnp.einsum("sila,slax->isx", onehot, vec_blocks, precision=PRECISE)
    return jnp.concatenate([band, dense_vec.reshape(knot_span, seg_count * DOF)], 1)


def summed_over(packed, axis):
    size = lax.axis_size(axis)
    assert size & (size - 1) == 0
    bit = 1
    while bit < size:
        packed = packed + lax.ppermute(packed, axis, [(i, i ^ bit) for i in range(size)])
        bit *= 2
    return packed


def dense_from_band(rows, seg_count):
    knot_span = rows.shape[0]
    width = rows.shape[2] // DOF
    extended = knot_span * DOF
    within = jnp.arange(width * DOF, dtype=jnp.int32)
    column = jnp.arange(extended, dtype=jnp.int32)
    knot = jnp.arange(knot_span, dtype=jnp.int32)
    select = (
        column[None, None, :]
        == DOF * (knot[:, None, None] - (ORDER - 1)) + within[None, :, None]
    ).astype(jnp.float32)
    placed = jnp.einsum("iak,ikc->iac", rows, select, precision=PRECISE)
    placed = jnp.transpose(placed.reshape(knot_span, seg_count, DOF, extended), (1, 0, 2, 3))
    return placed.reshape(seg_count, extended, extended)


PIVOT = 128


def sweep_kernel(d_ref, o_ref, *pivot_refs):
    count, order, _ = d_ref.shape
    o_ref[...] = d_ref[...]
    lane_row = lax.broadcasted_iota(jnp.int32, (1, PIVOT), 1)
    for blk in range(order // PIVOT):
        lo = blk * PIVOT
        for b in range(count):
            pivot_refs[b][...] = o_ref[b, lo:lo + PIVOT, lo:lo + PIVOT]

        def lane_value(row, at):
            return jnp.sum(jnp.where(lane_row == at, row, 0.0), axis=1, keepdims=True)

        def pivot_step(row, ahead, k, ahead_at):
            inv = 1.0 / lane_value(row, k)
            scaled = row * inv
            link = lane_value(row, ahead_at)
            return jnp.where(lane_row == k, link * inv, ahead - link * scaled), scaled, inv

        def full_update(p_ref, row, scaled, inv, k):
            is_k = lane_row == k
            col = jnp.broadcast_to(
                jnp.transpose(jnp.broadcast_to(row, (8, PIVOT)))[:, 0:1], (PIVOT, PIVOT)
            )
            upd = p_ref[...] - col * scaled
            p_ref[...] = jnp.where(is_k, col * inv, upd)
            p_ref[pl.ds(k, 1), :] = jnp.where(is_k, -inv, scaled)

        def step(k, carried):
            ahead_at = jnp.minimum(k + 1, PIVOT - 1)
            out = []
            for p_ref, (row, prev_row, prev_scaled, prev_inv) in zip(pivot_refs, carried):
                ahead = p_ref[pl.ds(ahead_at, 1), :]
                link = lane_value(prev_row, ahead_at)
                ahead = jnp.where(
                    lane_row == k - 1, link * prev_inv, ahead - link * prev_scaled
                )
                next_row, scaled, inv = pivot_step(row, ahead, k, ahead_at)
                full_update(p_ref, prev_row, prev_scaled, prev_inv, k - 1)
                out.append((next_row, row, scaled, inv))
            return tuple(out)

        first = []
        for p_ref in pivot_refs:
            row = p_ref[pl.ds(0, 1), :]
            next_row, scaled, inv = pivot_step(row, p_ref[pl.ds(1, 1), :], 0, 1)
            first.append((next_row, row, scaled, inv))
        last = lax.fori_loop(1, PIVOT, step, tuple(first), unroll=2)
        for p_ref, (_, prev_row, prev_scaled, prev_inv) in zip(pivot_refs, last):
            full_update(p_ref, prev_row, prev_scaled, prev_inv, PIVOT - 1)
        for b in range(count):
            pneg = pivot_refs[b][...]
            col_blk = o_ref[b, :, lo:lo + PIVOT]
            row_blk = o_ref[b, lo:lo + PIVOT, :]
            t = jnp.dot(col_blk, pneg, precision=PRECISE, preferred_element_type=jnp.float32)
            o_ref[b] = o_ref[b] + jnp.dot(t, row_blk, precision=PRECISE, preferred_element_type=jnp.float32)
            o_ref[b, :, lo:lo + PIVOT] = -t
            o_ref[b, lo:lo + PIVOT, :] = -jnp.dot(pneg, row_blk, precision=PRECISE, preferred_element_type=jnp.float32)
            o_ref[b, lo:lo + PIVOT, lo:lo + PIVOT] = pneg


def negated_inverse(mats):
    count, order, _ = mats.shape
    return pl.pallas_call(
        sweep_kernel,
        out_shape=jax.ShapeDtypeStruct(mats.shape, mats.dtype),
        in_specs=[pl.BlockSpec(memory_space=pltpu.VMEM)],
        out_specs=pl.BlockSpec(memory_space=pltpu.VMEM),
        scratch_shapes=[pltpu.VMEM((PIVOT, PIVOT), jnp.float32)] * count,
    )(mats)


def eliminate(inverse, coupling, right_side, next_coupling):
    ahead = jnp.einsum("bij,bjk->bik", next_coupling, inverse, precision=PRECISE)
    behind = jnp.einsum("bji,bjk->bik", coupling, inverse, precision=PRECISE)
    to_next = (
        jnp.einsum("bik,bjk->bij", ahead, next_coupling, precision=PRECISE),
        jnp.einsum("bik,bkj->bij", ahead, coupling, precision=PRECISE),
        jnp.einsum("bik,bk->bi", ahead, right_side, precision=PRECISE),
    )
    to_prev = (
        jnp.einsum("bik,bkj->bij", behind, coupling, precision=PRECISE),
        jnp.einsum("bik,bk->bi", behind, right_side, precision=PRECISE),
    )
    return (to_next, to_prev)


def local(
    cam_diag, cam_lower, cam_rhs, obs_cam_jac, obs_point_jac, obs_residual, point_prior, knot_start
):
    blocks = cam_diag.shape[1]
    border = (ORDER - 1) * DOF
    local_count = cam_rhs.shape[0]
    packed = summed_over(
        band_terms(obs_cam_jac, obs_point_jac, obs_residual, point_prior, knot_start), "lm"
    )
    knot_span = packed.shape[0]
    rows = local_count * DOF
    schur_mat = dense_from_band(
        packed[:, : rows * (2 * ORDER - 1) * DOF].reshape(knot_span, rows, -1), local_count
    )
    schur_vec = jnp.transpose(
        packed[:, rows * (2 * ORDER - 1) * DOF :].reshape(knot_span, local_count, DOF), (1, 0, 2)
    ).reshape(local_count, -1)
    arrived_mat, arrived_vec = passed_along(
        (schur_mat[local_count - 1, blocks:, :], schur_vec[local_count - 1, blocks:]), "tm", 1
    )
    spill_mat = jnp.concatenate([arrived_mat[None], schur_mat[:-1, blocks:, :]], 0)
    spill_vec = jnp.concatenate([arrived_vec[None], schur_vec[:-1, blocks:]], 0)
    diagonal = (
        cam_diag.reshape(local_count, blocks, blocks)
        + schur_mat[:, :blocks, :blocks]
        + jnp.pad(spill_mat[:, :, blocks:], ((0, 0), (0, blocks - border), (0, blocks - border)))
    )
    coupling = cam_lower.reshape(local_count, blocks, blocks) + jnp.pad(
        spill_mat[:, :, :blocks], ((0, 0), (0, blocks - border), (0, 0))
    )
    right_side = (
        cam_rhs - schur_vec[:, :blocks] - jnp.pad(spill_vec, ((0, 0), (0, blocks - border)))
    )
    (after_coupling,) = passed_in_halves((coupling[0],), -1)
    level_one = jnp.stack([diagonal[1], diagonal[3]])
    lm_size = lax.axis_size("lm")
    if lm_size % 2 == 0:
        parity = lax.axis_index("lm") % 2
        mine = -negated_inverse(lax.dynamic_index_in_dim(level_one, parity, 0, keepdims=True))[0]
        other = lax.ppermute(mine, "lm", [(i, i ^ 1) for i in range(lm_size)])
        inverses = jnp.where(parity == 0, jnp.stack([mine, other]), jnp.stack([other, mine]))
    else:
        inverses = -negated_inverse(level_one)
    pair = eliminate(
        inverses,
        jnp.stack([coupling[1], coupling[3]]),
        jnp.stack([right_side[1], right_side[3]]),
        jnp.stack([coupling[2], after_coupling]),
    )
    next_first, prev_first = jax.tree.map(lambda x: x[0], pair)
    next_last, prev_last = jax.tree.map(lambda x: x[1], pair)
    mid_diag = diagonal[2] - next_first[0] - prev_last[0]
    mid_coupling = -next_first[1]
    mid_rhs = right_side[2] - next_first[2] - prev_last[1]
    arrived_last = passed_in_halves((next_last[0], next_last[2]), 1)
    next_mid, prev_mid = jax.tree.map(
        lambda x: x[0],
        eliminate(
            -negated_inverse(mid_diag[None]), mid_coupling[None], mid_rhs[None], -next_last[1][None]
        ),
    )
    head_diag = diagonal[0] - prev_first[0] - prev_mid[0] - arrived_last[0]
    head_rhs = right_side[0] - prev_first[1] - prev_mid[1] - arrived_last[1]
    arrived = passed_in_halves((next_mid[0], next_mid[1], next_mid[2]), 1)
    out_diag = head_diag - arrived[0]
    out_coupling = -arrived[1]
    out_rhs = head_rhs - arrived[2]
    return (out_diag, out_coupling, out_rhs[None, :])


def solution(mesh):
    placed = (
        P("tm", None),
        P("tm", None),
        P("tm", None),
        P(None, None, "tm", "lm"),
        P(None, None, "tm", "lm"),
        P(None, "tm", "lm"),
        P("tm", "lm"),
        P("tm", "lm"),
    )
    return jax.shard_map(
        local,
        mesh=mesh,
        in_specs=placed,
        out_specs=(P("tm", None), P("tm", None), P("tm", None)),
        check_vma=False,
    )
```
